32 devices in a mesh: cfg: 2 (over x), space: 16 (over z, y, core).
Axes of the slice: x: 2, y: 2, z: 4, core: 2. Of those that a mesh axis runs over, the one named last changes fastest.
Arguments:
- eigenvectors: bfloat16 [12, 2, 3, 256, 2048], P('cfg', None, None, None, 'space'), parts along dimension 0, may hold values from -6 to 6
- gauge_links: float32 [12, 3, 2, 3, 3, 2048], P('cfg', None, None, None, None, 'space'), parts along dimension 0, may hold values from -3.5 to 3.5
- perambulators: bfloat16 [32, 2, 256, 1024], P(('cfg', 'space')), parts along dimension 0, may hold values from -0.375 to 0.375
- directions: int32 [3], replicated, may hold values from 0 to 2, each once
- momenta: int32 [1, 3], replicated, may hold values from -2 to 2
- pair_times: int32 [4, 2], replicated, may hold values from 0 to 5, as said below
Outputs:
- elementals: bfloat16 [12, 1536, 256], P('cfg', 'space'), parts along dimension 0
- correlators: float32 [32, 3, 2], P(('cfg', 'space')), parts along dimension 0
The draws below stay inside these ranges and needn't reach their ends.
There are 2 independent parts, one for each index of `cfg`. The reference program is written for one: setup_inputs(seed, part) draws one part's arguments, and reference() takes and returns one part's arrays. A program takes and returns all parts, laid end to end along the dimension named above; an argument that names none is the same for every part. Nothing has to cross between parts.
Inputs may be any that keep to these rules, and one draw needn't show every extreme that they name: `directions`: each direction appears exactly once. `pair_times`: no two time pairs have the same source and sink timeslice.
All inputs are finite; a program needn't handle non-finite values.
Results may differ from the reference program's by a relative error of at most 0.03.
Values may be sent and summed in bfloat16 or wider, within the bound.
No kernel may reach another device: no remote copies, remote signals or barrier semaphores. Data moves between devices by JAX's collectives and lax.ppermute only.
A program may use at most 128 MiB of HBM per device.

```python
import math
import jax
import jax.numpy as jnp
from jax import lax

NEV = 256
NSPIN = 4
NMOM = 1
NT = 6
LY = 32
LZ = 8
LX = 8
NOPS = 3
ROWS_E = 1536
NPAIR = 4


def draw_pair_times(key, part):
    order = jax.random.permutation(jax.random.fold_in(key, 17), NT * NT)[:NPAIR].astype(jnp.int32)
    source_time = order // NT
    sink_time = order % NT
    return jnp.stack([source_time, sink_time], 1).astype(jnp.int32)


def levels(stream_key, dims, cuts, least, high):
    def one(dim, parts):
        draws = jax.random.uniform(jax.random.fold_in(jax.random.fold_in(stream_key, 6), dim), (parts,), jnp.float32, least / len(cuts), high / len(cuts))
        return jnp.repeat(jnp.exp(draws), dims[dim] // parts).reshape((-1,) + (1,) * (len(dims) - dim - 1))

    factor_of = one(*cuts[0])
    for cut in cuts[1:]:
        factor_of = factor_of * one(*cut)
    return factor_of


def gaussian(own_key, dims, width, reach, cuts=(), kind=jnp.bfloat16):
    drawn = jax.random.normal(own_key, dims, jnp.float32) * width
    if len(cuts) > 0:
        drawn = levels(own_key, dims, cuts, -0.22, 0.18) * drawn
    return jnp.clip(drawn, min=-reach, max=reach).astype(kind)


def setup_inputs(seed: int = 0, part: int = 0) -> dict:
    seeds = jax.random.split(jax.random.key(seed), 7)
    own_keys = jax.random.split(jax.random.fold_in(seeds[6], part), 7)
    eigenvectors = gaussian(own_keys[0], (NT, 2, 3, NEV, LX * LY * LZ), 1.0, 6.0, ((4, 16),))
    gauge_links = gaussian(own_keys[1], (NT, 3, 2, 3, 3, LX * LY * LZ), 3 ** -0.5, 3.5, ((5, 16),), jnp.float32)
    perambulators = gaussian(own_keys[2], (NPAIR * NSPIN, 2, NEV, NSPIN * NEV), NEV ** -0.5, 0.375, ((0, 16),))
    directions = jax.random.permutation(seeds[3], 3).astype(jnp.int32)
    momenta = jax.random.randint(seeds[4], (NMOM, 3), -2, 3).astype(jnp.int32)
    pair_times = draw_pair_times(jax.random.fold_in(seeds[6], 71), part)
    return dict(eigenvectors=eigenvectors, gauge_links=gauge_links, perambulators=perambulators, directions=directions, momenta=momenta, pair_times=pair_times)


def carry_color(link, field):
    real_part = 0.0
    imag_part = 0.0
    for inner_color in range(3):
        link_real = link[0, :, inner_color][:, None, :]
        link_imag = link[1, :, inner_color][:, None, :]
        field_real = field[0, inner_color].astype(jnp.float32)[None]
        field_imag = field[1, inner_color].astype(jnp.float32)[None]
        real_part = real_part + link_real * field_real - link_imag * field_imag
        imag_part = imag_part + link_real * field_imag + link_imag * field_real
    return jnp.stack([real_part, imag_part], 0).astype(jnp.bfloat16)

def phase_angles(momenta, coords, extents):
    fraction = 0.0
    for course in range(3):
        turns = momenta[:, course:course + 1] * coords[course][None, :] % extents[course]
        fraction = fraction + turns.astype(jnp.float32) / extents[course]
    return 2.0 * math.pi * fraction

def with_phase(angle, field):
    cosine = jnp.cos(angle)[:, None, None, :]
    sine_part = jnp.sin(angle)[:, None, None, :]
    field_real = field[0].astype(jnp.float32)[None]
    field_imag = field[1].astype(jnp.float32)[None]
    real_part = cosine * field_real - sine_part * field_imag
    imag_part = sine_part * field_real + cosine * field_imag
    return jnp.stack([real_part, imag_part], 1).astype(jnp.bfloat16)

def correlations(phased, displaced):
    left_f = phased.astype(jnp.float32)
    right_f = displaced.astype(jnp.float32)
    form = 'mcis,dcjs->dmij'
    real_part = jnp.einsum(form, left_f[:, 0], right_f[:, 0]) + jnp.einsum(form, left_f[:, 1], right_f[:, 1])
    imag_part = jnp.einsum(form, left_f[:, 0], right_f[:, 1]) - jnp.einsum(form, left_f[:, 1], right_f[:, 0])
    return jnp.stack([real_part, imag_part], 2)

def contract_panel(sink, source, panel):
    panel_real = panel[0]
    panel_imag = panel[1]
    sink_real = sink[:, 0]
    sink_imag = sink[:, 1]
    form = 'amn,nk->amk'
    left_real = jnp.einsum(form, sink_real, panel_real) - jnp.einsum(form, sink_imag, panel_imag)
    left_imag = jnp.einsum(form, sink_real, panel_imag) + jnp.einsum(form, sink_imag, panel_real)
    blocks_real = panel_real.reshape(NEV, NSPIN, NEV)
    blocks_imag = panel_imag.reshape(NEV, NSPIN, NEV)
    source_real = source[:, 0]
    source_imag = source[:, 1]
    other = 'mrk,akn->amrn'
    right_real = jnp.einsum(other, blocks_real, source_real) - jnp.einsum(other, blocks_imag, source_imag)
    right_imag = jnp.einsum(other, blocks_real, source_imag) + jnp.einsum(other, blocks_imag, source_real)
    right_real = right_real.reshape(NOPS, NEV, NSPIN * NEV)
    right_imag = right_imag.reshape(NOPS, NEV, NSPIN * NEV)
    trace_real = lax.optimization_barrier(jnp.sum(left_real * right_real + left_imag * right_imag, axis=(1, 2)))
    trace_imag = lax.optimization_barrier(jnp.sum(left_imag * right_real - left_real * right_imag, axis=(1, 2)))
    return jnp.stack([trace_real, trace_imag], -1) * (1.0 / (16.0 * NEV))

def reference(eigenvectors, gauge_links, perambulators, directions, momenta, pair_times):
    sites = LX * LY * LZ
    position = jnp.arange(sites, dtype=jnp.int32)
    coords = (position // (LY * LZ), position // LZ % LY, position % LZ)
    angle = phase_angles(momenta, coords, (LX, LY, LZ))

    def one_time(moment):
        field = eigenvectors[moment]
        cube = field.reshape(2, 3, NEV, LX, LY, LZ)
        carried = []
        for course in range(3):
            nearby = jnp.roll(cube, -1, axis=3 + course).reshape(2, 3, NEV, sites)
            carried.append(carry_color(gauge_links[moment, course], nearby))
        carried = jnp.stack(carried, 0)
        displaced = jnp.take(carried, directions, axis=0)
        phased = with_phase(angle, field)
        return correlations(phased, displaced).reshape(ROWS_E, NEV)
    summands = lax.map(one_time, jnp.arange(NT, dtype=jnp.int32))
    elementals = (summands * (1.0 / math.sqrt(3.0 * sites))).astype(jnp.bfloat16)
    stacked = elementals.astype(jnp.float32).reshape(NT, NOPS, 2, NEV, NEV)

    def one_row(row_number):
        pair_row = row_number // NSPIN
        sink = stacked[pair_times[pair_row, 1]]
        source = stacked[pair_times[pair_row, 0]]
        panel = perambulators[row_number].astype(jnp.float32)
        return contract_panel(sink, source, panel)
    correlators = lax.map(one_row, jnp.arange(NPAIR * NSPIN, dtype=jnp.int32))
    return (elementals, correlators)
```

```python
import math

import jax
import jax.numpy as jnp
from jax import lax
from jax.sharding import PartitionSpec as P

NSPIN = 4
LY = 32
LZ = 8


def shifted(block, axis, distance):
    devices = range(lax.axis_size(axis))
    route = [((i - distance) % len(devices), i) for i in devices]
    return lax.ppermute(block, axis, route)


def swapped(value, axis, bit):
    return lax.ppermute(value, axis, [(i, i ^ 1 << bit) for i in range(lax.axis_size(axis))])


def phase_angles(momenta, coords, extents):
    fraction = 0.0
    for course in range(3):
        turns = momenta[:, course : course + 1] * coords[course][None, :] % extents[course]
        fraction = fraction + turns.astype(jnp.float32) / extents[course]
    return 2.0 * math.pi * fraction


def to_rows(field):
    count_t, _, _, count_ev, sites = field.shape
    return field.transpose(0, 3, 1, 2, 4).reshape(count_t, count_ev, 6 * sites)


def carried(link, field):
    field = field.astype(jnp.float32)
    real_part = 0.0
    imag_part = 0.0
    for inner in range(3):
        link_real = link[:, 0, :, inner][:, :, None, :]
        link_imag = link[:, 1, :, inner][:, :, None, :]
        field_real = field[:, 0, inner][:, None]
        field_imag = field[:, 1, inner][:, None]
        real_part = real_part + link_real * field_real - link_imag * field_imag
        imag_part = imag_part + link_real * field_imag + link_imag * field_real
    return jnp.stack([real_part, imag_part], 1).astype(jnp.bfloat16)


def local_sums(eigenvectors, gauge_links, far_tile, row_in, directions, angle):
    sites = eigenvectors.shape[-1]
    along_y = jnp.concatenate([eigenvectors[..., LZ:], row_in], axis=-1)
    column_pos = jnp.arange(sites, dtype=jnp.int32) % LZ
    along_z = jnp.where(
        column_pos == LZ - 1,
        jnp.roll(eigenvectors, LZ - 1, axis=-1),
        jnp.roll(eigenvectors, -1, axis=-1),
    )
    right = []
    for slot in range(directions.shape[0]):
        course = directions[slot]
        near = jnp.where(course == 0, far_tile, jnp.where(course == 1, along_y, along_z))
        link = lax.dynamic_index_in_dim(gauge_links, course, 1, keepdims=False)
        right.append(to_rows(carried(link, near)))
    right = jnp.stack(right, 1)
    cosine = jnp.cos(angle)[None, None, None, :]
    sine_part = jnp.sin(angle)[None, None, None, :]
    field_real = eigenvectors[:, 0].astype(jnp.float32)
    field_imag = eigenvectors[:, 1].astype(jnp.float32)
    phased_real = (cosine * field_real - sine_part * field_imag).astype(jnp.bfloat16)
    phased_imag = (sine_part * field_real + cosine * field_imag).astype(jnp.bfloat16)
    real_rows = to_rows(jnp.stack([phased_real, phased_imag], 1))
    imag_rows = to_rows(jnp.stack([-phased_imag, phased_real], 1))
    left = jnp.concatenate([real_rows, imag_rows], axis=1)
    joined = jnp.einsum("tPk,tajk->taPj", left, right, preferred_element_type=jnp.float32)
    return joined.reshape(joined.shape[0], -1, joined.shape[-1])


def contract_panel(sink, source, panel):
    count_ev = panel.shape[1]
    count_ops = sink.shape[0]
    sink_real = sink[:, 0]
    sink_imag = sink[:, 1]
    sink_wide = jnp.concatenate(
        [
            jnp.concatenate([sink_real, -sink_imag], axis=2),
            jnp.concatenate([sink_imag, sink_real], axis=2),
        ],
        axis=1,
    )
    panel_stack = panel.reshape(2 * count_ev, NSPIN * count_ev)
    left = jnp.einsum("amk,kn->amn", sink_wide, panel_stack, preferred_element_type=jnp.float32)
    left = left.reshape(count_ops, 2, count_ev, NSPIN, count_ev)
    blocks = panel.reshape(2, count_ev * NSPIN, count_ev)
    panel_wide = jnp.concatenate(
        [
            jnp.concatenate([blocks[0], -blocks[1]], axis=1),
            jnp.concatenate([blocks[1], blocks[0]], axis=1),
        ],
        axis=0,
    )
    source_stack = source.transpose(1, 2, 0, 3).reshape(2 * count_ev, count_ops * count_ev)
    right = jnp.einsum("mk,kn->mn", panel_wide, source_stack, preferred_element_type=jnp.float32)
    right = right.reshape(2, count_ev, NSPIN, count_ops, count_ev).transpose(3, 0, 1, 2, 4)
    left_real = left[:, 0]
    left_imag = left[:, 1]
    right_real = right[:, 0]
    right_imag = right[:, 1]
    trace_real = jnp.sum(left_real * right_real + left_imag * right_imag, axis=(1, 2, 3))
    trace_imag = jnp.sum(left_imag * right_real - left_real * right_imag, axis=(1, 2, 3))
    return jnp.stack([trace_real, trace_imag], -1) * (1.0 / (16.0 * count_ev))


def body(eigenvectors, gauge_links, perambulators, directions, momenta, pair_times):
    time_count = eigenvectors.shape[0]
    count_ev = eigenvectors.shape[3]
    local_sites = eigenvectors.shape[4]
    nspace = lax.axis_size("space")
    device = lax.axis_index("space")
    half_rows = LY // 2
    extent_x = nspace // 2
    column = jnp.arange(local_sites, dtype=jnp.int32)
    coord_x = device // 2 + 0 * column
    coord_y = device % 2 * half_rows + column // LZ
    coord_z = column % LZ
    angle = phase_angles(momenta, (coord_x, coord_y, coord_z), (extent_x, LY, LZ))[0]
    far_tile = shifted(eigenvectors, "space", -2)
    row_in = swapped(eigenvectors[..., :LZ], "space", 0)
    summands = local_sums(eigenvectors, gauge_links, far_tile, row_in, directions, angle)
    scale = 1.0 / math.sqrt(3.0 * extent_x * LY * LZ)
    shares = lax.psum_scatter(summands, "space", scatter_dimension=1, tiled=True)
    own_rows = (shares * scale).astype(jnp.bfloat16)
    rows = own_rows.shape[1]
    target = jnp.arange(nspace, dtype=jnp.int32) // NSPIN
    wanted = jnp.stack([pair_times[target, 1], pair_times[target, 0]], 1)
    outgoing = jnp.take(own_rows, wanted.reshape(-1), axis=0).reshape(nspace, 2, rows, count_ev)
    incoming = lax.all_to_all(outgoing, "space", 0, 0, tiled=True)
    count_ops = summands.shape[1] // (2 * count_ev)
    gathered = incoming.transpose(1, 0, 2, 3).reshape(2, count_ops, 2, count_ev, count_ev)
    correlators = contract_panel(gathered[0], gathered[1], perambulators[0])[None]
    return (own_rows, correlators)


def solution(mesh):
    placed = (
        P("cfg", None, None, None, "space"),
        P("cfg", None, None, None, None, "space"),
        P(("cfg", "space"), None, None, None),
        P(),
        P(),
        P(),
    )
    return jax.shard_map(
        body,
        mesh=mesh,
        in_specs=placed,
        out_specs=(P("cfg", "space", None), P(("cfg", "space"), None, None)),
        check_vma=False,
    )
```

```python
import math

import jax
import jax.numpy as jnp
from jax import lax
from jax.sharding import PartitionSpec as P

NSPIN = 4
LY = 32
LZ = 8


def shifted(block, axis, distance):
    devices = range(lax.axis_size(axis))
    route = [((i - distance) % len(devices), i) for i in devices]
    return lax.ppermute(block, axis, route)


def swapped(value, axis, bit):
    return lax.ppermute(value, axis, [(i, i ^ 1 << bit) for i in range(lax.axis_size(axis))])


def phase_angles(momenta, coords, extents):
    fraction = 0.0
    for course in range(3):
        turns = momenta[:, course : course + 1] * coords[course][None, :] % extents[course]
        fraction = fraction + turns.astype(jnp.float32) / extents[course]
    return 2.0 * math.pi * fraction


def to_rows(field):
    count_t, _, _, count_ev, sites = field.shape
    return field.transpose(0, 3, 1, 2, 4).reshape(count_t, count_ev, 6 * sites)


def carried(link, field):
    field = field.astype(jnp.float32)
    real_part = 0.0
    imag_part = 0.0
    for inner in range(3):
        link_real = link[:, 0, :, inner][:, :, None, :]
        link_imag = link[:, 1, :, inner][:, :, None, :]
        field_real = field[:, 0, inner][:, None]
        field_imag = field[:, 1, inner][:, None]
        real_part = real_part + link_real * field_real - link_imag * field_imag
        imag_part = imag_part + link_real * field_imag + link_imag * field_real
    return jnp.stack([real_part, imag_part], 1).astype(jnp.bfloat16)


def local_sums(eigenvectors, gauge_links, far_tile, row_in, directions, angle):
    sites = eigenvectors.shape[-1]
    along_y = jnp.concatenate([eigenvectors[..., LZ:], row_in], axis=-1)
    column_pos = jnp.arange(sites, dtype=jnp.int32) % LZ
    along_z = jnp.where(
        column_pos == LZ - 1,
        jnp.roll(eigenvectors, LZ - 1, axis=-1),
        jnp.roll(eigenvectors, -1, axis=-1),
    )
    right = []
    for slot in range(directions.shape[0]):
        course = directions[slot]
        near = jnp.where(course == 0, far_tile, jnp.where(course == 1, along_y, along_z))
        link = lax.dynamic_index_in_dim(gauge_links, course, 1, keepdims=False)
        right.append(to_rows(carried(link, near)))
    right = jnp.stack(right, 1)
    cosine = jnp.cos(angle)[None, None, None, :]
    sine_part = jnp.sin(angle)[None, None, None, :]
    field_real = eigenvectors[:, 0].astype(jnp.float32)
    field_imag = eigenvectors[:, 1].astype(jnp.float32)
    phased_real = (cosine * field_real - sine_part * field_imag).astype(jnp.bfloat16)
    phased_imag = (sine_part * field_real + cosine * field_imag).astype(jnp.bfloat16)
    real_rows = to_rows(jnp.stack([phased_real, phased_imag], 1))
    imag_rows = to_rows(jnp.stack([-phased_imag, phased_real], 1))
    left = jnp.concatenate([real_rows, imag_rows], axis=1)
    joined = jnp.einsum("tPk,tajk->taPj", left, right, preferred_element_type=jnp.float32)
    return joined.reshape(joined.shape[0], -1, joined.shape[-1])


def contract_panel(sink, source, panel):
    count_ev = panel.shape[1]
    count_ops = sink.shape[0]
    sink_real = sink[:, 0]
    sink_imag = sink[:, 1]
    sink_wide = jnp.concatenate(
        [
            jnp.concatenate([sink_real, -sink_imag], axis=2),
            jnp.concatenate([sink_imag, sink_real], axis=2),
        ],
        axis=1,
    )
    panel_stack = panel.reshape(2 * count_ev, NSPIN * count_ev)
    left = jnp.einsum("amk,kn->amn", sink_wide, panel_stack, preferred_element_type=jnp.float32)
    left = left.reshape(count_ops, 2, count_ev, NSPIN, count_ev)
    blocks = panel.reshape(2, count_ev * NSPIN, count_ev)
    panel_wide = jnp.concatenate(
        [
            jnp.concatenate([blocks[0], -blocks[1]], axis=1),
            jnp.concatenate([blocks[1], blocks[0]], axis=1),
        ],
        axis=0,
    )
    source_stack = source.transpose(1, 2, 0, 3).reshape(2 * count_ev, count_ops * count_ev)
    right = jnp.einsum("mk,kn->mn", panel_wide, source_stack, preferred_element_type=jnp.float32)
    right = right.reshape(2, count_ev, NSPIN, count_ops, count_ev).transpose(3, 0, 1, 2, 4)
    left_real = left[:, 0]
    left_imag = left[:, 1]
    right_real = right[:, 0]
    right_imag = right[:, 1]
    trace_real = jnp.sum(left_real * right_real + left_imag * right_imag, axis=(1, 2, 3))
    trace_imag = jnp.sum(left_imag * right_real - left_real * right_imag, axis=(1, 2, 3))
    return jnp.stack([trace_real, trace_imag], -1) * (1.0 / (16.0 * count_ev))


def body(eigenvectors, gauge_links, perambulators, directions, momenta, pair_times):
    time_count = eigenvectors.shape[0]
    count_ev = eigenvectors.shape[3]
    local_sites = eigenvectors.shape[4]
    nspace = lax.axis_size("space")
    device = lax.axis_index("space")
    half_rows = LY // 2
    extent_x = nspace // 2
    column = jnp.arange(local_sites, dtype=jnp.int32)
    coord_x = device // 2 + 0 * column
    coord_y = device % 2 * half_rows + column // LZ
    coord_z = column % LZ
    angle = phase_angles(momenta, (coord_x, coord_y, coord_z), (extent_x, LY, LZ))[0]
    far_tile = shifted(eigenvectors, "space", -2)
    row_in = swapped(eigenvectors[..., :LZ], "space", 0)
    summands = local_sums(eigenvectors, gauge_links, far_tile, row_in, directions, angle)
    scale = 1.0 / math.sqrt(3.0 * extent_x * LY * LZ)
    partial = (summands * scale).astype(jnp.bfloat16)
    own_rows = lax.psum_scatter(partial, "space", scatter_dimension=1, tiled=True)
    rows = own_rows.shape[1]
    target = jnp.arange(nspace, dtype=jnp.int32) // NSPIN
    wanted = jnp.stack([pair_times[target, 1], pair_times[target, 0]], 1)
    outgoing = jnp.take(own_rows, wanted.reshape(-1), axis=0).reshape(nspace, 2, rows, count_ev)
    incoming = lax.all_to_all(outgoing, "space", 0, 0, tiled=True)
    count_ops = summands.shape[1] // (2 * count_ev)
    gathered = incoming.transpose(1, 0, 2, 3).reshape(2, count_ops, 2, count_ev, count_ev)
    correlators = contract_panel(gathered[0], gathered[1], perambulators[0])[None]
    return (own_rows, correlators)


def solution(mesh):
    placed = (
        P("cfg", None, None, None, "space"),
        P("cfg", None, None, None, None, "space"),
        P(("cfg", "space"), None, None, None),
        P(),
        P(),
        P(),
    )
    return jax.shard_map(
        body,
        mesh=mesh,
        in_specs=placed,
        out_specs=(P("cfg", "space", None), P(("cfg", "space"), None, None)),
        check_vma=False,
    )
```

```python
import functools
import math

import jax
import jax.numpy as jnp
from jax import lax
from jax.experimental import pallas as pl
from jax.experimental.pallas import tpu as pltpu
from jax.sharding import PartitionSpec as P

NSPIN = 4
LY = 32
LZ = 8


def shifted(block, axis, distance):
    devices = range(lax.axis_size(axis))
    route = [((i - distance) % len(devices), i) for i in devices]
    return lax.ppermute(block, axis, route)


def swapped(value, axis, bit):
    return lax.ppermute(value, axis, [(i, i ^ 1 << bit) for i in range(lax.axis_size(axis))])


def phase_angles(momenta, coords, extents):
    fraction = 0.0
    for course in range(3):
        turns = momenta[:, course : course + 1] * coords[course][None, :] % extents[course]
        fraction = fraction + turns.astype(jnp.float32) / extents[course]
    return 2.0 * math.pi * fraction


def sums_kernel(slot_ref, field_ref, far_ref, row_ref, link_ref, trig_ref, out_ref, *, scale):
    count_ev, sites = field_ref.shape[3], field_ref.shape[4]
    lane = lax.broadcasted_iota(jnp.int32, (count_ev, sites), 1)
    last_z = lane % LZ == LZ - 1
    last_row = lane >= sites - LZ
    cosine = trig_ref[0:1, :]
    sine_part = trig_ref[1:2, :]
    here = [[field_ref[0, part, colour].astype(jnp.float32) for colour in range(3)] for part in range(2)]
    phased_real = [(cosine * here[0][c] - sine_part * here[1][c]).astype(jnp.bfloat16) for c in range(3)]
    phased_imag = [(sine_part * here[0][c] + cosine * here[1][c]).astype(jnp.bfloat16) for c in range(3)]
    real_rows = jnp.concatenate(phased_real + phased_imag, axis=1)
    imag_rows = jnp.concatenate([-v for v in phased_imag] + phased_real, axis=1)
    left = jnp.concatenate([real_rows, imag_rows], axis=0)
    far = [[far_ref[0, part, colour].astype(jnp.float32) for colour in range(3)] for part in range(2)]
    along_y = [
        [
            jnp.where(last_row, row_ref[0, part, colour].astype(jnp.float32), pltpu.roll(here[part][colour], sites - LZ, 1))
            for colour in range(3)
        ]
        for part in range(2)
    ]
    along_z = [
        [
            jnp.where(last_z, pltpu.roll(here[part][colour], LZ - 1, 1), pltpu.roll(here[part][colour], sites - 1, 1))
            for colour in range(3)
        ]
        for part in range(2)
    ]
    rows = 2 * count_ev
    for course, near in enumerate((far, along_y, along_z)):
        moved_real = []
        moved_imag = []
        for outer in range(3):
            real_part = 0.0
            imag_part = 0.0
            for inner in range(3):
                link_real = link_ref[0, course, 0, outer, inner : inner + 1, :]
                link_imag = link_ref[0, course, 1, outer, inner : inner + 1, :]
                real_part = real_part + link_real * near[0][inner] - link_imag * near[1][inner]
                imag_part = imag_part + link_real * near[1][inner] + link_imag * near[0][inner]
            moved_real.append(real_part.astype(jnp.bfloat16))
            moved_imag.append(imag_part.astype(jnp.bfloat16))
        right = jnp.concatenate(moved_real + moved_imag, axis=1)
        joined = lax.dot_general(left, right, (((1,), (1,)), ((), ())), preferred_element_type=jnp.float32)
        start = pl.multiple_of(slot_ref[course] * rows, rows)
        out_ref[0, pl.ds(start, rows), :] = (joined * scale).astype(out_ref.dtype)


def local_sums(eigenvectors, gauge_links, far_tile, row_in, directions, angle, scale):
    time_count, _, _, count_ev, sites = eigenvectors.shape
    count_ops = directions.shape[0]
    slot_of = jnp.sum(
        (directions[None, :] == jnp.arange(count_ops, dtype=jnp.int32)[:, None]) * jnp.arange(count_ops, dtype=jnp.int32)[None, :],
        axis=1,
    ).astype(jnp.int32)
    row_wide = jnp.pad(row_in, ((0, 0),) * 4 + ((sites - LZ, 0),))
    trig = jnp.stack([jnp.cos(angle), jnp.sin(angle)], 0)
    field_spec = pl.BlockSpec((1, 2, 3, count_ev, sites), lambda t, slot: (t, 0, 0, 0, 0))
    link_spec = pl.BlockSpec((1,) + gauge_links.shape[1:], lambda t, slot: (t, 0, 0, 0, 0, 0))
    trig_spec = pl.BlockSpec(trig.shape, lambda t, slot: (0, 0))
    rows = count_ops * 2 * count_ev
    grid_spec = pltpu.PrefetchScalarGridSpec(
        num_scalar_prefetch=1,
        grid=(time_count,),
        in_specs=[field_spec, field_spec, field_spec, link_spec, trig_spec],
        out_specs=pl.BlockSpec((1, rows, count_ev), lambda t, slot: (t, 0, 0)),
    )
    return pl.pallas_call(
        functools.partial(sums_kernel, scale=scale),
        grid_spec=grid_spec,
        out_shape=jax.ShapeDtypeStruct((time_count, rows, count_ev), jnp.bfloat16),
    )(slot_of, eigenvectors, far_tile, row_wide, gauge_links, trig)


def contract_panel(sink, source, panel):
    count_ev = panel.shape[1]
    count_ops = sink.shape[0]
    sink_real = sink[:, 0]
    sink_imag = sink[:, 1]
    sink_wide = jnp.concatenate(
        [
            jnp.concatenate([sink_real, -sink_imag], axis=2),
            jnp.concatenate([sink_imag, sink_real], axis=2),
        ],
        axis=1,
    )
    panel_stack = panel.reshape(2 * count_ev, NSPIN * count_ev)
    left = jnp.einsum("amk,kn->amn", sink_wide, panel_stack, preferred_element_type=jnp.float32)
    left = left.reshape(count_ops, 2, count_ev, NSPIN, count_ev)
    blocks = panel.reshape(2, count_ev * NSPIN, count_ev)
    panel_wide = jnp.concatenate(
        [
            jnp.concatenate([blocks[0], -blocks[1]], axis=1),
            jnp.concatenate([blocks[1], blocks[0]], axis=1),
        ],
        axis=0,
    )
    source_stack = source.transpose(1, 2, 0, 3).reshape(2 * count_ev, count_ops * count_ev)
    right = jnp.einsum("mk,kn->mn", panel_wide, source_stack, preferred_element_type=jnp.float32)
    right = right.reshape(2, count_ev, NSPIN, count_ops, count_ev).transpose(3, 0, 1, 2, 4)
    left_real = left[:, 0]
    left_imag = left[:, 1]
    right_real = right[:, 0]
    right_imag = right[:, 1]
    trace_real = jnp.sum(left_real * right_real + left_imag * right_imag, axis=(1, 2, 3))
    trace_imag = jnp.sum(left_imag * right_real - left_real * right_imag, axis=(1, 2, 3))
    return jnp.stack([trace_real, trace_imag], -1) * (1.0 / (16.0 * count_ev))


def body(eigenvectors, gauge_links, perambulators, directions, momenta, pair_times):
    time_count = eigenvectors.shape[0]
    count_ev = eigenvectors.shape[3]
    local_sites = eigenvectors.shape[4]
    nspace = lax.axis_size("space")
    device = lax.axis_index("space")
    half_rows = LY // 2
    extent_x = nspace // 2
    column = jnp.arange(local_sites, dtype=jnp.int32)
    coord_x = device // 2 + 0 * column
    coord_y = device % 2 * half_rows + column // LZ
    coord_z = column % LZ
    angle = phase_angles(momenta, (coord_x, coord_y, coord_z), (extent_x, LY, LZ))[0]
    far_tile = shifted(eigenvectors, "space", -2)
    row_in = swapped(eigenvectors[..., :LZ], "space", 0)
    scale = 1.0 / math.sqrt(3.0 * extent_x * LY * LZ)
    partial = local_sums(eigenvectors, gauge_links, far_tile, row_in, directions, angle, scale)
    own_rows = lax.psum_scatter(partial, "space", scatter_dimension=1, tiled=True)
    rows = own_rows.shape[1]
    target = jnp.arange(nspace, dtype=jnp.int32) // NSPIN
    wanted = jnp.stack([pair_times[target, 1], pair_times[target, 0]], 1)
    outgoing = jnp.take(own_rows, wanted.reshape(-1), axis=0).reshape(nspace, 2, rows, count_ev)
    incoming = lax.all_to_all(outgoing, "space", 0, 0, tiled=True)
    count_ops = partial.shape[1] // (2 * count_ev)
    gathered = incoming.transpose(1, 0, 2, 3).reshape(2, count_ops, 2, count_ev, count_ev)
    correlators = contract_panel(gathered[0], gathered[1], perambulators[0])[None]
    return (own_rows, correlators)


def solution(mesh):
    placed = (
        P("cfg", None, None, None, "space"),
        P("cfg", None, None, None, None, "space"),
        P(("cfg", "space"), None, None, None),
        P(),
        P(),
        P(),
    )
    return jax.shard_map(
        body,
        mesh=mesh,
        in_specs=placed,
        out_specs=(P("cfg", "space", None), P(("cfg", "space"), None, None)),
        check_vma=False,
    )
```

```python
import functools
import math

import jax
import jax.numpy as jnp
from jax import lax
from jax.experimental import pallas as pl
from jax.experimental.pallas import tpu as pltpu
from jax.sharding import Mesh, PartitionSpec as P

NSPIN = 4
LY = 32
LZ = 8


def shifted(block, axis, distance):
    devices = range(lax.axis_size(axis))
    route = [((i - distance) % len(devices), i) for i in devices]
    return lax.ppermute(block, axis, route)


def swapped(value, axis, bit):
    return lax.ppermute(value, axis, [(i, i ^ 1 << bit) for i in range(lax.axis_size(axis))])


def phase_angles(momenta, coords, extents):
    fraction = 0.0
    for course in range(3):
        turns = momenta[:, course : course + 1] * coords[course][None, :] % extents[course]
        fraction = fraction + turns.astype(jnp.float32) / extents[course]
    return 2.0 * math.pi * fraction


def sums_kernel(slot_ref, field_ref, far_ref, row_ref, link_ref, trig_ref, out_ref, *, scale):
    count_ev, sites = field_ref.shape[3], field_ref.shape[4]
    lane = lax.broadcasted_iota(jnp.int32, (count_ev, sites), 1)
    last_z = lane % LZ == LZ - 1
    last_row = lane >= sites - LZ
    cosine = trig_ref[0:1, :]
    sine_part = trig_ref[1:2, :]
    here = [[field_ref[0, part, colour].astype(jnp.float32) for colour in range(3)] for part in range(2)]
    phased_real = [(cosine * here[0][c] - sine_part * here[1][c]).astype(jnp.bfloat16) for c in range(3)]
    phased_imag = [(sine_part * here[0][c] + cosine * here[1][c]).astype(jnp.bfloat16) for c in range(3)]
    real_rows = jnp.concatenate(phased_real + phased_imag, axis=1)
    imag_rows = jnp.concatenate([-v for v in phased_imag] + phased_real, axis=1)
    left = jnp.concatenate([real_rows, imag_rows], axis=0)
    far = [[far_ref[0, part, colour].astype(jnp.float32) for colour in range(3)] for part in range(2)]
    along_y = [
        [
            jnp.where(last_row, row_ref[0, part, colour].astype(jnp.float32), pltpu.roll(here[part][colour], sites - LZ, 1))
            for colour in range(3)
        ]
        for part in range(2)
    ]
    along_z = [
        [
            jnp.where(last_z, pltpu.roll(here[part][colour], LZ - 1, 1), pltpu.roll(here[part][colour], sites - 1, 1))
            for colour in range(3)
        ]
        for part in range(2)
    ]
    rows = 2 * count_ev
    for course, near in enumerate((far, along_y, along_z)):
        moved_real = []
        moved_imag = []
        for outer in range(3):
            real_part = 0.0
            imag_part = 0.0
            for inner in range(3):
                link_real = link_ref[0, course, 0, outer, inner : inner + 1, :]
                link_imag = link_ref[0, course, 1, outer, inner : inner + 1, :]
                real_part = real_part + link_real * near[0][inner] - link_imag * near[1][inner]
                imag_part = imag_part + link_real * near[1][inner] + link_imag * near[0][inner]
            moved_real.append(real_part.astype(jnp.bfloat16))
            moved_imag.append(imag_part.astype(jnp.bfloat16))
        right = jnp.concatenate(moved_real + moved_imag, axis=1)
        joined = lax.dot_general(left, right, (((1,), (1,)), ((), ())), preferred_element_type=jnp.float32)
        start = pl.multiple_of(slot_ref[course] * rows, rows)
        out_ref[0, pl.ds(start, rows), :] = (joined * scale).astype(out_ref.dtype)


def local_sums(eigenvectors, gauge_links, far_tile, row_in, directions, angle, scale):
    time_count, _, _, count_ev, sites = eigenvectors.shape
    count_ops = directions.shape[0]
    slot_of = jnp.sum(
        (directions[None, :] == jnp.arange(count_ops, dtype=jnp.int32)[:, None]) * jnp.arange(count_ops, dtype=jnp.int32)[None, :],
        axis=1,
    ).astype(jnp.int32)
    row_wide = jnp.pad(row_in, ((0, 0),) * 4 + ((sites - LZ, 0),))
    trig = jnp.stack([jnp.cos(angle), jnp.sin(angle)], 0)
    field_spec = pl.BlockSpec((1, 2, 3, count_ev, sites), lambda t, slot: (t, 0, 0, 0, 0))
    link_spec = pl.BlockSpec((1,) + gauge_links.shape[1:], lambda t, slot: (t, 0, 0, 0, 0, 0))
    trig_spec = pl.BlockSpec(trig.shape, lambda t, slot: (0, 0))
    rows = count_ops * 2 * count_ev
    grid_spec = pltpu.PrefetchScalarGridSpec(
        num_scalar_prefetch=1,
        grid=(time_count,),
        in_specs=[field_spec, field_spec, field_spec, link_spec, trig_spec],
        out_specs=pl.BlockSpec((1, rows, count_ev), lambda t, slot: (t, 0, 0)),
    )
    return pl.pallas_call(
        functools.partial(sums_kernel, scale=scale),
        grid_spec=grid_spec,
        out_shape=jax.ShapeDtypeStruct((time_count, rows, count_ev), jnp.float32),
    )(slot_of, eigenvectors, far_tile, row_wide, gauge_links, trig)


def contract_panel(sink, source, panel):
    count_ev = panel.shape[1]
    count_ops = sink.shape[0]
    sink_real = sink[:, 0]
    sink_imag = sink[:, 1]
    sink_wide = jnp.concatenate(
        [
            jnp.concatenate([sink_real, -sink_imag], axis=2),
            jnp.concatenate([sink_imag, sink_real], axis=2),
        ],
        axis=1,
    )
    panel_stack = panel.reshape(2 * count_ev, NSPIN * count_ev)
    left = jnp.einsum("amk,kn->amn", sink_wide, panel_stack, preferred_element_type=jnp.float32)
    left = left.reshape(count_ops, 2, count_ev, NSPIN, count_ev)
    blocks = panel.reshape(2, count_ev * NSPIN, count_ev)
    panel_wide = jnp.concatenate(
        [
            jnp.concatenate([blocks[0], -blocks[1]], axis=1),
            jnp.concatenate([blocks[1], blocks[0]], axis=1),
        ],
        axis=0,
    )
    source_stack = source.transpose(1, 2, 0, 3).reshape(2 * count_ev, count_ops * count_ev)
    right = jnp.einsum("mk,kn->mn", panel_wide, source_stack, preferred_element_type=jnp.float32)
    right = right.reshape(2, count_ev, NSPIN, count_ops, count_ev).transpose(3, 0, 1, 2, 4)
    left_real = left[:, 0]
    left_imag = left[:, 1]
    right_real = right[:, 0]
    right_imag = right[:, 1]
    trace_real = jnp.sum(left_real * right_real + left_imag * right_imag, axis=(1, 2, 3))
    trace_imag = jnp.sum(left_imag * right_real - left_real * right_imag, axis=(1, 2, 3))
    return jnp.stack([trace_real, trace_imag], -1) * (1.0 / (16.0 * count_ev))


def body(eigenvectors, gauge_links, perambulators, directions, momenta, pair_times):
    count_ev = eigenvectors.shape[3]
    local_sites = eigenvectors.shape[4]
    count_chips = lax.axis_size("chip")
    nspace = 2 * count_chips
    core = lax.axis_index("core")
    device = lax.axis_index("chip") * 2 + core
    half_rows = LY // 2
    extent_x = count_chips
    column = jnp.arange(local_sites, dtype=jnp.int32)
    coord_x = device // 2 + 0 * column
    coord_y = device % 2 * half_rows + column // LZ
    coord_z = column % LZ
    angle = phase_angles(momenta, (coord_x, coord_y, coord_z), (extent_x, LY, LZ))[0]
    far_tile = shifted(eigenvectors, "chip", -1)
    row_in = swapped(eigenvectors[..., :LZ], "core", 0)
    scale = 1.0 / math.sqrt(3.0 * extent_x * LY * LZ)
    partial = local_sums(eigenvectors, gauge_links, far_tile, row_in, directions, angle, scale)
    time_count, all_rows = partial.shape[0], partial.shape[1]
    rows = all_rows // nspace
    blocks = partial.reshape(time_count, count_chips, 2, rows, count_ev)
    chip_sums = lax.psum_scatter(blocks, "core", scatter_dimension=2, tiled=True)
    own_rows = lax.psum_scatter(chip_sums.astype(jnp.bfloat16), "chip", scatter_dimension=1, tiled=True)
    own_rows = own_rows.reshape(time_count, rows, count_ev)
    target = jnp.arange(nspace, dtype=jnp.int32) // NSPIN
    wanted = jnp.stack([pair_times[target, 1], pair_times[target, 0]], 1)
    outgoing = jnp.take(own_rows, wanted.reshape(-1), axis=0).reshape(nspace, 2, rows, count_ev)
    incoming = lax.all_to_all(outgoing, ("chip", "core"), 0, 0, tiled=True)
    count_ops = all_rows // (2 * count_ev)
    gathered = incoming.transpose(1, 0, 2, 3).reshape(2, count_ops, 2, count_ev, count_ev)
    correlators = contract_panel(gathered[0], gathered[1], perambulators[0])[None]
    return (own_rows, correlators)


def solution(mesh):
    count_cfg = mesh.shape["cfg"]
    count_chips = mesh.shape["space"] // 2
    split = Mesh(mesh.devices.reshape(count_cfg, count_chips, 2), ("cfg", "chip", "core"))
    space = ("chip", "core")
    placed = (
        P("cfg", None, None, None, space),
        P("cfg", None, None, None, None, space),
        P(("cfg",) + space, None, None, None),
        P(),
        P(),
        P(),
    )
    return jax.shard_map(
        body,
        mesh=split,
        in_specs=placed,
        out_specs=(P("cfg", space, None), P(("cfg",) + space, None, None)),
        check_vma=False,
    )
```

```python
import functools
import math

import jax
import jax.numpy as jnp
from jax import lax
from jax.experimental import pallas as pl
from jax.experimental.pallas import tpu as pltpu
from jax.sharding import PartitionSpec as P

NSPIN = 4
LY = 32
LZ = 8


def shifted(block, axis, distance):
    devices = range(lax.axis_size(axis))
    route = [((i - distance) % len(devices), i) for i in devices]
    return lax.ppermute(block, axis, route)


def swapped(value, axis, bit):
    return lax.ppermute(value, axis, [(i, i ^ 1 << bit) for i in range(lax.axis_size(axis))])


def phase_angles(momenta, coords, extents):
    fraction = 0.0
    for course in range(3):
        turns = momenta[:, course : course + 1] * coords[course][None, :] % extents[course]
        fraction = fraction + turns.astype(jnp.float32) / extents[course]
    return 2.0 * math.pi * fraction


def sums_kernel(slot_ref, field_ref, near_ref, link_ref, trig_ref, *rest, scale, course_list):
    out_ref = rest[-1]
    count_ev, sites = field_ref.shape[3], field_ref.shape[4]
    lane = lax.broadcasted_iota(jnp.int32, (count_ev, sites), 1)
    last_z = lane % LZ == LZ - 1
    last_row = lane >= sites - LZ
    cosine = trig_ref[0:1, :]
    sine_part = trig_ref[1:2, :]
    here = [[field_ref[0, part, colour].astype(jnp.float32) for colour in range(3)] for part in range(2)]
    phased_real = [(cosine * here[0][c] - sine_part * here[1][c]).astype(jnp.bfloat16) for c in range(3)]
    phased_imag = [(sine_part * here[0][c] + cosine * here[1][c]).astype(jnp.bfloat16) for c in range(3)]
    real_rows = jnp.concatenate(phased_real + phased_imag, axis=1)
    imag_rows = jnp.concatenate([-v for v in phased_imag] + phased_real, axis=1)
    left = jnp.concatenate([real_rows, imag_rows], axis=0)
    rows = 2 * count_ev
    for course in course_list:
        if course == 0:
            near = [[near_ref[0, part, colour].astype(jnp.float32) for colour in range(3)] for part in range(2)]
        elif course == 1:
            near = [
                [
                    jnp.where(last_row, near_ref[0, part, colour].astype(jnp.float32), pltpu.roll(here[part][colour], sites - LZ, 1))
                    for colour in range(3)
                ]
                for part in range(2)
            ]
        else:
            near = [
                [
                    jnp.where(last_z, pltpu.roll(here[part][colour], LZ - 1, 1), pltpu.roll(here[part][colour], sites - 1, 1))
                    for colour in range(3)
                ]
                for part in range(2)
            ]
        moved_real = []
        moved_imag = []
        for outer in range(3):
            real_part = 0.0
            imag_part = 0.0
            for inner in range(3):
                link_real = link_ref[0, course, 0, outer, inner : inner + 1, :]
                link_imag = link_ref[0, course, 1, outer, inner : inner + 1, :]
                real_part = real_part + link_real * near[0][inner] - link_imag * near[1][inner]
                imag_part = imag_part + link_real * near[1][inner] + link_imag * near[0][inner]
            moved_real.append(real_part.astype(jnp.bfloat16))
            moved_imag.append(imag_part.astype(jnp.bfloat16))
        right = jnp.concatenate(moved_real + moved_imag, axis=1)
        joined = lax.dot_general(left, right, (((1,), (1,)), ((), ())), preferred_element_type=jnp.float32)
        if len(course_list) == 1:
            out_ref[0] = (joined * scale).astype(out_ref.dtype)
        else:
            start = pl.multiple_of(slot_ref[course] * rows, rows)
            out_ref[0, pl.ds(start, rows), :] = (joined * scale).astype(out_ref.dtype)


def local_sums(eigenvectors, gauge_links, far_tile, row_in, directions, angle, scale):
    time_count, _, _, count_ev, sites = eigenvectors.shape
    count_ops = directions.shape[0]
    slot_of = jnp.sum(
        (directions[None, :] == jnp.arange(count_ops, dtype=jnp.int32)[:, None]) * jnp.arange(count_ops, dtype=jnp.int32)[None, :],
        axis=1,
    ).astype(jnp.int32)
    row_wide = jnp.pad(row_in, ((0, 0),) * 4 + ((sites - LZ, 0),))
    trig = jnp.stack([jnp.cos(angle), jnp.sin(angle)], 0)
    field_spec = pl.BlockSpec((1, 2, 3, count_ev, sites), lambda t, slot: (t, 0, 0, 0, 0))
    link_spec = pl.BlockSpec((1,) + gauge_links.shape[1:], lambda t, slot: (t, 0, 0, 0, 0, 0))
    trig_spec = pl.BlockSpec(trig.shape, lambda t, slot: (0, 0))
    rows = count_ops * 2 * count_ev
    near_courses = tuple(course for course in range(count_ops) if course != 0)
    first_spec = pltpu.PrefetchScalarGridSpec(
        num_scalar_prefetch=1,
        grid=(time_count,),
        in_specs=[field_spec, field_spec, link_spec, trig_spec],
        out_specs=pl.BlockSpec((1, rows, count_ev), lambda t, slot: (t, 0, 0)),
    )
    partial = pl.pallas_call(
        functools.partial(sums_kernel, scale=scale, course_list=near_courses),
        grid_spec=first_spec,
        out_shape=jax.ShapeDtypeStruct((time_count, rows, count_ev), jnp.bfloat16),
    )(slot_of, eigenvectors, row_wide, gauge_links, trig)
    second_spec = pltpu.PrefetchScalarGridSpec(
        num_scalar_prefetch=1,
        grid=(time_count,),
        in_specs=[field_spec, field_spec, link_spec, trig_spec, pl.BlockSpec(memory_space=pl.ANY)],
        out_specs=pl.BlockSpec((1, 2 * count_ev, count_ev), lambda t, slot: (t, slot[0], 0)),
    )
    return pl.pallas_call(
        functools.partial(sums_kernel, scale=scale, course_list=(0,)),
        grid_spec=second_spec,
        out_shape=jax.ShapeDtypeStruct((time_count, rows, count_ev), jnp.bfloat16),
        input_output_aliases={5: 0},
    )(slot_of, eigenvectors, far_tile, gauge_links, trig, partial)


def contract_panel(sink, source, panel):
    count_ev = panel.shape[1]
    count_ops = sink.shape[0]
    sink_real = sink[:, 0]
    sink_imag = sink[:, 1]
    sink_wide = jnp.concatenate(
        [
            jnp.concatenate([sink_real, -sink_imag], axis=2),
            jnp.concatenate([sink_imag, sink_real], axis=2),
        ],
        axis=1,
    )
    panel_stack = panel.reshape(2 * count_ev, NSPIN * count_ev)
    left = jnp.einsum("amk,kn->amn", sink_wide, panel_stack, preferred_element_type=jnp.float32)
    left = left.reshape(count_ops, 2, count_ev, NSPIN, count_ev)
    blocks = panel.reshape(2, count_ev * NSPIN, count_ev)
    panel_wide = jnp.concatenate(
        [
            jnp.concatenate([blocks[0], -blocks[1]], axis=1),
            jnp.concatenate([blocks[1], blocks[0]], axis=1),
        ],
        axis=0,
    )
    source_stack = source.transpose(1, 2, 0, 3).reshape(2 * count_ev, count_ops * count_ev)
    right = jnp.einsum("mk,kn->mn", panel_wide, source_stack, preferred_element_type=jnp.float32)
    right = right.reshape(2, count_ev, NSPIN, count_ops, count_ev).transpose(3, 0, 1, 2, 4)
    left_real = left[:, 0]
    left_imag = left[:, 1]
    right_real = right[:, 0]
    right_imag = right[:, 1]
    trace_real = jnp.sum(left_real * right_real + left_imag * right_imag, axis=(1, 2, 3))
    trace_imag = jnp.sum(left_imag * right_real - left_real * right_imag, axis=(1, 2, 3))
    return jnp.stack([trace_real, trace_imag], -1) * (1.0 / (16.0 * count_ev))


def body(eigenvectors, gauge_links, perambulators, directions, momenta, pair_times):
    time_count = eigenvectors.shape[0]
    count_ev = eigenvectors.shape[3]
    local_sites = eigenvectors.shape[4]
    nspace = lax.axis_size("space")
    device = lax.axis_index("space")
    half_rows = LY // 2
    extent_x = nspace // 2
    column = jnp.arange(local_sites, dtype=jnp.int32)
    coord_x = device // 2 + 0 * column
    coord_y = device % 2 * half_rows + column // LZ
    coord_z = column % LZ
    angle = phase_angles(momenta, (coord_x, coord_y, coord_z), (extent_x, LY, LZ))[0]
    far_tile = shifted(eigenvectors, "space", -2)
    row_in = swapped(eigenvectors[..., :LZ], "space", 0)
    scale = 1.0 / math.sqrt(3.0 * extent_x * LY * LZ)
    partial = local_sums(eigenvectors, gauge_links, far_tile, row_in, directions, angle, scale)
    own_rows = lax.psum_scatter(partial, "space", scatter_dimension=1, tiled=True)
    rows = own_rows.shape[1]
    target = jnp.arange(nspace, dtype=jnp.int32) // NSPIN
    wanted = jnp.stack([pair_times[target, 1], pair_times[target, 0]], 1)
    outgoing = jnp.take(own_rows, wanted.reshape(-1), axis=0).reshape(nspace, 2, rows, count_ev)
    incoming = lax.all_to_all(outgoing, "space", 0, 0, tiled=True)
    count_ops = partial.shape[1] // (2 * count_ev)
    gathered = incoming.transpose(1, 0, 2, 3).reshape(2, count_ops, 2, count_ev, count_ev)
    correlators = contract_panel(gathered[0], gathered[1], perambulators[0])[None]
    return (own_rows, correlators)


def solution(mesh):
    placed = (
        P("cfg", None, None, None, "space"),
        P("cfg", None, None, None, None, "space"),
        P(("cfg", "space"), None, None, None),
        P(),
        P(),
        P(),
    )
    return jax.shard_map(
        body,
        mesh=mesh,
        in_specs=placed,
        out_specs=(P("cfg", "space", None), P(("cfg", "space"), None, None)),
        check_vma=False,
    )
```

```python
import functools
import math

import jax
import jax.numpy as jnp
from jax import lax
from jax.experimental import pallas as pl
from jax.experimental.pallas import tpu as pltpu
from jax.sharding import Mesh, PartitionSpec as P

NSPIN = 4
LY = 32
LZ = 8
SPACE = ("slab", "member")


def shifted(block, axis, distance):
    devices = range(lax.axis_size(axis))
    route = [((i - distance) % len(devices), i) for i in devices]
    return lax.ppermute(block, axis, route)


def swapped(value, axis, bit):
    return lax.ppermute(value, axis, [(i, i ^ 1 << bit) for i in range(lax.axis_size(axis))])


def phase_angles(momenta, coords, extents):
    fraction = 0.0
    for course in range(3):
        turns = momenta[:, course : course + 1] * coords[course][None, :] % extents[course]
        fraction = fraction + turns.astype(jnp.float32) / extents[course]
    return 2.0 * math.pi * fraction


def sums_kernel(slot_ref, field_ref, near_ref, link_ref, trig_ref, *rest, scale, course_list):
    out_ref = rest[-1]
    count_ev, sites = field_ref.shape[3], field_ref.shape[4]
    lane = lax.broadcasted_iota(jnp.int32, (count_ev, sites), 1)
    last_z = lane % LZ == LZ - 1
    last_row = lane >= sites - LZ
    cosine = trig_ref[0:1, :]
    sine_part = trig_ref[1:2, :]
    here = [[field_ref[0, part, colour].astype(jnp.float32) for colour in range(3)] for part in range(2)]
    phased_real = [(cosine * here[0][c] - sine_part * here[1][c]).astype(jnp.bfloat16) for c in range(3)]
    phased_imag = [(sine_part * here[0][c] + cosine * here[1][c]).astype(jnp.bfloat16) for c in range(3)]
    real_rows = jnp.concatenate(phased_real + phased_imag, axis=1)
    imag_rows = jnp.concatenate([-v for v in phased_imag] + phased_real, axis=1)
    left = jnp.concatenate([real_rows, imag_rows], axis=0)
    rows = 2 * count_ev
    for course in course_list:
        if course == 0:
            near = [[near_ref[0, part, colour].astype(jnp.float32) for colour in range(3)] for part in range(2)]
        elif course == 1:
            near = [
                [
                    jnp.where(last_row, near_ref[0, part, colour].astype(jnp.float32), pltpu.roll(here[part][colour], sites - LZ, 1))
                    for colour in range(3)
                ]
                for part in range(2)
            ]
        else:
            near = [
                [
                    jnp.where(last_z, pltpu.roll(here[part][colour], LZ - 1, 1), pltpu.roll(here[part][colour], sites - 1, 1))
                    for colour in range(3)
                ]
                for part in range(2)
            ]
        moved_real = []
        moved_imag = []
        for outer in range(3):
            real_part = 0.0
            imag_part = 0.0
            for inner in range(3):
                link_real = link_ref[0, course, 0, outer, inner : inner + 1, :]
                link_imag = link_ref[0, course, 1, outer, inner : inner + 1, :]
                real_part = real_part + link_real * near[0][inner] - link_imag * near[1][inner]
                imag_part = imag_part + link_real * near[1][inner] + link_imag * near[0][inner]
            moved_real.append(real_part.astype(jnp.bfloat16))
            moved_imag.append(imag_part.astype(jnp.bfloat16))
        right = jnp.concatenate(moved_real + moved_imag, axis=1)
        joined = lax.dot_general(left, right, (((1,), (1,)), ((), ())), preferred_element_type=jnp.float32)
        if len(course_list) == 1:
            out_ref[0] = (joined * scale).astype(out_ref.dtype)
        else:
            start = pl.multiple_of(slot_ref[course] * rows, rows)
            out_ref[0, pl.ds(start, rows), :] = (joined * scale).astype(out_ref.dtype)


def local_sums(eigenvectors, gauge_links, far_tile, row_in, directions, angle, scale):
    time_count, _, _, count_ev, sites = eigenvectors.shape
    count_ops = directions.shape[0]
    slot_of = jnp.sum(
        (directions[None, :] == jnp.arange(count_ops, dtype=jnp.int32)[:, None]) * jnp.arange(count_ops, dtype=jnp.int32)[None, :],
        axis=1,
    ).astype(jnp.int32)
    row_wide = jnp.pad(row_in, ((0, 0),) * 4 + ((sites - LZ, 0),))
    trig = jnp.stack([jnp.cos(angle), jnp.sin(angle)], 0)
    field_spec = pl.BlockSpec((1, 2, 3, count_ev, sites), lambda t, slot: (t, 0, 0, 0, 0))
    link_spec = pl.BlockSpec((1,) + gauge_links.shape[1:], lambda t, slot: (t, 0, 0, 0, 0, 0))
    trig_spec = pl.BlockSpec(trig.shape, lambda t, slot: (0, 0))
    rows = count_ops * 2 * count_ev
    near_courses = tuple(course for course in range(count_ops) if course != 0)
    first_spec = pltpu.PrefetchScalarGridSpec(
        num_scalar_prefetch=1,
        grid=(time_count,),
        in_specs=[field_spec, field_spec, link_spec, trig_spec],
        out_specs=pl.BlockSpec((1, rows, count_ev), lambda t, slot: (t, 0, 0)),
    )
    partial = pl.pallas_call(
        functools.partial(sums_kernel, scale=scale, course_list=near_courses),
        grid_spec=first_spec,
        out_shape=jax.ShapeDtypeStruct((time_count, rows, count_ev), jnp.bfloat16),
    )(slot_of, eigenvectors, row_wide, gauge_links, trig)
    second_spec = pltpu.PrefetchScalarGridSpec(
        num_scalar_prefetch=1,
        grid=(time_count,),
        in_specs=[field_spec, field_spec, link_spec, trig_spec, pl.BlockSpec(memory_space=pl.ANY)],
        out_specs=pl.BlockSpec((1, 2 * count_ev, count_ev), lambda t, slot: (t, slot[0], 0)),
    )
    return pl.pallas_call(
        functools.partial(sums_kernel, scale=scale, course_list=(0,)),
        grid_spec=second_spec,
        out_shape=jax.ShapeDtypeStruct((time_count, rows, count_ev), jnp.bfloat16),
        input_output_aliases={5: 0},
    )(slot_of, eigenvectors, far_tile, gauge_links, trig, partial)


def contract_panel(sink, source, panel):
    count_ev = panel.shape[1]
    count_ops = sink.shape[0]
    sink_real = sink[:, 0]
    sink_imag = sink[:, 1]
    sink_wide = jnp.concatenate(
        [
            jnp.concatenate([sink_real, -sink_imag], axis=2),
            jnp.concatenate([sink_imag, sink_real], axis=2),
        ],
        axis=1,
    )
    panel_stack = panel.reshape(2 * count_ev, NSPIN * count_ev)
    left = jnp.einsum("amk,kn->amn", sink_wide, panel_stack, preferred_element_type=jnp.float32)
    left = left.reshape(count_ops, 2, count_ev, NSPIN, count_ev)
    blocks = panel.reshape(2, count_ev * NSPIN, count_ev)
    panel_wide = jnp.concatenate(
        [
            jnp.concatenate([blocks[0], -blocks[1]], axis=1),
            jnp.concatenate([blocks[1], blocks[0]], axis=1),
        ],
        axis=0,
    )
    source_stack = source.transpose(1, 2, 0, 3).reshape(2 * count_ev, count_ops * count_ev)
    right = jnp.einsum("mk,kn->mn", panel_wide, source_stack, preferred_element_type=jnp.float32)
    right = right.reshape(2, count_ev, NSPIN, count_ops, count_ev).transpose(3, 0, 1, 2, 4)
    left_real = left[:, 0]
    left_imag = left[:, 1]
    right_real = right[:, 0]
    right_imag = right[:, 1]
    trace_real = jnp.sum(left_real * right_real + left_imag * right_imag, axis=(1, 2, 3))
    trace_imag = jnp.sum(left_imag * right_real - left_real * right_imag, axis=(1, 2, 3))
    return jnp.stack([trace_real, trace_imag], -1) * (1.0 / (16.0 * count_ev))


def body(eigenvectors, gauge_links, perambulators, directions, momenta, pair_times):
    time_count = eigenvectors.shape[0]
    count_ev = eigenvectors.shape[3]
    local_sites = eigenvectors.shape[4]
    count_slabs = lax.axis_size("slab")
    nspace = NSPIN * count_slabs
    member = lax.axis_index("member")
    device = lax.axis_index("slab") * NSPIN + member
    half_rows = LY // 2
    extent_x = nspace // 2
    column = jnp.arange(local_sites, dtype=jnp.int32)
    coord_x = device // 2 + 0 * column
    coord_y = device % 2 * half_rows + column // LZ
    coord_z = column % LZ
    angle = phase_angles(momenta, (coord_x, coord_y, coord_z), (extent_x, LY, LZ))[0]
    far_tile = shifted(eigenvectors, SPACE, -2)
    row_in = swapped(eigenvectors[..., :LZ], SPACE, 0)
    scale = 1.0 / math.sqrt(3.0 * extent_x * LY * LZ)
    partial = local_sums(eigenvectors, gauge_links, far_tile, row_in, directions, angle, scale)
    own_rows = lax.psum_scatter(partial, SPACE, scatter_dimension=1, tiled=True)
    rows = own_rows.shape[1]
    slabs = jnp.arange(count_slabs, dtype=jnp.int32)
    wanted = jnp.stack([pair_times[slabs, 1], pair_times[slabs, 0]], 1)
    outgoing = jnp.take(own_rows, wanted.reshape(-1), axis=0).reshape(count_slabs, 2, rows, count_ev)
    across = lax.all_to_all(outgoing, "slab", 0, 0, tiled=True)
    spread = jnp.broadcast_to(across[None], (NSPIN,) + across.shape)
    within = lax.all_to_all(spread, "member", 0, 0, tiled=True)
    incoming = within.transpose(1, 0, 2, 3, 4).reshape(nspace, 2, rows, count_ev)
    count_ops = partial.shape[1] // (2 * count_ev)
    gathered = incoming.transpose(1, 0, 2, 3).reshape(2, count_ops, 2, count_ev, count_ev)
    correlators = contract_panel(gathered[0], gathered[1], perambulators[0])[None]
    return (own_rows, correlators)


def solution(mesh):
    count_cfg = mesh.shape["cfg"]
    count_slabs = mesh.shape["space"] // NSPIN
    split = Mesh(mesh.devices.reshape(count_cfg, count_slabs, NSPIN), ("cfg",) + SPACE)
    placed = (
        P("cfg", None, None, None, SPACE),
        P("cfg", None, None, None, None, SPACE),
        P(("cfg",) + SPACE, None, None, None),
        P(),
        P(),
        P(),
    )
    return jax.shard_map(
        body,
        mesh=split,
        in_specs=placed,
        out_specs=(P("cfg", SPACE, None), P(("cfg",) + SPACE, None, None)),
        check_vma=False,
    )
```

```python
import functools
import math

import jax
import jax.numpy as jnp
from jax import lax
from jax.experimental import pallas as pl
from jax.experimental.pallas import tpu as pltpu
from jax.sharding import Mesh, PartitionSpec as P

NSPIN = 4
LY = 32
LZ = 8
SPACE = ("slab", "member")


def shifted(block, axis, distance):
    devices = range(lax.axis_size(axis))
    route = [((i - distance) % len(devices), i) for i in devices]
    return lax.ppermute(block, axis, route)


def swapped(value, axis, bit):
    return lax.ppermute(value, axis, [(i, i ^ 1 << bit) for i in range(lax.axis_size(axis))])


def phase_angles(momenta, coords, extents):
    fraction = 0.0
    for course in range(3):
        turns = momenta[:, course : course + 1] * coords[course][None, :] % extents[course]
        fraction = fraction + turns.astype(jnp.float32) / extents[course]
    return 2.0 * math.pi * fraction


def sums_kernel(slot_ref, field_ref, near_ref, link_ref, trig_ref, *rest, scale, course_list):
    out_ref = rest[-1]
    count_ev, sites = field_ref.shape[3], field_ref.shape[4]
    lane = lax.broadcasted_iota(jnp.int32, (count_ev, sites), 1)
    last_z = lane % LZ == LZ - 1
    last_row = lane >= sites - LZ
    cosine = trig_ref[0:1, :]
    sine_part = trig_ref[1:2, :]
    here = [[field_ref[0, part, colour].astype(jnp.float32) for colour in range(3)] for part in range(2)]
    phased_real = [(cosine * here[0][c] - sine_part * here[1][c]).astype(jnp.bfloat16) for c in range(3)]
    phased_imag = [(sine_part * here[0][c] + cosine * here[1][c]).astype(jnp.bfloat16) for c in range(3)]
    real_rows = jnp.concatenate(phased_real + phased_imag, axis=1)
    imag_rows = jnp.concatenate([-v for v in phased_imag] + phased_real, axis=1)
    left = jnp.concatenate([real_rows, imag_rows], axis=0)
    rows = 2 * count_ev
    for course in course_list:
        if course == 0:
            near = [[near_ref[0, part, colour].astype(jnp.float32) for colour in range(3)] for part in range(2)]
        elif course == 1:
            near = [
                [
                    jnp.where(last_row, near_ref[0, part, colour].astype(jnp.float32), pltpu.roll(here[part][colour], sites - LZ, 1))
                    for colour in range(3)
                ]
                for part in range(2)
            ]
        else:
            near = [
                [
                    jnp.where(last_z, pltpu.roll(here[part][colour], LZ - 1, 1), pltpu.roll(here[part][colour], sites - 1, 1))
                    for colour in range(3)
                ]
                for part in range(2)
            ]
        moved_real = []
        moved_imag = []
        for outer in range(3):
            real_part = 0.0
            imag_part = 0.0
            for inner in range(3):
                link_real = link_ref[0, course, 0, outer, inner : inner + 1, :]
                link_imag = link_ref[0, course, 1, outer, inner : inner + 1, :]
                real_part = real_part + link_real * near[0][inner] - link_imag * near[1][inner]
                imag_part = imag_part + link_real * near[1][inner] + link_imag * near[0][inner]
            moved_real.append(real_part.astype(jnp.bfloat16))
            moved_imag.append(imag_part.astype(jnp.bfloat16))
        right = jnp.concatenate(moved_real + moved_imag, axis=1)
        joined = lax.dot_general(left, right, (((1,), (1,)), ((), ())), preferred_element_type=jnp.float32)
        if len(course_list) == 1:
            out_ref[0] = (joined * scale).astype(out_ref.dtype)
        else:
            start = pl.multiple_of(slot_ref[course] * rows, rows)
            out_ref[0, pl.ds(start, rows), :] = (joined * scale).astype(out_ref.dtype)


def local_sums(eigenvectors, gauge_links, far_tile, row_in, directions, angle, scale):
    time_count, _, _, count_ev, sites = eigenvectors.shape
    count_ops = directions.shape[0]
    slot_of = jnp.sum(
        (directions[None, :] == jnp.arange(count_ops, dtype=jnp.int32)[:, None]) * jnp.arange(count_ops, dtype=jnp.int32)[None, :],
        axis=1,
    ).astype(jnp.int32)
    row_wide = jnp.pad(row_in, ((0, 0),) * 4 + ((sites - LZ, 0),))
    trig = jnp.stack([jnp.cos(angle), jnp.sin(angle)], 0)
    field_spec = pl.BlockSpec((1, 2, 3, count_ev, sites), lambda t, slot: (t, 0, 0, 0, 0))
    link_spec = pl.BlockSpec((1,) + gauge_links.shape[1:], lambda t, slot: (t, 0, 0, 0, 0, 0))
    trig_spec = pl.BlockSpec(trig.shape, lambda t, slot: (0, 0))
    rows = count_ops * 2 * count_ev
    near_courses = tuple(course for course in range(count_ops) if course != 0)
    first_spec = pltpu.PrefetchScalarGridSpec(
        num_scalar_prefetch=1,
        grid=(time_count,),
        in_specs=[field_spec, field_spec, link_spec, trig_spec],
        out_specs=pl.BlockSpec((1, rows, count_ev), lambda t, slot: (t, 0, 0)),
    )
    partial = pl.pallas_call(
        functools.partial(sums_kernel, scale=scale, course_list=near_courses),
        grid_spec=first_spec,
        out_shape=jax.ShapeDtypeStruct((time_count, rows, count_ev), jnp.bfloat16),
    )(slot_of, eigenvectors, row_wide, gauge_links, trig)
    second_spec = pltpu.PrefetchScalarGridSpec(
        num_scalar_prefetch=1,
        grid=(time_count,),
        in_specs=[field_spec, field_spec, link_spec, trig_spec, pl.BlockSpec(memory_space=pl.ANY)],
        out_specs=pl.BlockSpec((1, 2 * count_ev, count_ev), lambda t, slot: (t, slot[0], 0)),
    )
    return pl.pallas_call(
        functools.partial(sums_kernel, scale=scale, course_list=(0,)),
        grid_spec=second_spec,
        out_shape=jax.ShapeDtypeStruct((time_count, rows, count_ev), jnp.bfloat16),
        input_output_aliases={5: 0},
    )(slot_of, eigenvectors, far_tile, gauge_links, trig, partial)


def panel_kernel(sink_ref, source_ref, stack_ref, wide_ref, out_ref):
    count_ev = sink_ref.shape[3]
    sink_real = sink_ref[0, 0, 0]
    sink_imag = sink_ref[0, 0, 1]
    sink_wide = jnp.concatenate(
        [
            jnp.concatenate([sink_real, -sink_imag], axis=1),
            jnp.concatenate([sink_imag, sink_real], axis=1),
        ],
        axis=0,
    )
    left = jnp.dot(sink_wide, stack_ref[...], preferred_element_type=jnp.float32)
    source_stack = jnp.concatenate([source_ref[0, 0, 0], source_ref[0, 0, 1]], axis=0)
    right = jnp.dot(wide_ref[...], source_stack, preferred_element_type=jnp.float32)
    total_real = 0.0
    total_imag = 0.0
    half = NSPIN * count_ev
    for spin in range(NSPIN):
        left_real = left[:count_ev, spin * count_ev : (spin + 1) * count_ev]
        left_imag = left[count_ev:, spin * count_ev : (spin + 1) * count_ev]
        right_real = right[spin * count_ev : (spin + 1) * count_ev]
        right_imag = right[half + spin * count_ev : half + (spin + 1) * count_ev]
        total_real = total_real + left_real * right_real + left_imag * right_imag
        total_imag = total_imag + left_imag * right_real - left_real * right_imag
    out_ref[0, 0:1, :] = jnp.sum(total_real, axis=0, keepdims=True)
    out_ref[0, 1:2, :] = jnp.sum(total_imag, axis=0, keepdims=True)


def contract_panel(gathered, panel):
    count_ops, count_ev = gathered.shape[1], panel.shape[1]
    stack = panel.reshape(2 * count_ev, NSPIN * count_ev)
    blocks = panel.reshape(2, count_ev, NSPIN, count_ev).transpose(0, 2, 1, 3).reshape(2, NSPIN * count_ev, count_ev)
    wide = jnp.concatenate(
        [
            jnp.concatenate([blocks[0], -blocks[1]], axis=1),
            jnp.concatenate([blocks[1], blocks[0]], axis=1),
        ],
        axis=0,
    )
    sums = pl.pallas_call(
        panel_kernel,
        grid=(count_ops,),
        in_specs=[
            pl.BlockSpec((1, 1, 2, count_ev, count_ev), lambda a: (0, a, 0, 0, 0)),
            pl.BlockSpec((1, 1, 2, count_ev, count_ev), lambda a: (1, a, 0, 0, 0)),
            pl.BlockSpec(stack.shape, lambda a: (0, 0)),
            pl.BlockSpec(wide.shape, lambda a: (0, 0)),
        ],
        out_specs=pl.BlockSpec((1, 2, count_ev), lambda a: (a, 0, 0)),
        out_shape=jax.ShapeDtypeStruct((count_ops, 2, count_ev), jnp.float32),
    )(gathered, gathered, stack, wide)
    return jnp.sum(sums, axis=-1) * (1.0 / (16.0 * count_ev))


def body(eigenvectors, gauge_links, perambulators, directions, momenta, pair_times):
    time_count = eigenvectors.shape[0]
    count_ev = eigenvectors.shape[3]
    local_sites = eigenvectors.shape[4]
    count_slabs = lax.axis_size("slab")
    nspace = NSPIN * count_slabs
    member = lax.axis_index("member")
    device = lax.axis_index("slab") * NSPIN + member
    half_rows = LY // 2
    extent_x = nspace // 2
    column = jnp.arange(local_sites, dtype=jnp.int32)
    coord_x = device // 2 + 0 * column
    coord_y = device % 2 * half_rows + column // LZ
    coord_z = column % LZ
    angle = phase_angles(momenta, (coord_x, coord_y, coord_z), (extent_x, LY, LZ))[0]
    far_tile = shifted(eigenvectors, SPACE, -2)
    row_in = swapped(eigenvectors[..., :LZ], SPACE, 0)
    scale = 1.0 / math.sqrt(3.0 * extent_x * LY * LZ)
    partial = local_sums(eigenvectors, gauge_links, far_tile, row_in, directions, angle, scale)
    own_rows = lax.psum_scatter(partial, SPACE, scatter_dimension=1, tiled=True)
    rows = own_rows.shape[1]
    slabs = jnp.arange(count_slabs, dtype=jnp.int32)
    wanted = jnp.stack([pair_times[slabs, 1], pair_times[slabs, 0]], 1)
    outgoing = jnp.take(own_rows, wanted.reshape(-1), axis=0).reshape(count_slabs, 2, rows, count_ev)
    across = lax.all_to_all(outgoing, "slab", 0, 0, tiled=True)
    spread = jnp.broadcast_to(across[None], (NSPIN,) + across.shape)
    within = lax.all_to_all(spread, "member", 0, 0, tiled=True)
    incoming = within.transpose(1, 0, 2, 3, 4).reshape(nspace, 2, rows, count_ev)
    count_ops = partial.shape[1] // (2 * count_ev)
    gathered = incoming.transpose(1, 0, 2, 3).reshape(2, count_ops, 2, count_ev, count_ev)
    correlators = contract_panel(gathered, perambulators[0])[None]
    return (own_rows, correlators)


def solution(mesh):
    count_cfg = mesh.shape["cfg"]
    count_slabs = mesh.shape["space"] // NSPIN
    split = Mesh(mesh.devices.reshape(count_cfg, count_slabs, NSPIN), ("cfg",) + SPACE)
    placed = (
        P("cfg", None, None, None, SPACE),
        P("cfg", None, None, None, None, SPACE),
        P(("cfg",) + SPACE, None, None, None),
        P(),
        P(),
        P(),
    )
    return jax.shard_map(
        body,
        mesh=split,
        in_specs=placed,
        out_specs=(P("cfg", SPACE, None), P(("cfg",) + SPACE, None, None)),
        check_vma=False,
    )
```

```python
import functools
import math

import jax
import jax.numpy as jnp
from jax import lax
from jax.experimental import pallas as pl
from jax.experimental.pallas import tpu as pltpu
from jax.sharding import Mesh, PartitionSpec as P

NSPIN = 4
LY = 32
LZ = 8
SPACE = ("slab", "member")


def shifted(block, axis, distance):
    devices = range(lax.axis_size(axis))
    route = [((i - distance) % len(devices), i) for i in devices]
    return lax.ppermute(block, axis, route)


def swapped(value, axis, bit):
    return lax.ppermute(value, axis, [(i, i ^ 1 << bit) for i in range(lax.axis_size(axis))])


def phase_angles(momenta, coords, extents):
    fraction = 0.0
    for course in range(3):
        turns = momenta[:, course : course + 1] * coords[course][None, :] % extents[course]
        fraction = fraction + turns.astype(jnp.float32) / extents[course]
    return 2.0 * math.pi * fraction


def sums_kernel(slot_ref, field_ref, near_ref, link_ref, trig_ref, *rest, scale, course_list):
    out_ref = rest[-1] if len(course_list) == 1 else rest[0]
    count_ev, sites = field_ref.shape[3], field_ref.shape[4]
    lane = lax.broadcasted_iota(jnp.int32, (count_ev, sites), 1)
    last_z = lane % LZ == LZ - 1
    last_row = lane >= sites - LZ
    if len(course_list) == 1:
        left = trig_ref[0]
    else:
        cosine = trig_ref[0:1, :]
        sine_part = trig_ref[1:2, :]
        here = [[field_ref[0, part, colour].astype(jnp.float32) for colour in range(3)] for part in range(2)]
        phased_real = [(cosine * here[0][c] - sine_part * here[1][c]).astype(jnp.bfloat16) for c in range(3)]
        phased_imag = [(sine_part * here[0][c] + cosine * here[1][c]).astype(jnp.bfloat16) for c in range(3)]
        real_rows = jnp.concatenate(phased_real + phased_imag, axis=1)
        imag_rows = jnp.concatenate([-v for v in phased_imag] + phased_real, axis=1)
        left = jnp.concatenate([real_rows, imag_rows], axis=0)
        rest[1][0] = left
    rows = 2 * count_ev
    for course in course_list:
        if course == 0:
            near = [[near_ref[0, part, colour].astype(jnp.float32) for colour in range(3)] for part in range(2)]
        elif course == 1:
            near = [
                [
                    jnp.where(last_row, near_ref[0, part, colour].astype(jnp.float32), pltpu.roll(here[part][colour], sites - LZ, 1))
                    for colour in range(3)
                ]
                for part in range(2)
            ]
        else:
            near = [
                [
                    jnp.where(last_z, pltpu.roll(here[part][colour], LZ - 1, 1), pltpu.roll(here[part][colour], sites - 1, 1))
                    for colour in range(3)
                ]
                for part in range(2)
            ]
        moved_real = []
        moved_imag = []
        for outer in range(3):
            real_part = 0.0
            imag_part = 0.0
            for inner in range(3):
                link_real = link_ref[0, course, 0, outer, inner : inner + 1, :]
                link_imag = link_ref[0, course, 1, outer, inner : inner + 1, :]
                real_part = real_part + link_real * near[0][inner] - link_imag * near[1][inner]
                imag_part = imag_part + link_real * near[1][inner] + link_imag * near[0][inner]
            moved_real.append(real_part.astype(jnp.bfloat16))
            moved_imag.append(imag_part.astype(jnp.bfloat16))
        right = jnp.concatenate(moved_real + moved_imag, axis=1)
        joined = lax.dot_general(left, right, (((1,), (1,)), ((), ())), preferred_element_type=jnp.float32)
        if len(course_list) == 1:
            out_ref[0] = (joined * scale).astype(out_ref.dtype)
        else:
            start = pl.multiple_of(slot_ref[course] * rows, rows)
            out_ref[0, pl.ds(start, rows), :] = (joined * scale).astype(out_ref.dtype)


def local_sums(eigenvectors, gauge_links, far_tile, row_in, directions, angle, scale):
    time_count, _, _, count_ev, sites = eigenvectors.shape
    count_ops = directions.shape[0]
    slot_of = jnp.sum(
        (directions[None, :] == jnp.arange(count_ops, dtype=jnp.int32)[:, None]) * jnp.arange(count_ops, dtype=jnp.int32)[None, :],
        axis=1,
    ).astype(jnp.int32)
    row_wide = jnp.pad(row_in, ((0, 0),) * 4 + ((sites - LZ, 0),))
    trig = jnp.stack([jnp.cos(angle), jnp.sin(angle)], 0)
    field_spec = pl.BlockSpec((1, 2, 3, count_ev, sites), lambda t, slot: (t, 0, 0, 0, 0))
    link_spec = pl.BlockSpec((1,) + gauge_links.shape[1:], lambda t, slot: (t, 0, 0, 0, 0, 0))
    trig_spec = pl.BlockSpec(trig.shape, lambda t, slot: (0, 0))
    rows = count_ops * 2 * count_ev
    near_courses = tuple(course for course in range(count_ops) if course != 0)
    left_rows = 2 * count_ev
    left_spec = pl.BlockSpec((1, left_rows, 6 * sites), lambda t, slot: (t, 0, 0))
    first_spec = pltpu.PrefetchScalarGridSpec(
        num_scalar_prefetch=1,
        grid=(time_count,),
        in_specs=[field_spec, field_spec, link_spec, trig_spec],
        out_specs=[pl.BlockSpec((1, rows, count_ev), lambda t, slot: (t, 0, 0)), left_spec],
    )
    partial, left = pl.pallas_call(
        functools.partial(sums_kernel, scale=scale, course_list=near_courses),
        grid_spec=first_spec,
        out_shape=(
            jax.ShapeDtypeStruct((time_count, rows, count_ev), jnp.bfloat16),
            jax.ShapeDtypeStruct((time_count, left_rows, 6 * sites), jnp.bfloat16),
        ),
    )(slot_of, eigenvectors, row_wide, gauge_links, trig)
    second_spec = pltpu.PrefetchScalarGridSpec(
        num_scalar_prefetch=1,
        grid=(time_count,),
        in_specs=[pl.BlockSpec(memory_space=pl.ANY), field_spec, link_spec, left_spec, pl.BlockSpec(memory_space=pl.ANY)],
        out_specs=pl.BlockSpec((1, 2 * count_ev, count_ev), lambda t, slot: (t, slot[0], 0)),
    )
    return pl.pallas_call(
        functools.partial(sums_kernel, scale=scale, course_list=(0,)),
        grid_spec=second_spec,
        out_shape=jax.ShapeDtypeStruct((time_count, rows, count_ev), jnp.bfloat16),
        input_output_aliases={5: 0},
    )(slot_of, eigenvectors, far_tile, gauge_links, left, partial)


def panel_kernel(sink_ref, source_ref, stack_ref, wide_ref, out_ref):
    count_ev = sink_ref.shape[3]
    sink_real = sink_ref[0, 0, 0]
    sink_imag = sink_ref[0, 0, 1]
    sink_wide = jnp.concatenate(
        [
            jnp.concatenate([sink_real, -sink_imag], axis=1),
            jnp.concatenate([sink_imag, sink_real], axis=1),
        ],
        axis=0,
    )
    left = jnp.dot(sink_wide, stack_ref[...], preferred_element_type=jnp.float32)
    source_stack = jnp.concatenate([source_ref[0, 0, 0], source_ref[0, 0, 1]], axis=0)
    right = jnp.dot(wide_ref[...], source_stack, preferred_element_type=jnp.float32)
    total_real = 0.0
    total_imag = 0.0
    half = NSPIN * count_ev
    for spin in range(NSPIN):
        left_real = left[:count_ev, spin * count_ev : (spin + 1) * count_ev]
        left_imag = left[count_ev:, spin * count_ev : (spin + 1) * count_ev]
        right_real = right[spin * count_ev : (spin + 1) * count_ev]
        right_imag = right[half + spin * count_ev : half + (spin + 1) * count_ev]
        total_real = total_real + left_real * right_real + left_imag * right_imag
        total_imag = total_imag + left_imag * right_real - left_real * right_imag
    out_ref[0, 0:1, :] = jnp.sum(total_real, axis=0, keepdims=True)
    out_ref[0, 1:2, :] = jnp.sum(total_imag, axis=0, keepdims=True)


def contract_panel(gathered, panel):
    count_ops, count_ev = gathered.shape[1], panel.shape[1]
    stack = panel.reshape(2 * count_ev, NSPIN * count_ev)
    blocks = panel.reshape(2, count_ev, NSPIN, count_ev).transpose(0, 2, 1, 3).reshape(2, NSPIN * count_ev, count_ev)
    wide = jnp.concatenate(
        [
            jnp.concatenate([blocks[0], -blocks[1]], axis=1),
            jnp.concatenate([blocks[1], blocks[0]], axis=1),
        ],
        axis=0,
    )
    sums = pl.pallas_call(
        panel_kernel,
        grid=(count_ops,),
        in_specs=[
            pl.BlockSpec((1, 1, 2, count_ev, count_ev), lambda a: (0, a, 0, 0, 0)),
            pl.BlockSpec((1, 1, 2, count_ev, count_ev), lambda a: (1, a, 0, 0, 0)),
            pl.BlockSpec(stack.shape, lambda a: (0, 0)),
            pl.BlockSpec(wide.shape, lambda a: (0, 0)),
        ],
        out_specs=pl.BlockSpec((1, 2, count_ev), lambda a: (a, 0, 0)),
        out_shape=jax.ShapeDtypeStruct((count_ops, 2, count_ev), jnp.float32),
    )(gathered, gathered, stack, wide)
    return jnp.sum(sums, axis=-1) * (1.0 / (16.0 * count_ev))


def body(eigenvectors, gauge_links, perambulators, directions, momenta, pair_times):
    time_count = eigenvectors.shape[0]
    count_ev = eigenvectors.shape[3]
    local_sites = eigenvectors.shape[4]
    count_slabs = lax.axis_size("slab")
    nspace = NSPIN * count_slabs
    member = lax.axis_index("member")
    device = lax.axis_index("slab") * NSPIN + member
    half_rows = LY // 2
    extent_x = nspace // 2
    column = jnp.arange(local_sites, dtype=jnp.int32)
    coord_x = device // 2 + 0 * column
    coord_y = device % 2 * half_rows + column // LZ
    coord_z = column % LZ
    angle = phase_angles(momenta, (coord_x, coord_y, coord_z), (extent_x, LY, LZ))[0]
    far_tile = shifted(eigenvectors, SPACE, -2)
    row_in = swapped(eigenvectors[..., :LZ], SPACE, 0)
    scale = 1.0 / math.sqrt(3.0 * extent_x * LY * LZ)
    partial = local_sums(eigenvectors, gauge_links, far_tile, row_in, directions, angle, scale)
    own_rows = lax.psum_scatter(partial, SPACE, scatter_dimension=1, tiled=True)
    rows = own_rows.shape[1]
    slabs = jnp.arange(count_slabs, dtype=jnp.int32)
    wanted = jnp.stack([pair_times[slabs, 1], pair_times[slabs, 0]], 1)
    outgoing = jnp.take(own_rows, wanted.reshape(-1), axis=0).reshape(count_slabs, 2, rows, count_ev)
    across = lax.all_to_all(outgoing, "slab", 0, 0, tiled=True)
    spread = jnp.broadcast_to(across[None], (NSPIN,) + across.shape)
    within = lax.all_to_all(spread, "member", 0, 0, tiled=True)
    incoming = within.transpose(1, 0, 2, 3, 4).reshape(nspace, 2, rows, count_ev)
    count_ops = partial.shape[1] // (2 * count_ev)
    gathered = incoming.transpose(1, 0, 2, 3).reshape(2, count_ops, 2, count_ev, count_ev)
    correlators = contract_panel(gathered, perambulators[0])[None]
    return (own_rows, correlators)


def solution(mesh):
    count_cfg = mesh.shape["cfg"]
    count_slabs = mesh.shape["space"] // NSPIN
    split = Mesh(mesh.devices.reshape(count_cfg, count_slabs, NSPIN), ("cfg",) + SPACE)
    placed = (
        P("cfg", None, None, None, SPACE),
        P("cfg", None, None, None, None, SPACE),
        P(("cfg",) + SPACE, None, None, None),
        P(),
        P(),
        P(),
    )
    return jax.shard_map(
        body,
        mesh=split,
        in_specs=placed,
        out_specs=(P("cfg", SPACE, None), P(("cfg",) + SPACE, None, None)),
        check_vma=False,
    )
```

```python
import functools
import math

import jax
import jax.numpy as jnp
from jax import lax
from jax.experimental import pallas as pl
from jax.experimental.pallas import tpu as pltpu
from jax.sharding import Mesh, PartitionSpec as P

NSPIN = 4
LY = 32
LZ = 8
SPACE = ("slab", "member")


def shifted(block, axis, distance):
    devices = range(lax.axis_size(axis))
    route = [((i - distance) % len(devices), i) for i in devices]
    return lax.ppermute(block, axis, route)


def swapped(value, axis, bit):
    return lax.ppermute(value, axis, [(i, i ^ 1 << bit) for i in range(lax.axis_size(axis))])


def phase_angles(momenta, coords, extents):
    fraction = 0.0
    for course in range(3):
        turns = momenta[:, course : course + 1] * coords[course][None, :] % extents[course]
        fraction = fraction + turns.astype(jnp.float32) / extents[course]
    return 2.0 * math.pi * fraction


def sums_kernel(slot_ref, field_ref, near_ref, link_ref, trig_ref, *rest, scale, course_list):
    out_ref = rest[-1] if len(course_list) == 1 else rest[0]
    count_ev, sites = field_ref.shape[3], field_ref.shape[4]
    lane = lax.broadcasted_iota(jnp.int32, (count_ev, sites), 1)
    last_z = lane % LZ == LZ - 1
    last_row = lane >= sites - LZ
    if len(course_list) == 1:
        left = trig_ref[0]
    else:
        cosine = trig_ref[0:1, :]
        sine_part = trig_ref[1:2, :]
        here = [[field_ref[0, part, colour].astype(jnp.float32) for colour in range(3)] for part in range(2)]
        phased_real = [(cosine * here[0][c] - sine_part * here[1][c]).astype(jnp.bfloat16) for c in range(3)]
        phased_imag = [(sine_part * here[0][c] + cosine * here[1][c]).astype(jnp.bfloat16) for c in range(3)]
        real_rows = jnp.concatenate(phased_real + phased_imag, axis=1)
        imag_rows = jnp.concatenate([-v for v in phased_imag] + phased_real, axis=1)
        left = jnp.concatenate([real_rows, imag_rows], axis=0)
        rest[1][0] = left
    rows = 2 * count_ev
    for course in course_list:
        if course == 0:
            near = [[near_ref[0, part, colour].astype(jnp.float32) for colour in range(3)] for part in range(2)]
        elif course == 1:
            near = [
                [
                    jnp.where(last_row, near_ref[0, part, colour].astype(jnp.float32), pltpu.roll(here[part][colour], sites - LZ, 1))
                    for colour in range(3)
                ]
                for part in range(2)
            ]
        else:
            near = [
                [
                    jnp.where(last_z, pltpu.roll(here[part][colour], LZ - 1, 1), pltpu.roll(here[part][colour], sites - 1, 1))
                    for colour in range(3)
                ]
                for part in range(2)
            ]
        moved_real = []
        moved_imag = []
        for outer in range(3):
            real_part = 0.0
            imag_part = 0.0
            for inner in range(3):
                link_real = link_ref[0, course, 0, outer, inner : inner + 1, :]
                link_imag = link_ref[0, course, 1, outer, inner : inner + 1, :]
                real_part = real_part + link_real * near[0][inner] - link_imag * near[1][inner]
                imag_part = imag_part + link_real * near[1][inner] + link_imag * near[0][inner]
            moved_real.append(real_part.astype(jnp.bfloat16))
            moved_imag.append(imag_part.astype(jnp.bfloat16))
        right = jnp.concatenate(moved_real + moved_imag, axis=1)
        joined = lax.dot_general(left, right, (((1,), (1,)), ((), ())), preferred_element_type=jnp.float32)
        if len(course_list) == 1:
            out_ref[0] = (joined * scale).astype(out_ref.dtype)
        else:
            start = pl.multiple_of(slot_ref[course] * rows, rows)
            out_ref[0, pl.ds(start, rows), :] = (joined * scale).astype(out_ref.dtype)


def local_sums(eigenvectors, gauge_links, far_tile, row_in, directions, angle, scale):
    time_count, _, _, count_ev, sites = eigenvectors.shape
    count_ops = directions.shape[0]
    slot_of = jnp.sum(
        (directions[None, :] == jnp.arange(count_ops, dtype=jnp.int32)[:, None]) * jnp.arange(count_ops, dtype=jnp.int32)[None, :],
        axis=1,
    ).astype(jnp.int32)
    row_wide = jnp.pad(row_in, ((0, 0),) * 4 + ((sites - LZ, 0),))
    trig = jnp.stack([jnp.cos(angle), jnp.sin(angle)], 0)
    field_spec = pl.BlockSpec((1, 2, 3, count_ev, sites), lambda t, slot: (t, 0, 0, 0, 0))
    link_spec = pl.BlockSpec((1,) + gauge_links.shape[1:], lambda t, slot: (t, 0, 0, 0, 0, 0))
    trig_spec = pl.BlockSpec(trig.shape, lambda t, slot: (0, 0))
    rows = count_ops * 2 * count_ev
    near_courses = tuple(course for course in range(count_ops) if course != 0)
    left_rows = 2 * count_ev
    left_spec = pl.BlockSpec((1, left_rows, 6 * sites), lambda t, slot: (t, 0, 0))
    first_spec = pltpu.PrefetchScalarGridSpec(
        num_scalar_prefetch=1,
        grid=(time_count,),
        in_specs=[field_spec, field_spec, link_spec, trig_spec],
        out_specs=[pl.BlockSpec((1, rows, count_ev), lambda t, slot: (t, 0, 0)), left_spec],
    )
    partial, left = pl.pallas_call(
        functools.partial(sums_kernel, scale=scale, course_list=near_courses),
        grid_spec=first_spec,
        out_shape=(
            jax.ShapeDtypeStruct((time_count, rows, count_ev), jnp.bfloat16),
            jax.ShapeDtypeStruct((time_count, left_rows, 6 * sites), jnp.bfloat16),
        ),
    )(slot_of, eigenvectors, row_wide, gauge_links, trig)
    second_spec = pltpu.PrefetchScalarGridSpec(
        num_scalar_prefetch=1,
        grid=(time_count,),
        in_specs=[pl.BlockSpec(memory_space=pl.ANY), field_spec, link_spec, left_spec, pl.BlockSpec(memory_space=pl.ANY)],
        out_specs=pl.BlockSpec((1, 2 * count_ev, count_ev), lambda t, slot: (t, slot[0], 0)),
    )
    return pl.pallas_call(
        functools.partial(sums_kernel, scale=scale, course_list=(0,)),
        grid_spec=second_spec,
        out_shape=jax.ShapeDtypeStruct((time_count, rows, count_ev), jnp.bfloat16),
        input_output_aliases={5: 0},
    )(slot_of, eigenvectors, far_tile, gauge_links, left, partial)


def panel_kernel(sink_ref, source_ref, stack_ref, wide_ref, out_ref):
    count_ev = sink_ref.shape[3]
    sink_real = sink_ref[0, 0, 0]
    sink_imag = sink_ref[0, 0, 1]
    sink_wide = jnp.concatenate(
        [
            jnp.concatenate([sink_real, -sink_imag], axis=1),
            jnp.concatenate([sink_imag, sink_real], axis=1),
        ],
        axis=0,
    )
    left = jnp.dot(sink_wide, stack_ref[...], preferred_element_type=jnp.float32)
    source_stack = jnp.concatenate([source_ref[0, 0, 0], source_ref[0, 0, 1]], axis=0)
    right = jnp.dot(wide_ref[...], source_stack, preferred_element_type=jnp.float32)
    total_real = 0.0
    total_imag = 0.0
    half = NSPIN * count_ev
    for spin in range(NSPIN):
        left_real = left[:count_ev, spin * count_ev : (spin + 1) * count_ev]
        left_imag = left[count_ev:, spin * count_ev : (spin + 1) * count_ev]
        right_real = right[spin * count_ev : (spin + 1) * count_ev]
        right_imag = right[half + spin * count_ev : half + (spin + 1) * count_ev]
        total_real = total_real + left_real * right_real + left_imag * right_imag
        total_imag = total_imag + left_imag * right_real - left_real * right_imag
    out_ref[0, 0:1, :] = jnp.sum(total_real, axis=0, keepdims=True)
    out_ref[0, 1:2, :] = jnp.sum(total_imag, axis=0, keepdims=True)


def contract_panel(gathered, panel):
    count_ops, count_ev = gathered.shape[1], panel.shape[1]
    stack = panel.reshape(2 * count_ev, NSPIN * count_ev)
    blocks = panel.reshape(2, count_ev, NSPIN, count_ev).transpose(0, 2, 1, 3).reshape(2, NSPIN * count_ev, count_ev)
    wide = jnp.concatenate(
        [
            jnp.concatenate([blocks[0], -blocks[1]], axis=1),
            jnp.concatenate([blocks[1], blocks[0]], axis=1),
        ],
        axis=0,
    )
    sums = pl.pallas_call(
        panel_kernel,
        grid=(count_ops,),
        in_specs=[
            pl.BlockSpec((1, 1, 2, count_ev, count_ev), lambda a: (0, a, 0, 0, 0)),
            pl.BlockSpec((1, 1, 2, count_ev, count_ev), lambda a: (1, a, 0, 0, 0)),
            pl.BlockSpec(stack.shape, lambda a: (0, 0)),
            pl.BlockSpec(wide.shape, lambda a: (0, 0)),
        ],
        out_specs=pl.BlockSpec((1, 2, count_ev), lambda a: (a, 0, 0)),
        out_shape=jax.ShapeDtypeStruct((count_ops, 2, count_ev), jnp.float32),
    )(gathered, gathered, stack, wide)
    return jnp.sum(sums, axis=-1) * (1.0 / (16.0 * count_ev))


def body(eigenvectors, gauge_links, perambulators, directions, momenta, pair_times):
    time_count = eigenvectors.shape[0]
    count_ev = eigenvectors.shape[3]
    local_sites = eigenvectors.shape[4]
    count_slabs = lax.axis_size("slab")
    nspace = NSPIN * count_slabs
    member = lax.axis_index("member")
    device = lax.axis_index("slab") * NSPIN + member
    half_rows = LY // 2
    extent_x = nspace // 2
    column = jnp.arange(local_sites, dtype=jnp.int32)
    coord_x = device // 2 + 0 * column
    coord_y = device % 2 * half_rows + column // LZ
    coord_z = column % LZ
    angle = phase_angles(momenta, (coord_x, coord_y, coord_z), (extent_x, LY, LZ))[0]
    far_tile = shifted(eigenvectors, SPACE, -2)
    row_in = swapped(eigenvectors[..., :LZ], SPACE, 0)
    scale = 1.0 / math.sqrt(3.0 * extent_x * LY * LZ)
    partial = local_sums(eigenvectors, gauge_links, far_tile, row_in, directions, angle, scale)
    rows = partial.shape[1] // nspace
    blocks = partial.reshape(time_count, count_slabs, NSPIN, rows, count_ev)
    slab_sums = lax.psum_scatter(blocks, "slab", scatter_dimension=1, tiled=True)
    own_rows = lax.psum_scatter(slab_sums, "member", scatter_dimension=2, tiled=True)
    own_rows = own_rows.reshape(time_count, rows, count_ev)
    slabs = jnp.arange(count_slabs, dtype=jnp.int32)
    wanted = jnp.stack([pair_times[slabs, 1], pair_times[slabs, 0]], 1)
    outgoing = jnp.take(own_rows, wanted.reshape(-1), axis=0).reshape(count_slabs, 2, rows, count_ev)
    across = lax.all_to_all(outgoing, "slab", 0, 0, tiled=True)
    spread = jnp.broadcast_to(across[None], (NSPIN,) + across.shape)
    within = lax.all_to_all(spread, "member", 0, 0, tiled=True)
    incoming = within.transpose(1, 0, 2, 3, 4).reshape(nspace, 2, rows, count_ev)
    count_ops = partial.shape[1] // (2 * count_ev)
    gathered = incoming.transpose(1, 0, 2, 3).reshape(2, count_ops, 2, count_ev, count_ev)
    correlators = contract_panel(gathered, perambulators[0])[None]
    return (own_rows, correlators)


def solution(mesh):
    count_cfg = mesh.shape["cfg"]
    count_slabs = mesh.shape["space"] // NSPIN
    split = Mesh(mesh.devices.reshape(count_cfg, count_slabs, NSPIN), ("cfg",) + SPACE)
    placed = (
        P("cfg", None, None, None, SPACE),
        P("cfg", None, None, None, None, SPACE),
        P(("cfg",) + SPACE, None, None, None),
        P(),
        P(),
        P(),
    )
    return jax.shard_map(
        body,
        mesh=split,
        in_specs=placed,
        out_specs=(P("cfg", SPACE, None), P(("cfg",) + SPACE, None, None)),
        check_vma=False,
    )
```

```python
import functools
import math

import jax
import jax.numpy as jnp
from jax import lax
from jax.experimental import pallas as pl
from jax.experimental.pallas import tpu as pltpu
from jax.sharding import Mesh, PartitionSpec as P

NSPIN = 4
LY = 32
LZ = 8
SPACE = ("slab", "member")


def shifted(block, axis, distance):
    devices = range(lax.axis_size(axis))
    route = [((i - distance) % len(devices), i) for i in devices]
    return lax.ppermute(block, axis, route)


def swapped(value, axis, bit):
    return lax.ppermute(value, axis, [(i, i ^ 1 << bit) for i in range(lax.axis_size(axis))])


def phase_angles(momenta, coords, extents):
    fraction = 0.0
    for course in range(3):
        turns = momenta[:, course : course + 1] * coords[course][None, :] % extents[course]
        fraction = fraction + turns.astype(jnp.float32) / extents[course]
    return 2.0 * math.pi * fraction


def sums_kernel(slot_ref, field_ref, near_ref, link_ref, trig_ref, *rest, scale, course_list):
    out_ref = rest[-1] if len(course_list) == 1 else rest[0]
    count_ev, sites = field_ref.shape[3], field_ref.shape[4]
    lane = lax.broadcasted_iota(jnp.int32, (count_ev, sites), 1)
    last_z = lane % LZ == LZ - 1
    last_row = lane >= sites - LZ
    if len(course_list) == 1:
        left = trig_ref[0]
    else:
        cosine = trig_ref[0:1, :]
        sine_part = trig_ref[1:2, :]
        here = [[field_ref[0, part, colour].astype(jnp.float32) for colour in range(3)] for part in range(2)]
        phased_real = [(cosine * here[0][c] - sine_part * here[1][c]).astype(jnp.bfloat16) for c in range(3)]
        phased_imag = [(sine_part * here[0][c] + cosine * here[1][c]).astype(jnp.bfloat16) for c in range(3)]
        real_rows = jnp.concatenate(phased_real + phased_imag, axis=1)
        imag_rows = jnp.concatenate([-v for v in phased_imag] + phased_real, axis=1)
        left = jnp.concatenate([real_rows, imag_rows], axis=0)
        rest[1][0] = left
    rows = 2 * count_ev
    for course in course_list:
        if course == 0:
            near = [[near_ref[0, part, colour].astype(jnp.float32) for colour in range(3)] for part in range(2)]
        elif course == 1:
            near = [
                [
                    jnp.where(last_row, near_ref[0, part, colour].astype(jnp.float32), pltpu.roll(here[part][colour], sites - LZ, 1))
                    for colour in range(3)
                ]
                for part in range(2)
            ]
        else:
            near = [
                [
                    jnp.where(last_z, pltpu.roll(here[part][colour], LZ - 1, 1), pltpu.roll(here[part][colour], sites - 1, 1))
                    for colour in range(3)
                ]
                for part in range(2)
            ]
        moved_real = []
        moved_imag = []
        for outer in range(3):
            real_part = 0.0
            imag_part = 0.0
            for inner in range(3):
                link_real = link_ref[0, course, 0, outer, inner : inner + 1, :]
                link_imag = link_ref[0, course, 1, outer, inner : inner + 1, :]
                real_part = real_part + link_real * near[0][inner] - link_imag * near[1][inner]
                imag_part = imag_part + link_real * near[1][inner] + link_imag * near[0][inner]
            moved_real.append(real_part.astype(jnp.bfloat16))
            moved_imag.append(imag_part.astype(jnp.bfloat16))
        right = jnp.concatenate(moved_real + moved_imag, axis=1)
        joined = lax.dot_general(left, right, (((1,), (1,)), ((), ())), preferred_element_type=jnp.float32)
        if len(course_list) == 1:
            out_ref[0] = (joined * scale).astype(out_ref.dtype)
        else:
            start = pl.multiple_of(slot_ref[course] * rows, rows)
            out_ref[0, pl.ds(start, rows), :] = (joined * scale).astype(out_ref.dtype)


def local_sums(eigenvectors, gauge_links, far_tile, row_in, directions, angle, scale):
    time_count, _, _, count_ev, sites = eigenvectors.shape
    count_ops = directions.shape[0]
    slot_of = jnp.sum(
        (directions[None, :] == jnp.arange(count_ops, dtype=jnp.int32)[:, None]) * jnp.arange(count_ops, dtype=jnp.int32)[None, :],
        axis=1,
    ).astype(jnp.int32)
    row_wide = jnp.pad(row_in, ((0, 0),) * 4 + ((sites - LZ, 0),))
    trig = jnp.stack([jnp.cos(angle), jnp.sin(angle)], 0)
    field_spec = pl.BlockSpec((1, 2, 3, count_ev, sites), lambda t, slot: (t, 0, 0, 0, 0))
    link_spec = pl.BlockSpec((1,) + gauge_links.shape[1:], lambda t, slot: (t, 0, 0, 0, 0, 0))
    trig_spec = pl.BlockSpec(trig.shape, lambda t, slot: (0, 0))
    rows = count_ops * 2 * count_ev
    near_courses = tuple(course for course in range(count_ops) if course != 0)
    left_rows = 2 * count_ev
    left_spec = pl.BlockSpec((1, left_rows, 6 * sites), lambda t, slot: (t, 0, 0))
    first_spec = pltpu.PrefetchScalarGridSpec(
        num_scalar_prefetch=1,
        grid=(time_count,),
        in_specs=[field_spec, field_spec, link_spec, trig_spec],
        out_specs=[pl.BlockSpec((1, rows, count_ev), lambda t, slot: (t, 0, 0)), left_spec],
    )
    partial, left = pl.pallas_call(
        functools.partial(sums_kernel, scale=scale, course_list=near_courses),
        grid_spec=first_spec,
        out_shape=(
            jax.ShapeDtypeStruct((time_count, rows, count_ev), jnp.bfloat16),
            jax.ShapeDtypeStruct((time_count, left_rows, 6 * sites), jnp.bfloat16),
        ),
    )(slot_of, eigenvectors, row_wide, gauge_links, trig)
    for first, far_part in far_tile:
        span = far_part.shape[0]
        second_spec = pltpu.PrefetchScalarGridSpec(
            num_scalar_prefetch=1,
            grid=(span,),
            in_specs=[
                pl.BlockSpec(memory_space=pl.ANY),
                pl.BlockSpec((1, 2, 3, count_ev, sites), lambda t, slot: (t, 0, 0, 0, 0)),
                pl.BlockSpec((1,) + gauge_links.shape[1:], lambda t, slot, first=first: (t + first, 0, 0, 0, 0, 0)),
                pl.BlockSpec((1, left_rows, 6 * sites), lambda t, slot, first=first: (t + first, 0, 0)),
                pl.BlockSpec(memory_space=pl.ANY),
            ],
            out_specs=pl.BlockSpec((1, 2 * count_ev, count_ev), lambda t, slot, first=first: (t + first, slot[0], 0)),
        )
        partial = pl.pallas_call(
            functools.partial(sums_kernel, scale=scale, course_list=(0,)),
            grid_spec=second_spec,
            out_shape=jax.ShapeDtypeStruct((time_count, rows, count_ev), jnp.bfloat16),
            input_output_aliases={5: 0},
        )(slot_of, eigenvectors, far_part, gauge_links, left, partial)
    return partial


def panel_kernel(sink_ref, source_ref, stack_ref, wide_ref, out_ref):
    count_ev = sink_ref.shape[3]
    sink_real = sink_ref[0, 0, 0]
    sink_imag = sink_ref[0, 0, 1]
    sink_wide = jnp.concatenate(
        [
            jnp.concatenate([sink_real, -sink_imag], axis=1),
            jnp.concatenate([sink_imag, sink_real], axis=1),
        ],
        axis=0,
    )
    left = jnp.dot(sink_wide, stack_ref[...], preferred_element_type=jnp.float32)
    source_stack = jnp.concatenate([source_ref[0, 0, 0], source_ref[0, 0, 1]], axis=0)
    right = jnp.dot(wide_ref[...], source_stack, preferred_element_type=jnp.float32)
    total_real = 0.0
    total_imag = 0.0
    half = NSPIN * count_ev
    for spin in range(NSPIN):
        left_real = left[:count_ev, spin * count_ev : (spin + 1) * count_ev]
        left_imag = left[count_ev:, spin * count_ev : (spin + 1) * count_ev]
        right_real = right[spin * count_ev : (spin + 1) * count_ev]
        right_imag = right[half + spin * count_ev : half + (spin + 1) * count_ev]
        total_real = total_real + left_real * right_real + left_imag * right_imag
        total_imag = total_imag + left_imag * right_real - left_real * right_imag
    out_ref[0, 0:1, :] = jnp.sum(total_real, axis=0, keepdims=True)
    out_ref[0, 1:2, :] = jnp.sum(total_imag, axis=0, keepdims=True)


def contract_panel(gathered, panel):
    count_ops, count_ev = gathered.shape[1], panel.shape[1]
    stack = panel.reshape(2 * count_ev, NSPIN * count_ev)
    blocks = panel.reshape(2, count_ev, NSPIN, count_ev).transpose(0, 2, 1, 3).reshape(2, NSPIN * count_ev, count_ev)
    wide = jnp.concatenate(
        [
            jnp.concatenate([blocks[0], -blocks[1]], axis=1),
            jnp.concatenate([blocks[1], blocks[0]], axis=1),
        ],
        axis=0,
    )
    sums = pl.pallas_call(
        panel_kernel,
        grid=(count_ops,),
        in_specs=[
            pl.BlockSpec((1, 1, 2, count_ev, count_ev), lambda a: (0, a, 0, 0, 0)),
            pl.BlockSpec((1, 1, 2, count_ev, count_ev), lambda a: (1, a, 0, 0, 0)),
            pl.BlockSpec(stack.shape, lambda a: (0, 0)),
            pl.BlockSpec(wide.shape, lambda a: (0, 0)),
        ],
        out_specs=pl.BlockSpec((1, 2, count_ev), lambda a: (a, 0, 0)),
        out_shape=jax.ShapeDtypeStruct((count_ops, 2, count_ev), jnp.float32),
    )(gathered, gathered, stack, wide)
    return jnp.sum(sums, axis=-1) * (1.0 / (16.0 * count_ev))


def body(eigenvectors, gauge_links, perambulators, directions, momenta, pair_times):
    time_count = eigenvectors.shape[0]
    count_ev = eigenvectors.shape[3]
    local_sites = eigenvectors.shape[4]
    count_slabs = lax.axis_size("slab")
    nspace = NSPIN * count_slabs
    member = lax.axis_index("member")
    device = lax.axis_index("slab") * NSPIN + member
    half_rows = LY // 2
    extent_x = nspace // 2
    column = jnp.arange(local_sites, dtype=jnp.int32)
    coord_x = device // 2 + 0 * column
    coord_y = device % 2 * half_rows + column // LZ
    coord_z = column % LZ
    angle = phase_angles(momenta, (coord_x, coord_y, coord_z), (extent_x, LY, LZ))[0]
    halves = 2 if time_count % 2 == 0 else 1
    span = time_count // halves
    far_tile = [(h * span, shifted(eigenvectors[h * span : (h + 1) * span], SPACE, -2)) for h in range(halves)]
    row_in = swapped(eigenvectors[..., :LZ], SPACE, 0)
    scale = 1.0 / math.sqrt(3.0 * extent_x * LY * LZ)
    partial = local_sums(eigenvectors, gauge_links, far_tile, row_in, directions, angle, scale)
    own_rows = lax.psum_scatter(partial, SPACE, scatter_dimension=1, tiled=True)
    rows = own_rows.shape[1]
    slabs = jnp.arange(count_slabs, dtype=jnp.int32)
    wanted = jnp.stack([pair_times[slabs, 1], pair_times[slabs, 0]], 1)
    outgoing = jnp.take(own_rows, wanted.reshape(-1), axis=0).reshape(count_slabs, 2, rows, count_ev)
    across = lax.all_to_all(outgoing, "slab", 0, 0, tiled=True)
    spread = jnp.broadcast_to(across[None], (NSPIN,) + across.shape)
    within = lax.all_to_all(spread, "member", 0, 0, tiled=True)
    incoming = within.transpose(1, 0, 2, 3, 4).reshape(nspace, 2, rows, count_ev)
    count_ops = partial.shape[1] // (2 * count_ev)
    gathered = incoming.transpose(1, 0, 2, 3).reshape(2, count_ops, 2, count_ev, count_ev)
    correlators = contract_panel(gathered, perambulators[0])[None]
    return (own_rows, correlators)


def solution(mesh):
    count_cfg = mesh.shape["cfg"]
    count_slabs = mesh.shape["space"] // NSPIN
    split = Mesh(mesh.devices.reshape(count_cfg, count_slabs, NSPIN), ("cfg",) + SPACE)
    placed = (
        P("cfg", None, None, None, SPACE),
        P("cfg", None, None, None, None, SPACE),
        P(("cfg",) + SPACE, None, None, None),
        P(),
        P(),
        P(),
    )
    return jax.shard_map(
        body,
        mesh=split,
        in_specs=placed,
        out_specs=(P("cfg", SPACE, None), P(("cfg",) + SPACE, None, None)),
        check_vma=False,
    )
```

```python
import functools
import math

import jax
import jax.numpy as jnp
from jax import lax
from jax.experimental import pallas as pl
from jax.experimental.pallas import tpu as pltpu
from jax.sharding import Mesh, PartitionSpec as P

NSPIN = 4
LY = 32
LZ = 8
SPACE = ("slab", "member")


def shifted(block, axis, distance):
    devices = range(lax.axis_size(axis))
    route = [((i - distance) % len(devices), i) for i in devices]
    return lax.ppermute(block, axis, route)


def swapped(value, axis, bit):
    return lax.ppermute(value, axis, [(i, i ^ 1 << bit) for i in range(lax.axis_size(axis))])


def phase_angles(momenta, coords, extents):
    fraction = 0.0
    for course in range(3):
        turns = momenta[:, course : course + 1] * coords[course][None, :] % extents[course]
        fraction = fraction + turns.astype(jnp.float32) / extents[course]
    return 2.0 * math.pi * fraction


def sums_kernel(slot_ref, field_ref, near_ref, link_ref, trig_ref, *rest, scale, course_list):
    out_ref = rest[-1] if len(course_list) == 1 else rest[0]
    count_ev, sites = field_ref.shape[3], field_ref.shape[4]
    lane = lax.broadcasted_iota(jnp.int32, (count_ev, sites), 1)
    last_z = lane % LZ == LZ - 1
    last_row = lane >= sites - LZ
    if len(course_list) == 1:
        left = trig_ref[0]
    else:
        cosine = trig_ref[0:1, :]
        sine_part = trig_ref[1:2, :]
        here = [[field_ref[0, part, colour].astype(jnp.float32) for colour in range(3)] for part in range(2)]
        phased_real = [(cosine * here[0][c] - sine_part * here[1][c]).astype(jnp.bfloat16) for c in range(3)]
        phased_imag = [(sine_part * here[0][c] + cosine * here[1][c]).astype(jnp.bfloat16) for c in range(3)]
        real_rows = jnp.concatenate(phased_real + phased_imag, axis=1)
        imag_rows = jnp.concatenate([-v for v in phased_imag] + phased_real, axis=1)
        left = jnp.concatenate([real_rows, imag_rows], axis=0)
        rest[1][0] = left
    rows = 2 * count_ev
    for course in course_list:
        if course == 0:
            near = [[near_ref[0, part, colour].astype(jnp.float32) for colour in range(3)] for part in range(2)]
        elif course == 1:
            near = [
                [
                    jnp.where(last_row, near_ref[0, part, colour].astype(jnp.float32), pltpu.roll(here[part][colour], sites - LZ, 1))
                    for colour in range(3)
                ]
                for part in range(2)
            ]
        else:
            near = [
                [
                    jnp.where(last_z, pltpu.roll(here[part][colour], LZ - 1, 1), pltpu.roll(here[part][colour], sites - 1, 1))
                    for colour in range(3)
                ]
                for part in range(2)
            ]
        moved_real = []
        moved_imag = []
        for outer in range(3):
            real_part = 0.0
            imag_part = 0.0
            for inner in range(3):
                link_real = link_ref[0, course, 0, outer, inner : inner + 1, :]
                link_imag = link_ref[0, course, 1, outer, inner : inner + 1, :]
                real_part = real_part + link_real * near[0][inner] - link_imag * near[1][inner]
                imag_part = imag_part + link_real * near[1][inner] + link_imag * near[0][inner]
            moved_real.append(real_part.astype(jnp.bfloat16))
            moved_imag.append(imag_part.astype(jnp.bfloat16))
        right = jnp.concatenate(moved_real + moved_imag, axis=1)
        joined = lax.dot_general(left, right, (((1,), (1,)), ((), ())), preferred_element_type=jnp.float32)
        if len(course_list) == 1:
            out_ref[0] = (joined * scale).astype(out_ref.dtype)
        else:
            start = pl.multiple_of(slot_ref[course] * rows, rows)
            out_ref[0, pl.ds(start, rows), :] = (joined * scale).astype(out_ref.dtype)


def local_sums(eigenvectors, gauge_links, far_tile, row_in, directions, angle, scale):
    time_count, _, _, count_ev, sites = eigenvectors.shape
    count_ops = directions.shape[0]
    slot_of = jnp.sum(
        (directions[None, :] == jnp.arange(count_ops, dtype=jnp.int32)[:, None]) * jnp.arange(count_ops, dtype=jnp.int32)[None, :],
        axis=1,
    ).astype(jnp.int32)
    row_wide = jnp.pad(row_in, ((0, 0),) * 4 + ((sites - LZ, 0),))
    trig = jnp.stack([jnp.cos(angle), jnp.sin(angle)], 0)
    field_spec = pl.BlockSpec((1, 2, 3, count_ev, sites), lambda t, slot: (t, 0, 0, 0, 0))
    link_spec = pl.BlockSpec((1,) + gauge_links.shape[1:], lambda t, slot: (t, 0, 0, 0, 0, 0))
    trig_spec = pl.BlockSpec(trig.shape, lambda t, slot: (0, 0))
    rows = count_ops * 2 * count_ev
    near_courses = tuple(course for course in range(count_ops) if course != 0)
    left_rows = 2 * count_ev
    left_spec = pl.BlockSpec((1, left_rows, 6 * sites), lambda t, slot: (t, 0, 0))
    first_spec = pltpu.PrefetchScalarGridSpec(
        num_scalar_prefetch=1,
        grid=(time_count,),
        in_specs=[field_spec, field_spec, link_spec, trig_spec],
        out_specs=[pl.BlockSpec((1, rows, count_ev), lambda t, slot: (t, 0, 0)), left_spec],
    )
    partial, left = pl.pallas_call(
        functools.partial(sums_kernel, scale=scale, course_list=near_courses),
        grid_spec=first_spec,
        out_shape=(
            jax.ShapeDtypeStruct((time_count, rows, count_ev), jnp.bfloat16),
            jax.ShapeDtypeStruct((time_count, left_rows, 6 * sites), jnp.bfloat16),
        ),
    )(slot_of, eigenvectors, row_wide, gauge_links, trig)
    second_spec = pltpu.PrefetchScalarGridSpec(
        num_scalar_prefetch=1,
        grid=(time_count,),
        in_specs=[pl.BlockSpec(memory_space=pl.ANY), field_spec, link_spec, left_spec, pl.BlockSpec(memory_space=pl.ANY)],
        out_specs=pl.BlockSpec((1, 2 * count_ev, count_ev), lambda t, slot: (t, slot[0], 0)),
    )
    return pl.pallas_call(
        functools.partial(sums_kernel, scale=scale, course_list=(0,)),
        grid_spec=second_spec,
        out_shape=jax.ShapeDtypeStruct((time_count, rows, count_ev), jnp.bfloat16),
        input_output_aliases={5: 0},
    )(slot_of, eigenvectors, far_tile, gauge_links, left, partial)


def panel_kernel(sink_ref, source_ref, stack_ref, wide_ref, out_ref):
    count_ev = sink_ref.shape[3]
    sink_real = sink_ref[0, 0, 0]
    sink_imag = sink_ref[0, 0, 1]
    sink_wide = jnp.concatenate(
        [
            jnp.concatenate([sink_real, -sink_imag], axis=1),
            jnp.concatenate([sink_imag, sink_real], axis=1),
        ],
        axis=0,
    )
    left = jnp.dot(sink_wide, stack_ref[...], preferred_element_type=jnp.float32)
    source_stack = jnp.concatenate([source_ref[0, 0, 0], source_ref[0, 0, 1]], axis=0)
    right = jnp.dot(wide_ref[...], source_stack, preferred_element_type=jnp.float32)
    total_real = 0.0
    total_imag = 0.0
    half = NSPIN * count_ev
    for spin in range(NSPIN):
        left_real = left[:count_ev, spin * count_ev : (spin + 1) * count_ev]
        left_imag = left[count_ev:, spin * count_ev : (spin + 1) * count_ev]
        right_real = right[spin * count_ev : (spin + 1) * count_ev]
        right_imag = right[half + spin * count_ev : half + (spin + 1) * count_ev]
        total_real = total_real + left_real * right_real + left_imag * right_imag
        total_imag = total_imag + left_imag * right_real - left_real * right_imag
    out_ref[0, 0:1, :] = jnp.sum(total_real, axis=0, keepdims=True)
    out_ref[0, 1:2, :] = jnp.sum(total_imag, axis=0, keepdims=True)


def contract_panel(gathered, panel):
    count_ops, count_ev = gathered.shape[1], panel.shape[1]
    stack = panel.reshape(2 * count_ev, NSPIN * count_ev)
    blocks = panel.reshape(2, count_ev, NSPIN, count_ev).transpose(0, 2, 1, 3).reshape(2, NSPIN * count_ev, count_ev)
    wide = jnp.concatenate(
        [
            jnp.concatenate([blocks[0], -blocks[1]], axis=1),
            jnp.concatenate([blocks[1], blocks[0]], axis=1),
        ],
        axis=0,
    )
    sums = pl.pallas_call(
        panel_kernel,
        grid=(count_ops,),
        in_specs=[
            pl.BlockSpec((1, 1, 2, count_ev, count_ev), lambda a: (0, a, 0, 0, 0)),
            pl.BlockSpec((1, 1, 2, count_ev, count_ev), lambda a: (1, a, 0, 0, 0)),
            pl.BlockSpec(stack.shape, lambda a: (0, 0)),
            pl.BlockSpec(wide.shape, lambda a: (0, 0)),
        ],
        out_specs=pl.BlockSpec((1, 2, count_ev), lambda a: (a, 0, 0)),
        out_shape=jax.ShapeDtypeStruct((count_ops, 2, count_ev), jnp.float32),
    )(gathered, gathered, stack, wide)
    return jnp.sum(sums, axis=-1) * (1.0 / (16.0 * count_ev))


def body(eigenvectors, gauge_links, perambulators, directions, momenta, pair_times):
    time_count = eigenvectors.shape[0]
    count_ev = eigenvectors.shape[3]
    local_sites = eigenvectors.shape[4]
    count_slabs = lax.axis_size("slab")
    nspace = NSPIN * count_slabs
    member = lax.axis_index("member")
    device = lax.axis_index("slab") * NSPIN + member
    half_rows = LY // 2
    extent_x = nspace // 2
    column = jnp.arange(local_sites, dtype=jnp.int32)
    coord_x = device // 2 + 0 * column
    coord_y = device % 2 * half_rows + column // LZ
    coord_z = column % LZ
    angle = phase_angles(momenta, (coord_x, coord_y, coord_z), (extent_x, LY, LZ))[0]
    far_tile = shifted(eigenvectors, SPACE, -2)
    row_in = swapped(eigenvectors[..., :LZ], SPACE, 0)
    scale = 1.0 / math.sqrt(3.0 * extent_x * LY * LZ)
    partial = local_sums(eigenvectors, gauge_links, far_tile, row_in, directions, angle, scale)
    rows = partial.shape[1] // nspace
    blocks = partial.reshape(time_count, nspace, rows, count_ev).transpose(1, 0, 2, 3)
    own_rows = lax.psum_scatter(blocks, SPACE, scatter_dimension=0, tiled=True)[0]
    slabs = jnp.arange(count_slabs, dtype=jnp.int32)
    wanted = jnp.stack([pair_times[slabs, 1], pair_times[slabs, 0]], 1)
    outgoing = jnp.take(own_rows, wanted.reshape(-1), axis=0).reshape(count_slabs, 2, rows, count_ev)
    across = lax.all_to_all(outgoing, "slab", 0, 0, tiled=True)
    spread = jnp.broadcast_to(across[None], (NSPIN,) + across.shape)
    within = lax.all_to_all(spread, "member", 0, 0, tiled=True)
    incoming = within.transpose(1, 0, 2, 3, 4).reshape(nspace, 2, rows, count_ev)
    count_ops = partial.shape[1] // (2 * count_ev)
    gathered = incoming.transpose(1, 0, 2, 3).reshape(2, count_ops, 2, count_ev, count_ev)
    correlators = contract_panel(gathered, perambulators[0])[None]
    return (own_rows, correlators)


def solution(mesh):
    count_cfg = mesh.shape["cfg"]
    count_slabs = mesh.shape["space"] // NSPIN
    split = Mesh(mesh.devices.reshape(count_cfg, count_slabs, NSPIN), ("cfg",) + SPACE)
    placed = (
        P("cfg", None, None, None, SPACE),
        P("cfg", None, None, None, None, SPACE),
        P(("cfg",) + SPACE, None, None, None),
        P(),
        P(),
        P(),
    )
    return jax.shard_map(
        body,
        mesh=split,
        in_specs=placed,
        out_specs=(P("cfg", SPACE, None), P(("cfg",) + SPACE, None, None)),
        check_vma=False,
    )
```

```python
import functools
import math

import jax
import jax.numpy as jnp
from jax import lax
from jax.experimental import pallas as pl
from jax.experimental.pallas import tpu as pltpu
from jax.sharding import Mesh, PartitionSpec as P

NSPIN = 4
LY = 32
LZ = 8
SPACE = ("slab", "member")


def shifted(block, axis, distance):
    devices = range(lax.axis_size(axis))
    route = [((i - distance) % len(devices), i) for i in devices]
    return lax.ppermute(block, axis, route)


def swapped(value, axis, bit):
    return lax.ppermute(value, axis, [(i, i ^ 1 << bit) for i in range(lax.axis_size(axis))])


def phase_angles(momenta, coords, extents):
    fraction = 0.0
    for course in range(3):
        turns = momenta[:, course : course + 1] * coords[course][None, :] % extents[course]
        fraction = fraction + turns.astype(jnp.float32) / extents[course]
    return 2.0 * math.pi * fraction


def sums_kernel(slot_ref, field_ref, near_ref, link_ref, trig_ref, *rest, scale, course_list):
    out_ref = rest[-1] if len(course_list) == 1 else rest[0]
    count_ev, sites = field_ref.shape[3], field_ref.shape[4]
    lane = lax.broadcasted_iota(jnp.int32, (count_ev, sites), 1)
    last_z = lane % LZ == LZ - 1
    last_row = lane >= sites - LZ
    if len(course_list) == 1:
        left = trig_ref[0]
    else:
        cosine = trig_ref[0:1, :]
        sine_part = trig_ref[1:2, :]
        here = [[field_ref[0, part, colour].astype(jnp.float32) for colour in range(3)] for part in range(2)]
        phased_real = [(cosine * here[0][c] - sine_part * here[1][c]).astype(jnp.bfloat16) for c in range(3)]
        phased_imag = [(sine_part * here[0][c] + cosine * here[1][c]).astype(jnp.bfloat16) for c in range(3)]
        real_rows = jnp.concatenate(phased_real + phased_imag, axis=1)
        imag_rows = jnp.concatenate([-v for v in phased_imag] + phased_real, axis=1)
        left = jnp.concatenate([real_rows, imag_rows], axis=0)
        rest[1][0] = left
    rows = 2 * count_ev
    for course in course_list:
        if course == 0:
            near = [[near_ref[0, part, colour].astype(jnp.float32) for colour in range(3)] for part in range(2)]
        elif course == 1:
            near = [
                [
                    jnp.where(last_row, near_ref[0, part, colour].astype(jnp.float32), pltpu.roll(here[part][colour], sites - LZ, 1))
                    for colour in range(3)
                ]
                for part in range(2)
            ]
        else:
            near = [
                [
                    jnp.where(last_z, pltpu.roll(here[part][colour], LZ - 1, 1), pltpu.roll(here[part][colour], sites - 1, 1))
                    for colour in range(3)
                ]
                for part in range(2)
            ]
        moved_real = []
        moved_imag = []
        for outer in range(3):
            real_part = 0.0
            imag_part = 0.0
            for inner in range(3):
                link_real = link_ref[0, course, 0, outer, inner : inner + 1, :]
                link_imag = link_ref[0, course, 1, outer, inner : inner + 1, :]
                real_part = real_part + link_real * near[0][inner] - link_imag * near[1][inner]
                imag_part = imag_part + link_real * near[1][inner] + link_imag * near[0][inner]
            moved_real.append(real_part.astype(jnp.bfloat16))
            moved_imag.append(imag_part.astype(jnp.bfloat16))
        right = jnp.concatenate(moved_real + moved_imag, axis=1)
        joined = lax.dot_general(left, right, (((1,), (1,)), ((), ())), preferred_element_type=jnp.float32)
        if len(course_list) == 1:
            out_ref[0] = (joined * scale).astype(out_ref.dtype)
        else:
            start = pl.multiple_of(slot_ref[course] * rows, rows)
            out_ref[0, pl.ds(start, rows), :] = (joined * scale).astype(out_ref.dtype)


def local_sums(eigenvectors, gauge_links, far_tile, row_in, directions, angle, scale):
    time_count, _, _, count_ev, sites = eigenvectors.shape
    count_ops = directions.shape[0]
    slot_of = jnp.sum(
        (directions[None, :] == jnp.arange(count_ops, dtype=jnp.int32)[:, None]) * jnp.arange(count_ops, dtype=jnp.int32)[None, :],
        axis=1,
    ).astype(jnp.int32)
    row_wide = jnp.pad(row_in, ((0, 0),) * 4 + ((sites - LZ, 0),))
    trig = jnp.stack([jnp.cos(angle), jnp.sin(angle)], 0)
    field_spec = pl.BlockSpec((1, 2, 3, count_ev, sites), lambda t, slot: (t, 0, 0, 0, 0))
    link_spec = pl.BlockSpec((1,) + gauge_links.shape[1:], lambda t, slot: (t, 0, 0, 0, 0, 0))
    trig_spec = pl.BlockSpec(trig.shape, lambda t, slot: (0, 0))
    rows = count_ops * 2 * count_ev
    near_courses = tuple(course for course in range(count_ops) if course != 0)
    left_rows = 2 * count_ev
    left_spec = pl.BlockSpec((1, left_rows, 6 * sites), lambda t, slot: (t, 0, 0))
    first_spec = pltpu.PrefetchScalarGridSpec(
        num_scalar_prefetch=1,
        grid=(time_count,),
        in_specs=[field_spec, field_spec, link_spec, trig_spec],
        out_specs=[pl.BlockSpec((1, rows, count_ev), lambda t, slot: (t, 0, 0)), left_spec],
    )
    partial, left = pl.pallas_call(
        functools.partial(sums_kernel, scale=scale, course_list=near_courses),
        grid_spec=first_spec,
        out_shape=(
            jax.ShapeDtypeStruct((time_count, rows, count_ev), jnp.bfloat16),
            jax.ShapeDtypeStruct((time_count, left_rows, 6 * sites), jnp.bfloat16),
        ),
    )(slot_of, eigenvectors, row_wide, gauge_links, trig)
    second_spec = pltpu.PrefetchScalarGridSpec(
        num_scalar_prefetch=1,
        grid=(time_count,),
        in_specs=[pl.BlockSpec(memory_space=pl.ANY), field_spec, link_spec, left_spec, pl.BlockSpec(memory_space=pl.ANY)],
        out_specs=pl.BlockSpec((1, 2 * count_ev, count_ev), lambda t, slot: (t, slot[0], 0)),
    )
    return pl.pallas_call(
        functools.partial(sums_kernel, scale=scale, course_list=(0,)),
        grid_spec=second_spec,
        out_shape=jax.ShapeDtypeStruct((time_count, rows, count_ev), jnp.bfloat16),
        input_output_aliases={5: 0},
    )(slot_of, eigenvectors, far_tile, gauge_links, left, partial)


def panel_kernel(sink_ref, source_ref, stack_ref, wide_ref, out_ref):
    count_ev = sink_ref.shape[3]
    sink_real = sink_ref[0, 0, 0]
    sink_imag = sink_ref[0, 0, 1]
    sink_wide = jnp.concatenate(
        [
            jnp.concatenate([sink_real, -sink_imag], axis=1),
            jnp.concatenate([sink_imag, sink_real], axis=1),
        ],
        axis=0,
    )
    left = jnp.dot(sink_wide, stack_ref[...], preferred_element_type=jnp.float32)
    source_stack = jnp.concatenate([source_ref[0, 0, 0], source_ref[0, 0, 1]], axis=0)
    right = jnp.dot(wide_ref[...], source_stack, preferred_element_type=jnp.float32)
    total_real = 0.0
    total_imag = 0.0
    half = NSPIN * count_ev
    for spin in range(NSPIN):
        left_real = left[:count_ev, spin * count_ev : (spin + 1) * count_ev]
        left_imag = left[count_ev:, spin * count_ev : (spin + 1) * count_ev]
        right_real = right[spin * count_ev : (spin + 1) * count_ev]
        right_imag = right[half + spin * count_ev : half + (spin + 1) * count_ev]
        total_real = total_real + left_real * right_real + left_imag * right_imag
        total_imag = total_imag + left_imag * right_real - left_real * right_imag
    out_ref[0, 0:1, :] = jnp.sum(total_real, axis=0, keepdims=True)
    out_ref[0, 1:2, :] = jnp.sum(total_imag, axis=0, keepdims=True)


def contract_panel(gathered, panel):
    count_ops, count_ev = gathered.shape[1], panel.shape[1]
    stack = panel.reshape(2 * count_ev, NSPIN * count_ev)
    blocks = panel.reshape(2, count_ev, NSPIN, count_ev).transpose(0, 2, 1, 3).reshape(2, NSPIN * count_ev, count_ev)
    wide = jnp.concatenate(
        [
            jnp.concatenate([blocks[0], -blocks[1]], axis=1),
            jnp.concatenate([blocks[1], blocks[0]], axis=1),
        ],
        axis=0,
    )
    sums = pl.pallas_call(
        panel_kernel,
        grid=(count_ops,),
        in_specs=[
            pl.BlockSpec((1, 1, 2, count_ev, count_ev), lambda a: (0, a, 0, 0, 0)),
            pl.BlockSpec((1, 1, 2, count_ev, count_ev), lambda a: (1, a, 0, 0, 0)),
            pl.BlockSpec(stack.shape, lambda a: (0, 0)),
            pl.BlockSpec(wide.shape, lambda a: (0, 0)),
        ],
        out_specs=pl.BlockSpec((1, 2, count_ev), lambda a: (a, 0, 0)),
        out_shape=jax.ShapeDtypeStruct((count_ops, 2, count_ev), jnp.float32),
    )(gathered, gathered, stack, wide)
    return jnp.sum(sums, axis=-1) * (1.0 / (16.0 * count_ev))


def body(eigenvectors, gauge_links, perambulators, directions, momenta, pair_times):
    time_count = eigenvectors.shape[0]
    count_ev = eigenvectors.shape[3]
    local_sites = eigenvectors.shape[4]
    count_slabs = lax.axis_size("slab")
    nspace = NSPIN * count_slabs
    member = lax.axis_index("member")
    device = lax.axis_index("slab") * NSPIN + member
    half_rows = LY // 2
    extent_x = nspace // 2
    column = jnp.arange(local_sites, dtype=jnp.int32)
    coord_x = device // 2 + 0 * column
    coord_y = device % 2 * half_rows + column // LZ
    coord_z = column % LZ
    angle = phase_angles(momenta, (coord_x, coord_y, coord_z), (extent_x, LY, LZ))[0]
    far_tile = shifted(eigenvectors, SPACE, -2)
    row_in = swapped(eigenvectors[..., :LZ], SPACE, 0)
    scale = 1.0 / math.sqrt(3.0 * extent_x * LY * LZ)
    partial = local_sums(eigenvectors, gauge_links, far_tile, row_in, directions, angle, scale)
    own_rows = lax.psum_scatter(partial, SPACE, scatter_dimension=1, tiled=True)
    rows = own_rows.shape[1]
    slabs = jnp.arange(count_slabs, dtype=jnp.int32)
    wanted = jnp.stack([pair_times[slabs, 1], pair_times[slabs, 0]], 1)
    outgoing = jnp.take(own_rows, wanted.reshape(-1), axis=0).reshape(count_slabs, 2, rows, count_ev)
    if count_slabs <= 8:
        slab = lax.axis_index("slab")
        pieces = [jnp.take(outgoing, (slab + shift) % count_slabs, axis=0) for shift in range(count_slabs)]
        arrived = [pieces[0]] + [shifted(pieces[shift], "slab", shift) for shift in range(1, count_slabs)]
        arrived = jnp.stack(arrived, 0)
        across = jnp.take(arrived, (slab - jnp.arange(count_slabs, dtype=jnp.int32)) % count_slabs, axis=0)
    else:
        across = lax.all_to_all(outgoing, "slab", 0, 0, tiled=True)
    spread = jnp.broadcast_to(across[None], (NSPIN,) + across.shape)
    within = lax.all_to_all(spread, "member", 0, 0, tiled=True)
    incoming = within.transpose(1, 0, 2, 3, 4).reshape(nspace, 2, rows, count_ev)
    count_ops = partial.shape[1] // (2 * count_ev)
    gathered = incoming.transpose(1, 0, 2, 3).reshape(2, count_ops, 2, count_ev, count_ev)
    correlators = contract_panel(gathered, perambulators[0])[None]
    return (own_rows, correlators)


def solution(mesh):
    count_cfg = mesh.shape["cfg"]
    count_slabs = mesh.shape["space"] // NSPIN
    split = Mesh(mesh.devices.reshape(count_cfg, count_slabs, NSPIN), ("cfg",) + SPACE)
    placed = (
        P("cfg", None, None, None, SPACE),
        P("cfg", None, None, None, None, SPACE),
        P(("cfg",) + SPACE, None, None, None),
        P(),
        P(),
        P(),
    )
    return jax.shard_map(
        body,
        mesh=split,
        in_specs=placed,
        out_specs=(P("cfg", SPACE, None), P(("cfg",) + SPACE, None, None)),
        check_vma=False,
    )
```

```python
import functools
import math

import jax
import jax.numpy as jnp
from jax import lax
from jax.experimental import pallas as pl
from jax.experimental.pallas import tpu as pltpu
from jax.sharding import Mesh, PartitionSpec as P

NSPIN = 4
LY = 32
LZ = 8
SPACE = ("slab", "member")


def shifted(block, axis, distance):
    devices = range(lax.axis_size(axis))
    route = [((i - distance) % len(devices), i) for i in devices]
    return lax.ppermute(block, axis, route)


def swapped(value, axis, bit):
    return lax.ppermute(value, axis, [(i, i ^ 1 << bit) for i in range(lax.axis_size(axis))])


def phase_angles(momenta, coords, extents):
    fraction = 0.0
    for course in range(3):
        turns = momenta[:, course : course + 1] * coords[course][None, :] % extents[course]
        fraction = fraction + turns.astype(jnp.float32) / extents[course]
    return 2.0 * math.pi * fraction


def sums_kernel(slot_ref, field_ref, near_ref, link_ref, trig_ref, *rest, scale, course_list):
    out_ref = rest[-1] if len(course_list) == 1 else rest[0]
    count_ev, sites = field_ref.shape[3], field_ref.shape[4]
    lane = lax.broadcasted_iota(jnp.int32, (count_ev, sites), 1)
    last_z = lane % LZ == LZ - 1
    last_row = lane >= sites - LZ
    if len(course_list) == 1:
        left = trig_ref[0]
    else:
        cosine = trig_ref[0:1, :]
        sine_part = trig_ref[1:2, :]
        here = [[field_ref[0, part, colour].astype(jnp.float32) for colour in range(3)] for part in range(2)]
        phased_real = [(cosine * here[0][c] - sine_part * here[1][c]).astype(jnp.bfloat16) for c in range(3)]
        phased_imag = [(sine_part * here[0][c] + cosine * here[1][c]).astype(jnp.bfloat16) for c in range(3)]
        real_rows = jnp.concatenate(phased_real + phased_imag, axis=1)
        imag_rows = jnp.concatenate([-v for v in phased_imag] + phased_real, axis=1)
        left = jnp.concatenate([real_rows, imag_rows], axis=0)
        rest[1][0] = left
    rows = 2 * count_ev
    for course in course_list:
        if course == 0:
            near = [[near_ref[0, part, colour].astype(jnp.float32) for colour in range(3)] for part in range(2)]
        elif course == 1:
            near = [
                [
                    jnp.where(last_row, near_ref[0, part, colour].astype(jnp.float32), pltpu.roll(here[part][colour], sites - LZ, 1))
                    for colour in range(3)
                ]
                for part in range(2)
            ]
        else:
            near = [
                [
                    jnp.where(last_z, pltpu.roll(here[part][colour], LZ - 1, 1), pltpu.roll(here[part][colour], sites - 1, 1))
                    for colour in range(3)
                ]
                for part in range(2)
            ]
        moved_real = []
        moved_imag = []
        for outer in range(3):
            real_part = 0.0
            imag_part = 0.0
            for inner in range(3):
                link_real = link_ref[0, course, 0, outer, inner : inner + 1, :]
                link_imag = link_ref[0, course, 1, outer, inner : inner + 1, :]
                real_part = real_part + link_real * near[0][inner] - link_imag * near[1][inner]
                imag_part = imag_part + link_real * near[1][inner] + link_imag * near[0][inner]
            moved_real.append(real_part.astype(jnp.bfloat16))
            moved_imag.append(imag_part.astype(jnp.bfloat16))
        right = jnp.concatenate(moved_real + moved_imag, axis=1)
        joined = lax.dot_general(left, right, (((1,), (1,)), ((), ())), preferred_element_type=jnp.float32)
        if len(course_list) == 1:
            out_ref[0] = (joined * scale).astype(out_ref.dtype)
        else:
            start = pl.multiple_of(slot_ref[course] * rows, rows)
            out_ref[0, pl.ds(start, rows), :] = (joined * scale).astype(out_ref.dtype)


def local_sums(eigenvectors, gauge_links, far_tile, row_in, directions, angle, scale):
    time_count, _, _, count_ev, sites = eigenvectors.shape
    count_ops = directions.shape[0]
    slot_of = jnp.sum(
        (directions[None, :] == jnp.arange(count_ops, dtype=jnp.int32)[:, None]) * jnp.arange(count_ops, dtype=jnp.int32)[None, :],
        axis=1,
    ).astype(jnp.int32)
    row_wide = jnp.pad(row_in, ((0, 0),) * 4 + ((sites - LZ, 0),))
    trig = jnp.stack([jnp.cos(angle), jnp.sin(angle)], 0)
    field_spec = pl.BlockSpec((1, 2, 3, count_ev, sites), lambda t, slot: (t, 0, 0, 0, 0))
    link_spec = pl.BlockSpec((1,) + gauge_links.shape[1:], lambda t, slot: (t, 0, 0, 0, 0, 0))
    trig_spec = pl.BlockSpec(trig.shape, lambda t, slot: (0, 0))
    rows = count_ops * 2 * count_ev
    near_courses = tuple(course for course in range(count_ops) if course != 0)
    left_rows = 2 * count_ev
    left_spec = pl.BlockSpec((1, left_rows, 6 * sites), lambda t, slot: (t, 0, 0))
    first_spec = pltpu.PrefetchScalarGridSpec(
        num_scalar_prefetch=1,
        grid=(time_count,),
        in_specs=[field_spec, field_spec, link_spec, trig_spec],
        out_specs=[pl.BlockSpec((1, rows, count_ev), lambda t, slot: (t, 0, 0)), left_spec],
    )
    partial, left = pl.pallas_call(
        functools.partial(sums_kernel, scale=scale, course_list=near_courses),
        grid_spec=first_spec,
        out_shape=(
            jax.ShapeDtypeStruct((time_count, rows, count_ev), jnp.bfloat16),
            jax.ShapeDtypeStruct((time_count, left_rows, 6 * sites), jnp.bfloat16),
        ),
    )(slot_of, eigenvectors, row_wide, gauge_links, trig)
    second_spec = pltpu.PrefetchScalarGridSpec(
        num_scalar_prefetch=1,
        grid=(time_count,),
        in_specs=[pl.BlockSpec(memory_space=pl.ANY), field_spec, link_spec, left_spec, pl.BlockSpec(memory_space=pl.ANY)],
        out_specs=pl.BlockSpec((1, 2 * count_ev, count_ev), lambda t, slot: (t, slot[0], 0)),
    )
    return pl.pallas_call(
        functools.partial(sums_kernel, scale=scale, course_list=(0,)),
        grid_spec=second_spec,
        out_shape=jax.ShapeDtypeStruct((time_count, rows, count_ev), jnp.bfloat16),
        input_output_aliases={5: 0},
    )(slot_of, eigenvectors, far_tile, gauge_links, left, partial)


def panel_kernel(sink_ref, source_ref, stack_ref, wide_ref, out_ref):
    count_ev = sink_ref.shape[3]
    sink_real = sink_ref[0, 0, 0]
    sink_imag = sink_ref[0, 0, 1]
    sink_wide = jnp.concatenate(
        [
            jnp.concatenate([sink_real, -sink_imag], axis=1),
            jnp.concatenate([sink_imag, sink_real], axis=1),
        ],
        axis=0,
    )
    left = jnp.dot(sink_wide, stack_ref[...], preferred_element_type=jnp.float32)
    source_stack = jnp.concatenate([source_ref[0, 0, 0], source_ref[0, 0, 1]], axis=0)
    right = jnp.dot(wide_ref[...], source_stack, preferred_element_type=jnp.float32)
    total_real = 0.0
    total_imag = 0.0
    half = NSPIN * count_ev
    for spin in range(NSPIN):
        left_real = left[:count_ev, spin * count_ev : (spin + 1) * count_ev]
        left_imag = left[count_ev:, spin * count_ev : (spin + 1) * count_ev]
        right_real = right[spin * count_ev : (spin + 1) * count_ev]
        right_imag = right[half + spin * count_ev : half + (spin + 1) * count_ev]
        total_real = total_real + left_real * right_real + left_imag * right_imag
        total_imag = total_imag + left_imag * right_real - left_real * right_imag
    out_ref[0, 0:1, :] = jnp.sum(total_real, axis=0, keepdims=True)
    out_ref[0, 1:2, :] = jnp.sum(total_imag, axis=0, keepdims=True)


def contract_panel(gathered, panel):
    count_ops, count_ev = gathered.shape[1], panel.shape[1]
    stack = panel.reshape(2 * count_ev, NSPIN * count_ev)
    blocks = panel.reshape(2, count_ev, NSPIN, count_ev).transpose(0, 2, 1, 3).reshape(2, NSPIN * count_ev, count_ev)
    wide = jnp.concatenate(
        [
            jnp.concatenate([blocks[0], -blocks[1]], axis=1),
            jnp.concatenate([blocks[1], blocks[0]], axis=1),
        ],
        axis=0,
    )
    sums = pl.pallas_call(
        panel_kernel,
        grid=(count_ops,),
        in_specs=[
            pl.BlockSpec((1, 1, 2, count_ev, count_ev), lambda a: (0, a, 0, 0, 0)),
            pl.BlockSpec((1, 1, 2, count_ev, count_ev), lambda a: (1, a, 0, 0, 0)),
            pl.BlockSpec(stack.shape, lambda a: (0, 0)),
            pl.BlockSpec(wide.shape, lambda a: (0, 0)),
        ],
        out_specs=pl.BlockSpec((1, 2, count_ev), lambda a: (a, 0, 0)),
        out_shape=jax.ShapeDtypeStruct((count_ops, 2, count_ev), jnp.float32),
    )(gathered, gathered, stack, wide)
    return jnp.sum(sums, axis=-1) * (1.0 / (16.0 * count_ev))


def body(eigenvectors, gauge_links, perambulators, directions, momenta, pair_times):
    time_count = eigenvectors.shape[0]
    count_ev = eigenvectors.shape[3]
    local_sites = eigenvectors.shape[4]
    count_slabs = lax.axis_size("slab")
    nspace = NSPIN * count_slabs
    member = lax.axis_index("member")
    device = lax.axis_index("slab") * NSPIN + member
    half_rows = LY // 2
    extent_x = nspace // 2
    column = jnp.arange(local_sites, dtype=jnp.int32)
    coord_x = device // 2 + 0 * column
    coord_y = device % 2 * half_rows + column // LZ
    coord_z = column % LZ
    angle = phase_angles(momenta, (coord_x, coord_y, coord_z), (extent_x, LY, LZ))[0]
    far_tile = shifted(eigenvectors, SPACE, -2)
    row_in = swapped(eigenvectors[..., :LZ], SPACE, 0)
    scale = 1.0 / math.sqrt(3.0 * extent_x * LY * LZ)
    partial = local_sums(eigenvectors, gauge_links, far_tile, row_in, directions, angle, scale)
    own_rows = lax.psum_scatter(partial, SPACE, scatter_dimension=1, tiled=True)
    rows = own_rows.shape[1]
    slabs = jnp.arange(count_slabs, dtype=jnp.int32)
    wanted = jnp.stack([pair_times[slabs, 1], pair_times[slabs, 0]], 1)
    outgoing = jnp.take(own_rows, wanted.reshape(-1), axis=0).reshape(count_slabs, 2, rows, count_ev)
    if count_slabs <= 8:
        slab = lax.axis_index("slab")
        pieces = [jnp.take(outgoing, (slab + shift) % count_slabs, axis=0) for shift in range(count_slabs)]
        arrived = [pieces[0]] + [shifted(pieces[shift], "slab", shift) for shift in range(1, count_slabs)]
        arrived = jnp.stack(arrived, 0)
        across = jnp.take(arrived, (slab - jnp.arange(count_slabs, dtype=jnp.int32)) % count_slabs, axis=0)
    else:
        across = lax.all_to_all(outgoing, "slab", 0, 0, tiled=True)
    shared = [across] + [shifted(across, "member", shift) for shift in range(1, NSPIN)]
    shared = jnp.stack(shared, 0)
    within = jnp.take(shared, (member - jnp.arange(NSPIN, dtype=jnp.int32)) % NSPIN, axis=0)
    incoming = within.transpose(1, 0, 2, 3, 4).reshape(nspace, 2, rows, count_ev)
    count_ops = partial.shape[1] // (2 * count_ev)
    gathered = incoming.transpose(1, 0, 2, 3).reshape(2, count_ops, 2, count_ev, count_ev)
    correlators = contract_panel(gathered, perambulators[0])[None]
    return (own_rows, correlators)


def solution(mesh):
    count_cfg = mesh.shape["cfg"]
    count_slabs = mesh.shape["space"] // NSPIN
    split = Mesh(mesh.devices.reshape(count_cfg, count_slabs, NSPIN), ("cfg",) + SPACE)
    placed = (
        P("cfg", None, None, None, SPACE),
        P("cfg", None, None, None, None, SPACE),
        P(("cfg",) + SPACE, None, None, None),
        P(),
        P(),
        P(),
    )
    return jax.shard_map(
        body,
        mesh=split,
        in_specs=placed,
        out_specs=(P("cfg", SPACE, None), P(("cfg",) + SPACE, None, None)),
        check_vma=False,
    )
```

```python
import functools
import math

import jax
import jax.numpy as jnp
from jax import lax
from jax.experimental import pallas as pl
from jax.experimental.pallas import tpu as pltpu
from jax.sharding import Mesh, PartitionSpec as P

NSPIN = 4
LY = 32
LZ = 8
SPACE = ("slab", "member")


def shifted(block, axis, distance):
    devices = range(lax.axis_size(axis))
    route = [((i - distance) % len(devices), i) for i in devices]
    return lax.ppermute(block, axis, route)


def swapped(value, axis, bit):
    return lax.ppermute(value, axis, [(i, i ^ 1 << bit) for i in range(lax.axis_size(axis))])


def phase_angles(momenta, coords, extents):
    fraction = 0.0
    for course in range(3):
        turns = momenta[:, course : course + 1] * coords[course][None, :] % extents[course]
        fraction = fraction + turns.astype(jnp.float32) / extents[course]
    return 2.0 * math.pi * fraction


def sums_kernel(slot_ref, field_ref, near_ref, link_ref, trig_ref, *rest, scale, course_list):
    out_ref = rest[-1] if len(course_list) == 1 else rest[0]
    count_ev, sites = field_ref.shape[3], field_ref.shape[4]
    lane = lax.broadcasted_iota(jnp.int32, (count_ev, sites), 1)
    last_z = lane % LZ == LZ - 1
    last_row = lane >= sites - LZ
    if len(course_list) == 1:
        left = trig_ref[0]
    else:
        cosine = trig_ref[0:1, :]
        sine_part = trig_ref[1:2, :]
        here = [[field_ref[0, part, colour].astype(jnp.float32) for colour in range(3)] for part in range(2)]
        phased_real = [(cosine * here[0][c] - sine_part * here[1][c]).astype(jnp.bfloat16) for c in range(3)]
        phased_imag = [(sine_part * here[0][c] + cosine * here[1][c]).astype(jnp.bfloat16) for c in range(3)]
        real_rows = jnp.concatenate(phased_real + phased_imag, axis=1)
        imag_rows = jnp.concatenate([-v for v in phased_imag] + phased_real, axis=1)
        left = jnp.concatenate([real_rows, imag_rows], axis=0)
        rest[1][0] = left
    rows = 2 * count_ev
    for course in course_list:
        if course == 0:
            near = [[near_ref[0, part, colour].astype(jnp.float32) for colour in range(3)] for part in range(2)]
        elif course == 1:
            near = [
                [
                    jnp.where(last_row, near_ref[0, part, colour].astype(jnp.float32), pltpu.roll(here[part][colour], sites - LZ, 1))
                    for colour in range(3)
                ]
                for part in range(2)
            ]
        else:
            near = [
                [
                    jnp.where(last_z, pltpu.roll(here[part][colour], LZ - 1, 1), pltpu.roll(here[part][colour], sites - 1, 1))
                    for colour in range(3)
                ]
                for part in range(2)
            ]
        moved_real = []
        moved_imag = []
        for outer in range(3):
            real_part = 0.0
            imag_part = 0.0
            for inner in range(3):
                link_real = link_ref[0, course, 0, outer, inner : inner + 1, :]
                link_imag = link_ref[0, course, 1, outer, inner : inner + 1, :]
                real_part = real_part + link_real * near[0][inner] - link_imag * near[1][inner]
                imag_part = imag_part + link_real * near[1][inner] + link_imag * near[0][inner]
            moved_real.append(real_part.astype(jnp.bfloat16))
            moved_imag.append(imag_part.astype(jnp.bfloat16))
        right = jnp.concatenate(moved_real + moved_imag, axis=1)
        joined = lax.dot_general(left, right, (((1,), (1,)), ((), ())), preferred_element_type=jnp.float32)
        if len(course_list) == 1:
            out_ref[0] = (joined * scale).astype(out_ref.dtype)
        else:
            start = pl.multiple_of(slot_ref[course] * rows, rows)
            out_ref[0, pl.ds(start, rows), :] = (joined * scale).astype(out_ref.dtype)


def local_sums(eigenvectors, gauge_links, far_tile, row_in, directions, angle, scale):
    time_count, _, _, count_ev, sites = eigenvectors.shape
    count_ops = directions.shape[0]
    slot_of = jnp.sum(
        (directions[None, :] == jnp.arange(count_ops, dtype=jnp.int32)[:, None]) * jnp.arange(count_ops, dtype=jnp.int32)[None, :],
        axis=1,
    ).astype(jnp.int32)
    row_wide = jnp.pad(row_in, ((0, 0),) * 4 + ((sites - LZ, 0),))
    trig = jnp.stack([jnp.cos(angle), jnp.sin(angle)], 0)
    field_spec = pl.BlockSpec((1, 2, 3, count_ev, sites), lambda t, slot: (t, 0, 0, 0, 0))
    link_spec = pl.BlockSpec((1,) + gauge_links.shape[1:], lambda t, slot: (t, 0, 0, 0, 0, 0))
    trig_spec = pl.BlockSpec(trig.shape, lambda t, slot: (0, 0))
    rows = count_ops * 2 * count_ev
    near_courses = tuple(course for course in range(count_ops) if course != 0)
    left_rows = 2 * count_ev
    left_spec = pl.BlockSpec((1, left_rows, 6 * sites), lambda t, slot: (t, 0, 0))
    first_spec = pltpu.PrefetchScalarGridSpec(
        num_scalar_prefetch=1,
        grid=(time_count,),
        in_specs=[field_spec, field_spec, link_spec, trig_spec],
        out_specs=[pl.BlockSpec((1, rows, count_ev), lambda t, slot: (t, 0, 0)), left_spec],
    )
    partial, left = pl.pallas_call(
        functools.partial(sums_kernel, scale=scale, course_list=near_courses),
        grid_spec=first_spec,
        out_shape=(
            jax.ShapeDtypeStruct((time_count, rows, count_ev), jnp.bfloat16),
            jax.ShapeDtypeStruct((time_count, left_rows, 6 * sites), jnp.bfloat16),
        ),
    )(slot_of, eigenvectors, row_wide, gauge_links, trig)
    second_spec = pltpu.PrefetchScalarGridSpec(
        num_scalar_prefetch=1,
        grid=(time_count,),
        in_specs=[pl.BlockSpec(memory_space=pl.ANY), field_spec, link_spec, left_spec, pl.BlockSpec(memory_space=pl.ANY)],
        out_specs=pl.BlockSpec((1, 2 * count_ev, count_ev), lambda t, slot: (t, slot[0], 0)),
    )
    return pl.pallas_call(
        functools.partial(sums_kernel, scale=scale, course_list=(0,)),
        grid_spec=second_spec,
        out_shape=jax.ShapeDtypeStruct((time_count, rows, count_ev), jnp.bfloat16),
        input_output_aliases={5: 0},
    )(slot_of, eigenvectors, far_tile, gauge_links, left, partial)


def panel_kernel(sink_ref, source_ref, stack_ref, wide_ref, out_ref):
    count_ev = sink_ref.shape[3]
    sink_real = sink_ref[0, 0, 0]
    sink_imag = sink_ref[0, 0, 1]
    sink_wide = jnp.concatenate(
        [
            jnp.concatenate([sink_real, -sink_imag], axis=1),
            jnp.concatenate([sink_imag, sink_real], axis=1),
        ],
        axis=0,
    )
    left = jnp.dot(sink_wide, stack_ref[...], preferred_element_type=jnp.float32)
    source_stack = jnp.concatenate([source_ref[0, 0, 0], source_ref[0, 0, 1]], axis=0)
    right = jnp.dot(wide_ref[...], source_stack, preferred_element_type=jnp.float32)
    total_real = 0.0
    total_imag = 0.0
    half = NSPIN * count_ev
    for spin in range(NSPIN):
        left_real = left[:count_ev, spin * count_ev : (spin + 1) * count_ev]
        left_imag = left[count_ev:, spin * count_ev : (spin + 1) * count_ev]
        right_real = right[spin * count_ev : (spin + 1) * count_ev]
        right_imag = right[half + spin * count_ev : half + (spin + 1) * count_ev]
        total_real = total_real + left_real * right_real + left_imag * right_imag
        total_imag = total_imag + left_imag * right_real - left_real * right_imag
    out_ref[0, 0:1, :] = jnp.sum(total_real, axis=0, keepdims=True)
    out_ref[0, 1:2, :] = jnp.sum(total_imag, axis=0, keepdims=True)


def contract_panel(gathered, panel):
    count_ops, count_ev = gathered.shape[1], panel.shape[1]
    stack = panel.reshape(2 * count_ev, NSPIN * count_ev)
    blocks = panel.reshape(2, count_ev, NSPIN, count_ev).transpose(0, 2, 1, 3).reshape(2, NSPIN * count_ev, count_ev)
    wide = jnp.concatenate(
        [
            jnp.concatenate([blocks[0], -blocks[1]], axis=1),
            jnp.concatenate([blocks[1], blocks[0]], axis=1),
        ],
        axis=0,
    )
    sums = pl.pallas_call(
        panel_kernel,
        grid=(count_ops,),
        in_specs=[
            pl.BlockSpec((1, 1, 2, count_ev, count_ev), lambda a: (0, a, 0, 0, 0)),
            pl.BlockSpec((1, 1, 2, count_ev, count_ev), lambda a: (1, a, 0, 0, 0)),
            pl.BlockSpec(stack.shape, lambda a: (0, 0)),
            pl.BlockSpec(wide.shape, lambda a: (0, 0)),
        ],
        out_specs=pl.BlockSpec((1, 2, count_ev), lambda a: (a, 0, 0)),
        out_shape=jax.ShapeDtypeStruct((count_ops, 2, count_ev), jnp.float32),
    )(gathered, gathered, stack, wide)
    return jnp.sum(sums, axis=-1) * (1.0 / (16.0 * count_ev))


def body(eigenvectors, gauge_links, perambulators, directions, momenta, pair_times):
    time_count = eigenvectors.shape[0]
    count_ev = eigenvectors.shape[3]
    local_sites = eigenvectors.shape[4]
    count_slabs = lax.axis_size("slab")
    nspace = NSPIN * count_slabs
    member = lax.axis_index("member")
    device = lax.axis_index("slab") * NSPIN + member
    half_rows = LY // 2
    extent_x = nspace // 2
    column = jnp.arange(local_sites, dtype=jnp.int32)
    coord_x = device // 2 + 0 * column
    coord_y = device % 2 * half_rows + column // LZ
    coord_z = column % LZ
    angle = phase_angles(momenta, (coord_x, coord_y, coord_z), (extent_x, LY, LZ))[0]
    far_tile = shifted(eigenvectors, SPACE, -2)
    row_in = swapped(eigenvectors[..., :LZ], SPACE, 0)
    scale = 1.0 / math.sqrt(3.0 * extent_x * LY * LZ)
    partial = local_sums(eigenvectors, gauge_links, far_tile, row_in, directions, angle, scale)
    rows = partial.shape[1] // nspace
    if count_slabs <= 8:
        slab = lax.axis_index("slab")
        blocks = partial.reshape(time_count, count_slabs, NSPIN, rows, count_ev)
        slab_sum = lax.dynamic_index_in_dim(blocks, member, 2, keepdims=False).astype(jnp.float32)
        for shift in range(1, NSPIN):
            piece = lax.dynamic_index_in_dim(blocks, (member + shift) % NSPIN, 2, keepdims=False)
            slab_sum = slab_sum + shifted(piece, "member", shift).astype(jnp.float32)
        slab_part = slab_sum.astype(jnp.bfloat16)
        total = lax.dynamic_index_in_dim(slab_sum, slab, 1, keepdims=False)
        for shift in range(1, count_slabs):
            piece = lax.dynamic_index_in_dim(slab_part, (slab + shift) % count_slabs, 1, keepdims=False)
            total = total + shifted(piece, "slab", shift).astype(jnp.float32)
        own_rows = total.astype(jnp.bfloat16)
    else:
        own_rows = lax.psum_scatter(partial, SPACE, scatter_dimension=1, tiled=True)
    slabs = jnp.arange(count_slabs, dtype=jnp.int32)
    wanted = jnp.stack([pair_times[slabs, 1], pair_times[slabs, 0]], 1)
    outgoing = jnp.take(own_rows, wanted.reshape(-1), axis=0).reshape(count_slabs, 2, rows, count_ev)
    if count_slabs <= 8:
        pieces = [jnp.take(outgoing, (slab + shift) % count_slabs, axis=0) for shift in range(count_slabs)]
        arrived = [pieces[0]] + [shifted(pieces[shift], "slab", shift) for shift in range(1, count_slabs)]
        arrived = jnp.stack(arrived, 0)
        across = jnp.take(arrived, (slab - jnp.arange(count_slabs, dtype=jnp.int32)) % count_slabs, axis=0)
    else:
        across = lax.all_to_all(outgoing, "slab", 0, 0, tiled=True)
    shared = [across] + [shifted(across, "member", shift) for shift in range(1, NSPIN)]
    shared = jnp.stack(shared, 0)
    within = jnp.take(shared, (member - jnp.arange(NSPIN, dtype=jnp.int32)) % NSPIN, axis=0)
    incoming = within.transpose(1, 0, 2, 3, 4).reshape(nspace, 2, rows, count_ev)
    count_ops = partial.shape[1] // (2 * count_ev)
    gathered = incoming.transpose(1, 0, 2, 3).reshape(2, count_ops, 2, count_ev, count_ev)
    correlators = contract_panel(gathered, perambulators[0])[None]
    return (own_rows, correlators)


def solution(mesh):
    count_cfg = mesh.shape["cfg"]
    count_slabs = mesh.shape["space"] // NSPIN
    split = Mesh(mesh.devices.reshape(count_cfg, count_slabs, NSPIN), ("cfg",) + SPACE)
    placed = (
        P("cfg", None, None, None, SPACE),
        P("cfg", None, None, None, None, SPACE),
        P(("cfg",) + SPACE, None, None, None),
        P(),
        P(),
        P(),
    )
    return jax.shard_map(
        body,
        mesh=split,
        in_specs=placed,
        out_specs=(P("cfg", SPACE, None), P(("cfg",) + SPACE, None, None)),
        check_vma=False,
    )
```

```python
import functools
import math

import jax
import jax.numpy as jnp
from jax import lax
from jax.experimental import pallas as pl
from jax.experimental.pallas import tpu as pltpu
from jax.sharding import Mesh, PartitionSpec as P

NSPIN = 4
LY = 32
LZ = 8
SPACE = ("slab", "member")


def shifted(block, axis, distance):
    devices = range(lax.axis_size(axis))
    route = [((i - distance) % len(devices), i) for i in devices]
    return lax.ppermute(block, axis, route)


def swapped(value, axis, bit):
    return lax.ppermute(value, axis, [(i, i ^ 1 << bit) for i in range(lax.axis_size(axis))])


def phase_angles(momenta, coords, extents):
    fraction = 0.0
    for course in range(3):
        turns = momenta[:, course : course + 1] * coords[course][None, :] % extents[course]
        fraction = fraction + turns.astype(jnp.float32) / extents[course]
    return 2.0 * math.pi * fraction


def sums_kernel(slot_ref, field_ref, near_ref, link_ref, trig_ref, *rest, scale, course_list):
    out_ref = rest[-1] if len(course_list) == 1 else rest[0]
    count_ev, sites = field_ref.shape[3], field_ref.shape[4]
    lane = lax.broadcasted_iota(jnp.int32, (count_ev, sites), 1)
    last_z = lane % LZ == LZ - 1
    last_row = lane >= sites - LZ
    if len(course_list) == 1:
        left = trig_ref[0]
    else:
        cosine = trig_ref[0:1, :]
        sine_part = trig_ref[1:2, :]
        here = [[field_ref[0, part, colour].astype(jnp.float32) for colour in range(3)] for part in range(2)]
        phased_real = [(cosine * here[0][c] - sine_part * here[1][c]).astype(jnp.bfloat16) for c in range(3)]
        phased_imag = [(sine_part * here[0][c] + cosine * here[1][c]).astype(jnp.bfloat16) for c in range(3)]
        real_rows = jnp.concatenate(phased_real + phased_imag, axis=1)
        imag_rows = jnp.concatenate([-v for v in phased_imag] + phased_real, axis=1)
        left = jnp.concatenate([real_rows, imag_rows], axis=0)
        rest[1][0] = left
    rows = 2 * count_ev
    for course in course_list:
        if course == 0:
            near = [[near_ref[0, part, colour].astype(jnp.float32) for colour in range(3)] for part in range(2)]
        elif course == 1:
            near = [
                [
                    jnp.where(last_row, near_ref[0, part, colour].astype(jnp.float32), pltpu.roll(here[part][colour], sites - LZ, 1))
                    for colour in range(3)
                ]
                for part in range(2)
            ]
        else:
            near = [
                [
                    jnp.where(last_z, pltpu.roll(here[part][colour], LZ - 1, 1), pltpu.roll(here[part][colour], sites - 1, 1))
                    for colour in range(3)
                ]
                for part in range(2)
            ]
        moved_real = []
        moved_imag = []
        for outer in range(3):
            real_part = 0.0
            imag_part = 0.0
            for inner in range(3):
                link_real = link_ref[0, course, 0, outer, inner : inner + 1, :]
                link_imag = link_ref[0, course, 1, outer, inner : inner + 1, :]
                real_part = real_part + link_real * near[0][inner] - link_imag * near[1][inner]
                imag_part = imag_part + link_real * near[1][inner] + link_imag * near[0][inner]
            moved_real.append(real_part.astype(jnp.bfloat16))
            moved_imag.append(imag_part.astype(jnp.bfloat16))
        right = jnp.concatenate(moved_real + moved_imag, axis=1)
        joined = lax.dot_general(left, right, (((1,), (1,)), ((), ())), preferred_element_type=jnp.float32)
        if len(course_list) == 1:
            out_ref[0] = (joined * scale).astype(out_ref.dtype)
        else:
            start = pl.multiple_of(slot_ref[course] * rows, rows)
            out_ref[0, pl.ds(start, rows), :] = (joined * scale).astype(out_ref.dtype)


def local_sums(eigenvectors, gauge_links, far_tile, row_in, directions, angle, scale):
    time_count, _, _, count_ev, sites = eigenvectors.shape
    count_ops = directions.shape[0]
    slot_of = jnp.sum(
        (directions[None, :] == jnp.arange(count_ops, dtype=jnp.int32)[:, None]) * jnp.arange(count_ops, dtype=jnp.int32)[None, :],
        axis=1,
    ).astype(jnp.int32)
    row_wide = jnp.pad(row_in, ((0, 0),) * 4 + ((sites - LZ, 0),))
    trig = jnp.stack([jnp.cos(angle), jnp.sin(angle)], 0)
    field_spec = pl.BlockSpec((1, 2, 3, count_ev, sites), lambda t, slot: (t, 0, 0, 0, 0))
    link_spec = pl.BlockSpec((1,) + gauge_links.shape[1:], lambda t, slot: (t, 0, 0, 0, 0, 0))
    trig_spec = pl.BlockSpec(trig.shape, lambda t, slot: (0, 0))
    rows = count_ops * 2 * count_ev
    near_courses = tuple(course for course in range(count_ops) if course != 0)
    left_rows = 2 * count_ev
    left_spec = pl.BlockSpec((1, left_rows, 6 * sites), lambda t, slot: (t, 0, 0))
    first_spec = pltpu.PrefetchScalarGridSpec(
        num_scalar_prefetch=1,
        grid=(time_count,),
        in_specs=[field_spec, field_spec, link_spec, trig_spec],
        out_specs=[pl.BlockSpec((1, rows, count_ev), lambda t, slot: (t, 0, 0)), left_spec],
    )
    partial, left = pl.pallas_call(
        functools.partial(sums_kernel, scale=scale, course_list=near_courses),
        grid_spec=first_spec,
        out_shape=(
            jax.ShapeDtypeStruct((time_count, rows, count_ev), jnp.bfloat16),
            jax.ShapeDtypeStruct((time_count, left_rows, 6 * sites), jnp.bfloat16),
        ),
    )(slot_of, eigenvectors, row_wide, gauge_links, trig)
    second_spec = pltpu.PrefetchScalarGridSpec(
        num_scalar_prefetch=1,
        grid=(time_count,),
        in_specs=[pl.BlockSpec(memory_space=pl.ANY), field_spec, link_spec, left_spec, pl.BlockSpec(memory_space=pl.ANY)],
        out_specs=pl.BlockSpec((1, 2 * count_ev, count_ev), lambda t, slot: (t, slot[0], 0)),
    )
    return pl.pallas_call(
        functools.partial(sums_kernel, scale=scale, course_list=(0,)),
        grid_spec=second_spec,
        out_shape=jax.ShapeDtypeStruct((time_count, rows, count_ev), jnp.bfloat16),
        input_output_aliases={5: 0},
    )(slot_of, eigenvectors, far_tile, gauge_links, left, partial)


def panel_kernel(sink_ref, source_ref, stack_ref, wide_ref, out_ref):
    count_ev = sink_ref.shape[3]
    sink_real = sink_ref[0, 0, 0]
    sink_imag = sink_ref[0, 0, 1]
    sink_wide = jnp.concatenate(
        [
            jnp.concatenate([sink_real, -sink_imag], axis=1),
            jnp.concatenate([sink_imag, sink_real], axis=1),
        ],
        axis=0,
    )
    left = jnp.dot(sink_wide, stack_ref[...], preferred_element_type=jnp.float32)
    source_stack = jnp.concatenate([source_ref[0, 0, 0], source_ref[0, 0, 1]], axis=0)
    right = jnp.dot(wide_ref[...], source_stack, preferred_element_type=jnp.float32)
    total_real = 0.0
    total_imag = 0.0
    half = NSPIN * count_ev
    for spin in range(NSPIN):
        left_real = left[:count_ev, spin * count_ev : (spin + 1) * count_ev]
        left_imag = left[count_ev:, spin * count_ev : (spin + 1) * count_ev]
        right_real = right[spin * count_ev : (spin + 1) * count_ev]
        right_imag = right[half + spin * count_ev : half + (spin + 1) * count_ev]
        total_real = total_real + left_real * right_real + left_imag * right_imag
        total_imag = total_imag + left_imag * right_real - left_real * right_imag
    out_ref[0, 0:1, :] = jnp.sum(total_real, axis=0, keepdims=True)
    out_ref[0, 1:2, :] = jnp.sum(total_imag, axis=0, keepdims=True)


def contract_panel(gathered, panel):
    count_ops, count_ev = gathered.shape[1], panel.shape[1]
    stack = panel.reshape(2 * count_ev, NSPIN * count_ev)
    blocks = panel.reshape(2, count_ev, NSPIN, count_ev).transpose(0, 2, 1, 3).reshape(2, NSPIN * count_ev, count_ev)
    wide = jnp.concatenate(
        [
            jnp.concatenate([blocks[0], -blocks[1]], axis=1),
            jnp.concatenate([blocks[1], blocks[0]], axis=1),
        ],
        axis=0,
    )
    sums = pl.pallas_call(
        panel_kernel,
        grid=(count_ops,),
        in_specs=[
            pl.BlockSpec((1, 1, 2, count_ev, count_ev), lambda a: (0, a, 0, 0, 0)),
            pl.BlockSpec((1, 1, 2, count_ev, count_ev), lambda a: (1, a, 0, 0, 0)),
            pl.BlockSpec(stack.shape, lambda a: (0, 0)),
            pl.BlockSpec(wide.shape, lambda a: (0, 0)),
        ],
        out_specs=pl.BlockSpec((1, 2, count_ev), lambda a: (a, 0, 0)),
        out_shape=jax.ShapeDtypeStruct((count_ops, 2, count_ev), jnp.float32),
    )(gathered, gathered, stack, wide)
    return jnp.sum(sums, axis=-1) * (1.0 / (16.0 * count_ev))


def body(eigenvectors, gauge_links, perambulators, directions, momenta, pair_times):
    time_count = eigenvectors.shape[0]
    count_ev = eigenvectors.shape[3]
    local_sites = eigenvectors.shape[4]
    count_slabs = lax.axis_size("slab")
    nspace = NSPIN * count_slabs
    member = lax.axis_index("member")
    device = lax.axis_index("slab") * NSPIN + member
    half_rows = LY // 2
    extent_x = nspace // 2
    column = jnp.arange(local_sites, dtype=jnp.int32)
    coord_x = device // 2 + 0 * column
    coord_y = device % 2 * half_rows + column // LZ
    coord_z = column % LZ
    angle = phase_angles(momenta, (coord_x, coord_y, coord_z), (extent_x, LY, LZ))[0]
    far_tile = shifted(eigenvectors, SPACE, -2)
    row_in = swapped(eigenvectors[..., :LZ], SPACE, 0)
    scale = 1.0 / math.sqrt(3.0 * extent_x * LY * LZ)
    partial = local_sums(eigenvectors, gauge_links, far_tile, row_in, directions, angle, scale)
    rows = partial.shape[1] // nspace
    if count_slabs <= 8:
        slab = lax.axis_index("slab")
        core = member % 2
        side = member // 2
        blocks = partial.reshape(time_count, count_slabs, 2, 2, rows, count_ev)
        keep = lax.dynamic_index_in_dim(blocks, core, 3, keepdims=False).astype(jnp.float32)
        send = lax.dynamic_index_in_dim(blocks, 1 - core, 3, keepdims=False)
        chip_sum = keep + swapped(send, "member", 0).astype(jnp.float32)
        keep = lax.dynamic_index_in_dim(chip_sum, side, 2, keepdims=False)
        send = lax.dynamic_index_in_dim(chip_sum, 1 - side, 2, keepdims=False).astype(jnp.bfloat16)
        slab_sum = keep + swapped(send, "member", 1).astype(jnp.float32)
        slab_part = slab_sum.astype(jnp.bfloat16)
        total = lax.dynamic_index_in_dim(slab_sum, slab, 1, keepdims=False)
        for shift in range(1, count_slabs):
            piece = lax.dynamic_index_in_dim(slab_part, (slab + shift) % count_slabs, 1, keepdims=False)
            total = total + shifted(piece, "slab", shift).astype(jnp.float32)
        own_rows = total.astype(jnp.bfloat16)
    else:
        own_rows = lax.psum_scatter(partial, SPACE, scatter_dimension=1, tiled=True)
    slabs = jnp.arange(count_slabs, dtype=jnp.int32)
    wanted = jnp.stack([pair_times[slabs, 1], pair_times[slabs, 0]], 1)
    outgoing = jnp.take(own_rows, wanted.reshape(-1), axis=0).reshape(count_slabs, 2, rows, count_ev)
    if count_slabs <= 8:
        pieces = [jnp.take(outgoing, (slab + shift) % count_slabs, axis=0) for shift in range(count_slabs)]
        arrived = [pieces[0]] + [shifted(pieces[shift], "slab", shift) for shift in range(1, count_slabs)]
        arrived = jnp.stack(arrived, 0)
        across = jnp.take(arrived, (slab - jnp.arange(count_slabs, dtype=jnp.int32)) % count_slabs, axis=0)
    else:
        across = lax.all_to_all(outgoing, "slab", 0, 0, tiled=True)
    shared = [across] + [shifted(across, "member", shift) for shift in range(1, NSPIN)]
    shared = jnp.stack(shared, 0)
    within = jnp.take(shared, (member - jnp.arange(NSPIN, dtype=jnp.int32)) % NSPIN, axis=0)
    incoming = within.transpose(1, 0, 2, 3, 4).reshape(nspace, 2, rows, count_ev)
    count_ops = partial.shape[1] // (2 * count_ev)
    gathered = incoming.transpose(1, 0, 2, 3).reshape(2, count_ops, 2, count_ev, count_ev)
    correlators = contract_panel(gathered, perambulators[0])[None]
    return (own_rows, correlators)


def solution(mesh):
    count_cfg = mesh.shape["cfg"]
    count_slabs = mesh.shape["space"] // NSPIN
    split = Mesh(mesh.devices.reshape(count_cfg, count_slabs, NSPIN), ("cfg",) + SPACE)
    placed = (
        P("cfg", None, None, None, SPACE),
        P("cfg", None, None, None, None, SPACE),
        P(("cfg",) + SPACE, None, None, None),
        P(),
        P(),
        P(),
    )
    return jax.shard_map(
        body,
        mesh=split,
        in_specs=placed,
        out_specs=(P("cfg", SPACE, None), P(("cfg",) + SPACE, None, None)),
        check_vma=False,
    )
```

```python
import functools
import math

import jax
import jax.numpy as jnp
from jax import lax
from jax.experimental import pallas as pl
from jax.experimental.pallas import tpu as pltpu
from jax.sharding import Mesh, PartitionSpec as P

NSPIN = 4
LY = 32
LZ = 8
SPACE = ("slab", "member")


def shifted(block, axis, distance):
    devices = range(lax.axis_size(axis))
    route = [((i - distance) % len(devices), i) for i in devices]
    return lax.ppermute(block, axis, route)


def swapped(value, axis, bit):
    return lax.ppermute(value, axis, [(i, i ^ 1 << bit) for i in range(lax.axis_size(axis))])


def phase_angles(momenta, coords, extents):
    fraction = 0.0
    for course in range(3):
        turns = momenta[:, course : course + 1] * coords[course][None, :] % extents[course]
        fraction = fraction + turns.astype(jnp.float32) / extents[course]
    return 2.0 * math.pi * fraction


def sums_kernel(slot_ref, field_ref, near_ref, link_ref, trig_ref, *rest, scale, course_list):
    out_ref = rest[-1] if len(course_list) == 1 else rest[0]
    count_ev, sites = field_ref.shape[3], field_ref.shape[4]
    lane = lax.broadcasted_iota(jnp.int32, (count_ev, sites), 1)
    last_z = lane % LZ == LZ - 1
    last_row = lane >= sites - LZ
    if len(course_list) == 1:
        left = trig_ref[0]
    else:
        cosine = trig_ref[0:1, :]
        sine_part = trig_ref[1:2, :]
        here = [[field_ref[0, part, colour].astype(jnp.float32) for colour in range(3)] for part in range(2)]
        phased_real = [(cosine * here[0][c] - sine_part * here[1][c]).astype(jnp.bfloat16) for c in range(3)]
        phased_imag = [(sine_part * here[0][c] + cosine * here[1][c]).astype(jnp.bfloat16) for c in range(3)]
        real_rows = jnp.concatenate(phased_real + phased_imag, axis=1)
        imag_rows = jnp.concatenate([-v for v in phased_imag] + phased_real, axis=1)
        left = jnp.concatenate([real_rows, imag_rows], axis=0)
        rest[1][0] = left
    rows = 2 * count_ev
    for course in course_list:
        if course == 0:
            near = [[near_ref[0, part, colour].astype(jnp.float32) for colour in range(3)] for part in range(2)]
        elif course == 1:
            near = [
                [
                    jnp.where(last_row, near_ref[0, part, colour].astype(jnp.float32), pltpu.roll(here[part][colour], sites - LZ, 1))
                    for colour in range(3)
                ]
                for part in range(2)
            ]
        else:
            near = [
                [
                    jnp.where(last_z, pltpu.roll(here[part][colour], LZ - 1, 1), pltpu.roll(here[part][colour], sites - 1, 1))
                    for colour in range(3)
                ]
                for part in range(2)
            ]
        moved_real = []
        moved_imag = []
        for outer in range(3):
            real_part = 0.0
            imag_part = 0.0
            for inner in range(3):
                link_real = link_ref[0, course, 0, outer, inner : inner + 1, :]
                link_imag = link_ref[0, course, 1, outer, inner : inner + 1, :]
                real_part = real_part + link_real * near[0][inner] - link_imag * near[1][inner]
                imag_part = imag_part + link_real * near[1][inner] + link_imag * near[0][inner]
            moved_real.append(real_part.astype(jnp.bfloat16))
            moved_imag.append(imag_part.astype(jnp.bfloat16))
        right = jnp.concatenate(moved_real + moved_imag, axis=1)
        joined = lax.dot_general(left, right, (((1,), (1,)), ((), ())), preferred_element_type=jnp.float32)
        if len(course_list) == 1:
            out_ref[0] = (joined * scale).astype(out_ref.dtype)
        else:
            start = pl.multiple_of(slot_ref[course] * rows, rows)
            out_ref[0, pl.ds(start, rows), :] = (joined * scale).astype(out_ref.dtype)


def local_sums(eigenvectors, gauge_links, far_tile, row_in, directions, angle, scale):
    time_count, _, _, count_ev, sites = eigenvectors.shape
    count_ops = directions.shape[0]
    slot_of = jnp.sum(
        (directions[None, :] == jnp.arange(count_ops, dtype=jnp.int32)[:, None]) * jnp.arange(count_ops, dtype=jnp.int32)[None, :],
        axis=1,
    ).astype(jnp.int32)
    row_wide = jnp.pad(row_in, ((0, 0),) * 4 + ((sites - LZ, 0),))
    trig = jnp.stack([jnp.cos(angle), jnp.sin(angle)], 0)
    field_spec = pl.BlockSpec((1, 2, 3, count_ev, sites), lambda t, slot: (t, 0, 0, 0, 0))
    link_spec = pl.BlockSpec((1,) + gauge_links.shape[1:], lambda t, slot: (t, 0, 0, 0, 0, 0))
    trig_spec = pl.BlockSpec(trig.shape, lambda t, slot: (0, 0))
    rows = count_ops * 2 * count_ev
    near_courses = tuple(course for course in range(count_ops) if course != 0)
    left_rows = 2 * count_ev
    left_spec = pl.BlockSpec((1, left_rows, 6 * sites), lambda t, slot: (t, 0, 0))
    first_spec = pltpu.PrefetchScalarGridSpec(
        num_scalar_prefetch=1,
        grid=(time_count,),
        in_specs=[field_spec, field_spec, link_spec, trig_spec],
        out_specs=[pl.BlockSpec((1, rows, count_ev), lambda t, slot: (t, 0, 0)), left_spec],
    )
    partial, left = pl.pallas_call(
        functools.partial(sums_kernel, scale=scale, course_list=near_courses),
        grid_spec=first_spec,
        out_shape=(
            jax.ShapeDtypeStruct((time_count, rows, count_ev), jnp.bfloat16),
            jax.ShapeDtypeStruct((time_count, left_rows, 6 * sites), jnp.bfloat16),
        ),
    )(slot_of, eigenvectors, row_wide, gauge_links, trig)
    second_spec = pltpu.PrefetchScalarGridSpec(
        num_scalar_prefetch=1,
        grid=(time_count,),
        in_specs=[pl.BlockSpec(memory_space=pl.ANY), field_spec, link_spec, left_spec, pl.BlockSpec(memory_space=pl.ANY)],
        out_specs=pl.BlockSpec((1, 2 * count_ev, count_ev), lambda t, slot: (t, slot[0], 0)),
    )
    return pl.pallas_call(
        functools.partial(sums_kernel, scale=scale, course_list=(0,)),
        grid_spec=second_spec,
        out_shape=jax.ShapeDtypeStruct((time_count, rows, count_ev), jnp.bfloat16),
        input_output_aliases={5: 0},
    )(slot_of, eigenvectors, far_tile, gauge_links, left, partial)


def panel_kernel(sink_ref, source_ref, stack_ref, wide_ref, out_ref):
    count_ev = sink_ref.shape[3]
    sink_real = sink_ref[0, 0, 0]
    sink_imag = sink_ref[0, 0, 1]
    sink_wide = jnp.concatenate(
        [
            jnp.concatenate([sink_real, -sink_imag], axis=1),
            jnp.concatenate([sink_imag, sink_real], axis=1),
        ],
        axis=0,
    )
    left = jnp.dot(sink_wide, stack_ref[...], preferred_element_type=jnp.float32)
    source_stack = jnp.concatenate([source_ref[0, 0, 0], source_ref[0, 0, 1]], axis=0)
    right = jnp.dot(wide_ref[...], source_stack, preferred_element_type=jnp.float32)
    total_real = 0.0
    total_imag = 0.0
    half = NSPIN * count_ev
    for spin in range(NSPIN):
        left_real = left[:count_ev, spin * count_ev : (spin + 1) * count_ev]
        left_imag = left[count_ev:, spin * count_ev : (spin + 1) * count_ev]
        right_real = right[spin * count_ev : (spin + 1) * count_ev]
        right_imag = right[half + spin * count_ev : half + (spin + 1) * count_ev]
        total_real = total_real + left_real * right_real + left_imag * right_imag
        total_imag = total_imag + left_imag * right_real - left_real * right_imag
    out_ref[0, 0:1, :] = jnp.sum(total_real, axis=0, keepdims=True)
    out_ref[0, 1:2, :] = jnp.sum(total_imag, axis=0, keepdims=True)


def contract_panel(gathered, panel):
    count_ops, count_ev = gathered.shape[1], panel.shape[1]
    stack = panel.reshape(2 * count_ev, NSPIN * count_ev)
    blocks = panel.reshape(2, count_ev, NSPIN, count_ev).transpose(0, 2, 1, 3).reshape(2, NSPIN * count_ev, count_ev)
    wide = jnp.concatenate(
        [
            jnp.concatenate([blocks[0], -blocks[1]], axis=1),
            jnp.concatenate([blocks[1], blocks[0]], axis=1),
        ],
        axis=0,
    )
    sums = pl.pallas_call(
        panel_kernel,
        grid=(count_ops,),
        in_specs=[
            pl.BlockSpec((1, 1, 2, count_ev, count_ev), lambda a: (0, a, 0, 0, 0)),
            pl.BlockSpec((1, 1, 2, count_ev, count_ev), lambda a: (1, a, 0, 0, 0)),
            pl.BlockSpec(stack.shape, lambda a: (0, 0)),
            pl.BlockSpec(wide.shape, lambda a: (0, 0)),
        ],
        out_specs=pl.BlockSpec((1, 2, count_ev), lambda a: (a, 0, 0)),
        out_shape=jax.ShapeDtypeStruct((count_ops, 2, count_ev), jnp.float32),
    )(gathered, gathered, stack, wide)
    return jnp.sum(sums, axis=-1) * (1.0 / (16.0 * count_ev))


def body(eigenvectors, gauge_links, perambulators, directions, momenta, pair_times):
    time_count = eigenvectors.shape[0]
    count_ev = eigenvectors.shape[3]
    local_sites = eigenvectors.shape[4]
    count_slabs = lax.axis_size("slab")
    nspace = NSPIN * count_slabs
    member = lax.axis_index("member")
    device = lax.axis_index("slab") * NSPIN + member
    half_rows = LY // 2
    extent_x = nspace // 2
    column = jnp.arange(local_sites, dtype=jnp.int32)
    coord_x = device // 2 + 0 * column
    coord_y = device % 2 * half_rows + column // LZ
    coord_z = column % LZ
    angle = phase_angles(momenta, (coord_x, coord_y, coord_z), (extent_x, LY, LZ))[0]
    far_tile = shifted(eigenvectors, SPACE, -2)
    row_in = swapped(eigenvectors[..., :LZ], SPACE, 0)
    scale = 1.0 / math.sqrt(3.0 * extent_x * LY * LZ)
    partial = local_sums(eigenvectors, gauge_links, far_tile, row_in, directions, angle, scale)
    rows = partial.shape[1] // nspace
    if count_slabs <= 8:
        slab = lax.axis_index("slab")
        core = member % 2
        side = member // 2
        blocks = partial.reshape(time_count, count_slabs, 2, 2, rows, count_ev)
        keep = lax.dynamic_index_in_dim(blocks, core, 3, keepdims=False).astype(jnp.float32)
        send = lax.dynamic_index_in_dim(blocks, 1 - core, 3, keepdims=False)
        chip_sum = keep + swapped(send, "member", 0).astype(jnp.float32)
        halves = 2 if time_count % 2 == 0 else 1
        span = time_count // halves
        own_parts = []
        for half in range(halves):
            chunk = chip_sum[half * span : (half + 1) * span]
            keep = lax.dynamic_index_in_dim(chunk, side, 2, keepdims=False)
            send = lax.dynamic_index_in_dim(chunk, 1 - side, 2, keepdims=False).astype(jnp.bfloat16)
            slab_sum = keep + swapped(send, "member", 1).astype(jnp.float32)
            slab_part = slab_sum.astype(jnp.bfloat16)
            total = lax.dynamic_index_in_dim(slab_sum, slab, 1, keepdims=False)
            for shift in range(1, count_slabs):
                piece = lax.dynamic_index_in_dim(slab_part, (slab + shift) % count_slabs, 1, keepdims=False)
                total = total + shifted(piece, "slab", shift).astype(jnp.float32)
            own_parts.append(total.astype(jnp.bfloat16))
        own_rows = jnp.concatenate(own_parts, 0)
    else:
        own_rows = lax.psum_scatter(partial, SPACE, scatter_dimension=1, tiled=True)
    slabs = jnp.arange(count_slabs, dtype=jnp.int32)
    wanted = jnp.stack([pair_times[slabs, 1], pair_times[slabs, 0]], 1)
    outgoing = jnp.take(own_rows, wanted.reshape(-1), axis=0).reshape(count_slabs, 2, rows, count_ev)
    if count_slabs <= 8:
        pieces = [jnp.take(outgoing, (slab + shift) % count_slabs, axis=0) for shift in range(count_slabs)]
        arrived = [pieces[0]] + [shifted(pieces[shift], "slab", shift) for shift in range(1, count_slabs)]
        arrived = jnp.stack(arrived, 0)
        across = jnp.take(arrived, (slab - jnp.arange(count_slabs, dtype=jnp.int32)) % count_slabs, axis=0)
    else:
        across = lax.all_to_all(outgoing, "slab", 0, 0, tiled=True)
    shared = [across] + [shifted(across, "member", shift) for shift in range(1, NSPIN)]
    shared = jnp.stack(shared, 0)
    within = jnp.take(shared, (member - jnp.arange(NSPIN, dtype=jnp.int32)) % NSPIN, axis=0)
    incoming = within.transpose(1, 0, 2, 3, 4).reshape(nspace, 2, rows, count_ev)
    count_ops = partial.shape[1] // (2 * count_ev)
    gathered = incoming.transpose(1, 0, 2, 3).reshape(2, count_ops, 2, count_ev, count_ev)
    correlators = contract_panel(gathered, perambulators[0])[None]
    return (own_rows, correlators)


def solution(mesh):
    count_cfg = mesh.shape["cfg"]
    count_slabs = mesh.shape["space"] // NSPIN
    split = Mesh(mesh.devices.reshape(count_cfg, count_slabs, NSPIN), ("cfg",) + SPACE)
    placed = (
        P("cfg", None, None, None, SPACE),
        P("cfg", None, None, None, None, SPACE),
        P(("cfg",) + SPACE, None, None, None),
        P(),
        P(),
        P(),
    )
    return jax.shard_map(
        body,
        mesh=split,
        in_specs=placed,
        out_specs=(P("cfg", SPACE, None), P(("cfg",) + SPACE, None, None)),
        check_vma=False,
    )
```

```python
import functools
import math

import jax
import jax.numpy as jnp
from jax import lax
from jax.experimental import pallas as pl
from jax.experimental.pallas import tpu as pltpu
from jax.sharding import Mesh, PartitionSpec as P

NSPIN = 4
LY = 32
LZ = 8
SPACE = ("slab", "member")


def shifted(block, axis, distance):
    devices = range(lax.axis_size(axis))
    route = [((i - distance) % len(devices), i) for i in devices]
    return lax.ppermute(block, axis, route)


def swapped(value, axis, bit):
    return lax.ppermute(value, axis, [(i, i ^ 1 << bit) for i in range(lax.axis_size(axis))])


def phase_angles(momenta, coords, extents):
    fraction = 0.0
    for course in range(3):
        turns = momenta[:, course : course + 1] * coords[course][None, :] % extents[course]
        fraction = fraction + turns.astype(jnp.float32) / extents[course]
    return 2.0 * math.pi * fraction


def sums_kernel(slot_ref, field_ref, near_ref, link_ref, trig_ref, *rest, scale, course_list):
    out_ref = rest[-1] if len(course_list) == 1 else rest[0]
    count_ev, sites = field_ref.shape[3], field_ref.shape[4]
    lane = lax.broadcasted_iota(jnp.int32, (count_ev, sites), 1)
    last_z = lane % LZ == LZ - 1
    last_row = lane >= sites - LZ
    if len(course_list) == 1:
        left = trig_ref[0]
    else:
        cosine = trig_ref[0:1, :]
        sine_part = trig_ref[1:2, :]
        here = [[field_ref[0, part, colour].astype(jnp.float32) for colour in range(3)] for part in range(2)]
        phased_real = [(cosine * here[0][c] - sine_part * here[1][c]).astype(jnp.bfloat16) for c in range(3)]
        phased_imag = [(sine_part * here[0][c] + cosine * here[1][c]).astype(jnp.bfloat16) for c in range(3)]
        real_rows = jnp.concatenate(phased_real + phased_imag, axis=1)
        imag_rows = jnp.concatenate([-v for v in phased_imag] + phased_real, axis=1)
        left = jnp.concatenate([real_rows, imag_rows], axis=0)
        rest[1][0] = left
    rows = 2 * count_ev
    for course in course_list:
        if course == 0:
            near = [[near_ref[0, part, colour].astype(jnp.float32) for colour in range(3)] for part in range(2)]
        elif course == 1:
            near = [
                [
                    jnp.where(last_row, near_ref[0, part, colour].astype(jnp.float32), pltpu.roll(here[part][colour], sites - LZ, 1))
                    for colour in range(3)
                ]
                for part in range(2)
            ]
        else:
            near = [
                [
                    jnp.where(last_z, pltpu.roll(here[part][colour], LZ - 1, 1), pltpu.roll(here[part][colour], sites - 1, 1))
                    for colour in range(3)
                ]
                for part in range(2)
            ]
        moved_real = []
        moved_imag = []
        for outer in range(3):
            real_part = 0.0
            imag_part = 0.0
            for inner in range(3):
                link_real = link_ref[0, course, 0, outer, inner : inner + 1, :]
                link_imag = link_ref[0, course, 1, outer, inner : inner + 1, :]
                real_part = real_part + link_real * near[0][inner] - link_imag * near[1][inner]
                imag_part = imag_part + link_real * near[1][inner] + link_imag * near[0][inner]
            moved_real.append(real_part.astype(jnp.bfloat16))
            moved_imag.append(imag_part.astype(jnp.bfloat16))
        right = jnp.concatenate(moved_real + moved_imag, axis=1)
        joined = lax.dot_general(left, right, (((1,), (1,)), ((), ())), preferred_element_type=jnp.float32)
        if len(course_list) == 1:
            out_ref[0] = (joined * scale).astype(out_ref.dtype)
        else:
            start = pl.multiple_of(slot_ref[course] * rows, rows)
            out_ref[0, pl.ds(start, rows), :] = (joined * scale).astype(out_ref.dtype)


def local_sums(eigenvectors, gauge_links, far_tile, row_in, directions, angle, scale):
    time_count, _, _, count_ev, sites = eigenvectors.shape
    count_ops = directions.shape[0]
    slot_of = jnp.sum(
        (directions[None, :] == jnp.arange(count_ops, dtype=jnp.int32)[:, None]) * jnp.arange(count_ops, dtype=jnp.int32)[None, :],
        axis=1,
    ).astype(jnp.int32)
    row_wide = jnp.pad(row_in, ((0, 0),) * 4 + ((sites - LZ, 0),))
    trig = jnp.stack([jnp.cos(angle), jnp.sin(angle)], 0)
    field_spec = pl.BlockSpec((1, 2, 3, count_ev, sites), lambda t, slot: (t, 0, 0, 0, 0))
    link_spec = pl.BlockSpec((1,) + gauge_links.shape[1:], lambda t, slot: (t, 0, 0, 0, 0, 0))
    trig_spec = pl.BlockSpec(trig.shape, lambda t, slot: (0, 0))
    rows = count_ops * 2 * count_ev
    near_courses = tuple(course for course in range(count_ops) if course != 0)
    left_rows = 2 * count_ev
    left_spec = pl.BlockSpec((1, left_rows, 6 * sites), lambda t, slot: (t, 0, 0))
    first_spec = pltpu.PrefetchScalarGridSpec(
        num_scalar_prefetch=1,
        grid=(time_count,),
        in_specs=[field_spec, field_spec, link_spec, trig_spec],
        out_specs=[pl.BlockSpec((1, rows, count_ev), lambda t, slot: (t, 0, 0)), left_spec],
    )
    partial, left = pl.pallas_call(
        functools.partial(sums_kernel, scale=scale, course_list=near_courses),
        grid_spec=first_spec,
        out_shape=(
            jax.ShapeDtypeStruct((time_count, rows, count_ev), jnp.bfloat16),
            jax.ShapeDtypeStruct((time_count, left_rows, 6 * sites), jnp.bfloat16),
        ),
    )(slot_of, eigenvectors, row_wide, gauge_links, trig)
    second_spec = pltpu.PrefetchScalarGridSpec(
        num_scalar_prefetch=1,
        grid=(time_count,),
        in_specs=[pl.BlockSpec(memory_space=pl.ANY), field_spec, link_spec, left_spec, pl.BlockSpec(memory_space=pl.ANY)],
        out_specs=pl.BlockSpec((1, 2 * count_ev, count_ev), lambda t, slot: (t, slot[0], 0)),
    )
    return pl.pallas_call(
        functools.partial(sums_kernel, scale=scale, course_list=(0,)),
        grid_spec=second_spec,
        out_shape=jax.ShapeDtypeStruct((time_count, rows, count_ev), jnp.bfloat16),
        input_output_aliases={5: 0},
    )(slot_of, eigenvectors, far_tile, gauge_links, left, partial)


def panel_kernel(sink_ref, source_ref, stack_ref, wide_ref, out_ref):
    count_ev = sink_ref.shape[3]
    sink_real = sink_ref[0, 0, 0]
    sink_imag = sink_ref[0, 0, 1]
    sink_wide = jnp.concatenate(
        [
            jnp.concatenate([sink_real, -sink_imag], axis=1),
            jnp.concatenate([sink_imag, sink_real], axis=1),
        ],
        axis=0,
    )
    left = jnp.dot(sink_wide, stack_ref[...], preferred_element_type=jnp.float32)
    source_stack = jnp.concatenate([source_ref[0, 0, 0], source_ref[0, 0, 1]], axis=0)
    right = jnp.dot(wide_ref[...], source_stack, preferred_element_type=jnp.float32)
    total_real = 0.0
    total_imag = 0.0
    half = NSPIN * count_ev
    for spin in range(NSPIN):
        left_real = left[:count_ev, spin * count_ev : (spin + 1) * count_ev]
        left_imag = left[count_ev:, spin * count_ev : (spin + 1) * count_ev]
        right_real = right[spin * count_ev : (spin + 1) * count_ev]
        right_imag = right[half + spin * count_ev : half + (spin + 1) * count_ev]
        total_real = total_real + left_real * right_real + left_imag * right_imag
        total_imag = total_imag + left_imag * right_real - left_real * right_imag
    out_ref[0, 0:1, :] = jnp.sum(total_real, axis=0, keepdims=True)
    out_ref[0, 1:2, :] = jnp.sum(total_imag, axis=0, keepdims=True)


def contract_panel(gathered, panel):
    count_ops, count_ev = gathered.shape[1], panel.shape[1]
    stack = panel.reshape(2 * count_ev, NSPIN * count_ev)
    blocks = panel.reshape(2, count_ev, NSPIN, count_ev).transpose(0, 2, 1, 3).reshape(2, NSPIN * count_ev, count_ev)
    wide = jnp.concatenate(
        [
            jnp.concatenate([blocks[0], -blocks[1]], axis=1),
            jnp.concatenate([blocks[1], blocks[0]], axis=1),
        ],
        axis=0,
    )
    sums = pl.pallas_call(
        panel_kernel,
        grid=(count_ops,),
        in_specs=[
            pl.BlockSpec((1, 1, 2, count_ev, count_ev), lambda a: (0, a, 0, 0, 0)),
            pl.BlockSpec((1, 1, 2, count_ev, count_ev), lambda a: (1, a, 0, 0, 0)),
            pl.BlockSpec(stack.shape, lambda a: (0, 0)),
            pl.BlockSpec(wide.shape, lambda a: (0, 0)),
        ],
        out_specs=pl.BlockSpec((1, 2, count_ev), lambda a: (a, 0, 0)),
        out_shape=jax.ShapeDtypeStruct((count_ops, 2, count_ev), jnp.float32),
    )(gathered, gathered, stack, wide)
    return jnp.sum(sums, axis=-1) * (1.0 / (16.0 * count_ev))


def body(eigenvectors, gauge_links, perambulators, directions, momenta, pair_times):
    time_count = eigenvectors.shape[0]
    count_ev = eigenvectors.shape[3]
    local_sites = eigenvectors.shape[4]
    count_slabs = lax.axis_size("slab")
    nspace = NSPIN * count_slabs
    member = lax.axis_index("member")
    device = lax.axis_index("slab") * NSPIN + member
    half_rows = LY // 2
    extent_x = nspace // 2
    column = jnp.arange(local_sites, dtype=jnp.int32)
    coord_x = device // 2 + 0 * column
    coord_y = device % 2 * half_rows + column // LZ
    coord_z = column % LZ
    angle = phase_angles(momenta, (coord_x, coord_y, coord_z), (extent_x, LY, LZ))[0]
    far_tile = shifted(eigenvectors, SPACE, -2)
    row_in = swapped(eigenvectors[..., :LZ], SPACE, 0)
    scale = 1.0 / math.sqrt(3.0 * extent_x * LY * LZ)
    partial = local_sums(eigenvectors, gauge_links, far_tile, row_in, directions, angle, scale)
    rows = partial.shape[1] // nspace
    if count_slabs <= 8:
        slab = lax.axis_index("slab")
        core = member % 2
        side = member // 2
        blocks = partial.reshape(time_count, count_slabs, 2, 2, rows, count_ev)
        halves = 3 if time_count % 3 == 0 else (2 if time_count % 2 == 0 else 1)
        span = time_count // halves
        own_parts = []
        for half in range(halves):
            part_blocks = blocks[half * span : (half + 1) * span]
            keep = lax.dynamic_index_in_dim(part_blocks, core, 3, keepdims=False).astype(jnp.float32)
            send = lax.dynamic_index_in_dim(part_blocks, 1 - core, 3, keepdims=False)
            chunk = keep + swapped(send, "member", 0).astype(jnp.float32)
            keep = lax.dynamic_index_in_dim(chunk, side, 2, keepdims=False)
            send = lax.dynamic_index_in_dim(chunk, 1 - side, 2, keepdims=False).astype(jnp.bfloat16)
            slab_sum = keep + swapped(send, "member", 1).astype(jnp.float32)
            slab_part = slab_sum.astype(jnp.bfloat16)
            total = lax.dynamic_index_in_dim(slab_sum, slab, 1, keepdims=False)
            for shift in range(1, count_slabs):
                piece = lax.dynamic_index_in_dim(slab_part, (slab + shift) % count_slabs, 1, keepdims=False)
                total = total + shifted(piece, "slab", shift).astype(jnp.float32)
            own_parts.append(total.astype(jnp.bfloat16))
        own_rows = jnp.concatenate(own_parts, 0)
    else:
        own_rows = lax.psum_scatter(partial, SPACE, scatter_dimension=1, tiled=True)
    slabs = jnp.arange(count_slabs, dtype=jnp.int32)
    wanted = jnp.stack([pair_times[slabs, 1], pair_times[slabs, 0]], 1)
    outgoing = jnp.take(own_rows, wanted.reshape(-1), axis=0).reshape(count_slabs, 2, rows, count_ev)
    if count_slabs <= 8:
        pieces = [jnp.take(outgoing, (slab + shift) % count_slabs, axis=0) for shift in range(count_slabs)]
        arrived = [pieces[0]] + [shifted(pieces[shift], "slab", shift) for shift in range(1, count_slabs)]
        arrived = jnp.stack(arrived, 0)
        across = jnp.take(arrived, (slab - jnp.arange(count_slabs, dtype=jnp.int32)) % count_slabs, axis=0)
    else:
        across = lax.all_to_all(outgoing, "slab", 0, 0, tiled=True)
    shared = [across] + [shifted(across, "member", shift) for shift in range(1, NSPIN)]
    shared = jnp.stack(shared, 0)
    within = jnp.take(shared, (member - jnp.arange(NSPIN, dtype=jnp.int32)) % NSPIN, axis=0)
    incoming = within.transpose(1, 0, 2, 3, 4).reshape(nspace, 2, rows, count_ev)
    count_ops = partial.shape[1] // (2 * count_ev)
    gathered = incoming.transpose(1, 0, 2, 3).reshape(2, count_ops, 2, count_ev, count_ev)
    correlators = contract_panel(gathered, perambulators[0])[None]
    return (own_rows, correlators)


def solution(mesh):
    count_cfg = mesh.shape["cfg"]
    count_slabs = mesh.shape["space"] // NSPIN
    split = Mesh(mesh.devices.reshape(count_cfg, count_slabs, NSPIN), ("cfg",) + SPACE)
    placed = (
        P("cfg", None, None, None, SPACE),
        P("cfg", None, None, None, None, SPACE),
        P(("cfg",) + SPACE, None, None, None),
        P(),
        P(),
        P(),
    )
    return jax.shard_map(
        body,
        mesh=split,
        in_specs=placed,
        out_specs=(P("cfg", SPACE, None), P(("cfg",) + SPACE, None, None)),
        check_vma=False,
    )
```

```python
import functools
import math

import jax
import jax.numpy as jnp
from jax import lax
from jax.experimental import pallas as pl
from jax.experimental.pallas import tpu as pltpu
from jax.sharding import Mesh, PartitionSpec as P

NSPIN = 4
LY = 32
LZ = 8
SPACE = ("slab", "member")


def shifted(block, axis, distance):
    devices = range(lax.axis_size(axis))
    route = [((i - distance) % len(devices), i) for i in devices]
    return lax.ppermute(block, axis, route)


def swapped(value, axis, bit):
    return lax.ppermute(value, axis, [(i, i ^ 1 << bit) for i in range(lax.axis_size(axis))])


def phase_angles(momenta, coords, extents):
    fraction = 0.0
    for course in range(3):
        turns = momenta[:, course : course + 1] * coords[course][None, :] % extents[course]
        fraction = fraction + turns.astype(jnp.float32) / extents[course]
    return 2.0 * math.pi * fraction


def sums_kernel(slot_ref, field_ref, near_ref, link_ref, trig_ref, *rest, scale, course_list):
    out_ref = rest[-1] if len(course_list) == 1 else rest[0]
    count_ev, sites = field_ref.shape[3], field_ref.shape[4]
    lane = lax.broadcasted_iota(jnp.int32, (count_ev, sites), 1)
    last_z = lane % LZ == LZ - 1
    last_row = lane >= sites - LZ
    if len(course_list) == 1:
        left = trig_ref[0]
    else:
        cosine = trig_ref[0:1, :]
        sine_part = trig_ref[1:2, :]
        here = [[field_ref[0, part, colour].astype(jnp.float32) for colour in range(3)] for part in range(2)]
        phased_real = [(cosine * here[0][c] - sine_part * here[1][c]).astype(jnp.bfloat16) for c in range(3)]
        phased_imag = [(sine_part * here[0][c] + cosine * here[1][c]).astype(jnp.bfloat16) for c in range(3)]
        real_rows = jnp.concatenate(phased_real + phased_imag, axis=1)
        imag_rows = jnp.concatenate([-v for v in phased_imag] + phased_real, axis=1)
        left = jnp.concatenate([real_rows, imag_rows], axis=0)
        rest[1][0] = left
    rows = 2 * count_ev
    for course in course_list:
        if course == 0:
            near = [[near_ref[0, part, colour].astype(jnp.float32) for colour in range(3)] for part in range(2)]
        elif course == 1:
            near = [
                [
                    jnp.where(last_row, near_ref[0, part, colour].astype(jnp.float32), pltpu.roll(here[part][colour], sites - LZ, 1))
                    for colour in range(3)
                ]
                for part in range(2)
            ]
        else:
            near = [
                [
                    jnp.where(last_z, pltpu.roll(here[part][colour], LZ - 1, 1), pltpu.roll(here[part][colour], sites - 1, 1))
                    for colour in range(3)
                ]
                for part in range(2)
            ]
        moved_real = []
        moved_imag = []
        for outer in range(3):
            real_part = 0.0
            imag_part = 0.0
            for inner in range(3):
                link_real = link_ref[0, course, 0, outer, inner : inner + 1, :]
                link_imag = link_ref[0, course, 1, outer, inner : inner + 1, :]
                real_part = real_part + link_real * near[0][inner] - link_imag * near[1][inner]
                imag_part = imag_part + link_real * near[1][inner] + link_imag * near[0][inner]
            moved_real.append(real_part.astype(jnp.bfloat16))
            moved_imag.append(imag_part.astype(jnp.bfloat16))
        right = jnp.concatenate(moved_real + moved_imag, axis=1)
        joined = lax.dot_general(left, right, (((1,), (1,)), ((), ())), preferred_element_type=jnp.float32)
        if len(course_list) == 1:
            out_ref[0] = rest[0][0]
            start = pl.multiple_of(slot_ref[course] * rows, rows)
            out_ref[0, pl.ds(start, rows), :] = (joined * scale).astype(out_ref.dtype)
        else:
            start = pl.multiple_of(slot_ref[course] * rows, rows)
            out_ref[0, pl.ds(start, rows), :] = (joined * scale).astype(out_ref.dtype)


def local_sums(eigenvectors, gauge_links, far_tile, row_in, directions, angle, scale):
    time_count, _, _, count_ev, sites = eigenvectors.shape
    count_ops = directions.shape[0]
    slot_of = jnp.sum(
        (directions[None, :] == jnp.arange(count_ops, dtype=jnp.int32)[:, None]) * jnp.arange(count_ops, dtype=jnp.int32)[None, :],
        axis=1,
    ).astype(jnp.int32)
    row_wide = jnp.pad(row_in, ((0, 0),) * 4 + ((sites - LZ, 0),))
    trig = jnp.stack([jnp.cos(angle), jnp.sin(angle)], 0)
    field_spec = pl.BlockSpec((1, 2, 3, count_ev, sites), lambda t, slot: (t, 0, 0, 0, 0))
    link_spec = pl.BlockSpec((1,) + gauge_links.shape[1:], lambda t, slot: (t, 0, 0, 0, 0, 0))
    trig_spec = pl.BlockSpec(trig.shape, lambda t, slot: (0, 0))
    rows = count_ops * 2 * count_ev
    near_courses = tuple(course for course in range(count_ops) if course != 0)
    left_rows = 2 * count_ev
    left_spec = pl.BlockSpec((1, left_rows, 6 * sites), lambda t, slot: (t, 0, 0))
    first_spec = pltpu.PrefetchScalarGridSpec(
        num_scalar_prefetch=1,
        grid=(time_count,),
        in_specs=[field_spec, field_spec, link_spec, trig_spec],
        out_specs=[pl.BlockSpec((1, rows, count_ev), lambda t, slot: (t, 0, 0)), left_spec],
    )
    partial, left = pl.pallas_call(
        functools.partial(sums_kernel, scale=scale, course_list=near_courses),
        grid_spec=first_spec,
        out_shape=(
            jax.ShapeDtypeStruct((time_count, rows, count_ev), jnp.bfloat16),
            jax.ShapeDtypeStruct((time_count, left_rows, 6 * sites), jnp.bfloat16),
        ),
    )(slot_of, eigenvectors, row_wide, gauge_links, trig)
    chunks = []
    for first, far_part in far_tile:
        span = far_part.shape[0]
        second_spec = pltpu.PrefetchScalarGridSpec(
            num_scalar_prefetch=1,
            grid=(span,),
            in_specs=[
                pl.BlockSpec(memory_space=pl.ANY),
                pl.BlockSpec((1, 2, 3, count_ev, sites), lambda t, slot: (t, 0, 0, 0, 0)),
                pl.BlockSpec((1,) + gauge_links.shape[1:], lambda t, slot, first=first: (t + first, 0, 0, 0, 0, 0)),
                pl.BlockSpec((1, left_rows, 6 * sites), lambda t, slot, first=first: (t + first, 0, 0)),
                pl.BlockSpec((1, rows, count_ev), lambda t, slot, first=first: (t + first, 0, 0)),
            ],
            out_specs=pl.BlockSpec((1, rows, count_ev), lambda t, slot: (t, 0, 0)),
        )
        chunks.append(
            pl.pallas_call(
                functools.partial(sums_kernel, scale=scale, course_list=(0,)),
                grid_spec=second_spec,
                out_shape=jax.ShapeDtypeStruct((span, rows, count_ev), jnp.bfloat16),
            )(slot_of, eigenvectors, far_part, gauge_links, left, partial)
        )
    return chunks


def panel_kernel(sink_ref, source_ref, stack_ref, wide_ref, out_ref):
    count_ev = sink_ref.shape[3]
    sink_real = sink_ref[0, 0, 0]
    sink_imag = sink_ref[0, 0, 1]
    sink_wide = jnp.concatenate(
        [
            jnp.concatenate([sink_real, -sink_imag], axis=1),
            jnp.concatenate([sink_imag, sink_real], axis=1),
        ],
        axis=0,
    )
    left = jnp.dot(sink_wide, stack_ref[...], preferred_element_type=jnp.float32)
    source_stack = jnp.concatenate([source_ref[0, 0, 0], source_ref[0, 0, 1]], axis=0)
    right = jnp.dot(wide_ref[...], source_stack, preferred_element_type=jnp.float32)
    total_real = 0.0
    total_imag = 0.0
    half = NSPIN * count_ev
    for spin in range(NSPIN):
        left_real = left[:count_ev, spin * count_ev : (spin + 1) * count_ev]
        left_imag = left[count_ev:, spin * count_ev : (spin + 1) * count_ev]
        right_real = right[spin * count_ev : (spin + 1) * count_ev]
        right_imag = right[half + spin * count_ev : half + (spin + 1) * count_ev]
        total_real = total_real + left_real * right_real + left_imag * right_imag
        total_imag = total_imag + left_imag * right_real - left_real * right_imag
    out_ref[0, 0:1, :] = jnp.sum(total_real, axis=0, keepdims=True)
    out_ref[0, 1:2, :] = jnp.sum(total_imag, axis=0, keepdims=True)


def contract_panel(gathered, panel):
    count_ops, count_ev = gathered.shape[1], panel.shape[1]
    stack = panel.reshape(2 * count_ev, NSPIN * count_ev)
    blocks = panel.reshape(2, count_ev, NSPIN, count_ev).transpose(0, 2, 1, 3).reshape(2, NSPIN * count_ev, count_ev)
    wide = jnp.concatenate(
        [
            jnp.concatenate([blocks[0], -blocks[1]], axis=1),
            jnp.concatenate([blocks[1], blocks[0]], axis=1),
        ],
        axis=0,
    )
    sums = pl.pallas_call(
        panel_kernel,
        grid=(count_ops,),
        in_specs=[
            pl.BlockSpec((1, 1, 2, count_ev, count_ev), lambda a: (0, a, 0, 0, 0)),
            pl.BlockSpec((1, 1, 2, count_ev, count_ev), lambda a: (1, a, 0, 0, 0)),
            pl.BlockSpec(stack.shape, lambda a: (0, 0)),
            pl.BlockSpec(wide.shape, lambda a: (0, 0)),
        ],
        out_specs=pl.BlockSpec((1, 2, count_ev), lambda a: (a, 0, 0)),
        out_shape=jax.ShapeDtypeStruct((count_ops, 2, count_ev), jnp.float32),
    )(gathered, gathered, stack, wide)
    return jnp.sum(sums, axis=-1) * (1.0 / (16.0 * count_ev))


def body(eigenvectors, gauge_links, perambulators, directions, momenta, pair_times):
    time_count = eigenvectors.shape[0]
    count_ev = eigenvectors.shape[3]
    local_sites = eigenvectors.shape[4]
    count_slabs = lax.axis_size("slab")
    nspace = NSPIN * count_slabs
    member = lax.axis_index("member")
    device = lax.axis_index("slab") * NSPIN + member
    half_rows = LY // 2
    extent_x = nspace // 2
    column = jnp.arange(local_sites, dtype=jnp.int32)
    coord_x = device // 2 + 0 * column
    coord_y = device % 2 * half_rows + column // LZ
    coord_z = column % LZ
    angle = phase_angles(momenta, (coord_x, coord_y, coord_z), (extent_x, LY, LZ))[0]
    halves = 3 if time_count % 3 == 0 else (2 if time_count % 2 == 0 else 1)
    span = time_count // halves
    far_tile = [(h * span, shifted(eigenvectors[h * span : (h + 1) * span], SPACE, -2)) for h in range(halves)]
    row_in = swapped(eigenvectors[..., :LZ], SPACE, 0)
    scale = 1.0 / math.sqrt(3.0 * extent_x * LY * LZ)
    partial_chunks = local_sums(eigenvectors, gauge_links, far_tile, row_in, directions, angle, scale)
    partial = jnp.concatenate(partial_chunks, 0)
    rows = partial.shape[1] // nspace
    if count_slabs <= 8:
        slab = lax.axis_index("slab")
        core = member % 2
        side = member // 2
        own_parts = []
        for half in range(halves):
            part_blocks = partial_chunks[half].reshape(span, count_slabs, 2, 2, rows, count_ev)
            keep = lax.dynamic_index_in_dim(part_blocks, core, 3, keepdims=False).astype(jnp.float32)
            send = lax.dynamic_index_in_dim(part_blocks, 1 - core, 3, keepdims=False)
            chunk = keep + swapped(send, "member", 0).astype(jnp.float32)
            keep = lax.dynamic_index_in_dim(chunk, side, 2, keepdims=False)
            send = lax.dynamic_index_in_dim(chunk, 1 - side, 2, keepdims=False).astype(jnp.bfloat16)
            slab_sum = keep + swapped(send, "member", 1).astype(jnp.float32)
            slab_part = slab_sum.astype(jnp.bfloat16)
            total = lax.dynamic_index_in_dim(slab_sum, slab, 1, keepdims=False)
            for shift in range(1, count_slabs):
                piece = lax.dynamic_index_in_dim(slab_part, (slab + shift) % count_slabs, 1, keepdims=False)
                total = total + shifted(piece, "slab", shift).astype(jnp.float32)
            own_parts.append(total.astype(jnp.bfloat16))
        own_rows = jnp.concatenate(own_parts, 0)
    else:
        own_rows = lax.psum_scatter(partial, SPACE, scatter_dimension=1, tiled=True)
    slabs = jnp.arange(count_slabs, dtype=jnp.int32)
    wanted = jnp.stack([pair_times[slabs, 1], pair_times[slabs, 0]], 1)
    outgoing = jnp.take(own_rows, wanted.reshape(-1), axis=0).reshape(count_slabs, 2, rows, count_ev)
    if count_slabs <= 8:
        pieces = [jnp.take(outgoing, (slab + shift) % count_slabs, axis=0) for shift in range(count_slabs)]
        arrived = [pieces[0]] + [shifted(pieces[shift], "slab", shift) for shift in range(1, count_slabs)]
        arrived = jnp.stack(arrived, 0)
        across = jnp.take(arrived, (slab - jnp.arange(count_slabs, dtype=jnp.int32)) % count_slabs, axis=0)
    else:
        across = lax.all_to_all(outgoing, "slab", 0, 0, tiled=True)
    shared = [across] + [shifted(across, "member", shift) for shift in range(1, NSPIN)]
    shared = jnp.stack(shared, 0)
    within = jnp.take(shared, (member - jnp.arange(NSPIN, dtype=jnp.int32)) % NSPIN, axis=0)
    incoming = within.transpose(1, 0, 2, 3, 4).reshape(nspace, 2, rows, count_ev)
    count_ops = partial.shape[1] // (2 * count_ev)
    gathered = incoming.transpose(1, 0, 2, 3).reshape(2, count_ops, 2, count_ev, count_ev)
    correlators = contract_panel(gathered, perambulators[0])[None]
    return (own_rows, correlators)


def solution(mesh):
    count_cfg = mesh.shape["cfg"]
    count_slabs = mesh.shape["space"] // NSPIN
    split = Mesh(mesh.devices.reshape(count_cfg, count_slabs, NSPIN), ("cfg",) + SPACE)
    placed = (
        P("cfg", None, None, None, SPACE),
        P("cfg", None, None, None, None, SPACE),
        P(("cfg",) + SPACE, None, None, None),
        P(),
        P(),
        P(),
    )
    return jax.shard_map(
        body,
        mesh=split,
        in_specs=placed,
        out_specs=(P("cfg", SPACE, None), P(("cfg",) + SPACE, None, None)),
        check_vma=False,
    )
```

```python
import functools
import math

import jax
import jax.numpy as jnp
from jax import lax
from jax.experimental import pallas as pl
from jax.experimental.pallas import tpu as pltpu
from jax.sharding import Mesh, PartitionSpec as P

NSPIN = 4
LY = 32
LZ = 8
SPACE = ("slab", "member")


def shifted(block, axis, distance):
    devices = range(lax.axis_size(axis))
    route = [((i - distance) % len(devices), i) for i in devices]
    return lax.ppermute(block, axis, route)


def swapped(value, axis, bit):
    return lax.ppermute(value, axis, [(i, i ^ 1 << bit) for i in range(lax.axis_size(axis))])


def phase_angles(momenta, coords, extents):
    fraction = 0.0
    for course in range(3):
        turns = momenta[:, course : course + 1] * coords[course][None, :] % extents[course]
        fraction = fraction + turns.astype(jnp.float32) / extents[course]
    return 2.0 * math.pi * fraction


def sums_kernel(slot_ref, field_ref, near_ref, link_ref, trig_ref, *rest, scale, course_list):
    out_ref = rest[-1] if len(course_list) == 1 else rest[0]
    count_ev, sites = field_ref.shape[3], field_ref.shape[4]
    lane = lax.broadcasted_iota(jnp.int32, (count_ev, sites), 1)
    last_z = lane % LZ == LZ - 1
    last_row = lane >= sites - LZ
    if len(course_list) == 1:
        left = trig_ref[0]
    else:
        cosine = trig_ref[0:1, :]
        sine_part = trig_ref[1:2, :]
        here = [[field_ref[0, part, colour].astype(jnp.float32) for colour in range(3)] for part in range(2)]
        phased_real = [(cosine * here[0][c] - sine_part * here[1][c]).astype(jnp.bfloat16) for c in range(3)]
        phased_imag = [(sine_part * here[0][c] + cosine * here[1][c]).astype(jnp.bfloat16) for c in range(3)]
        real_rows = jnp.concatenate(phased_real + phased_imag, axis=1)
        imag_rows = jnp.concatenate([-v for v in phased_imag] + phased_real, axis=1)
        left = jnp.concatenate([real_rows, imag_rows], axis=0)
        rest[1][0] = left
    rows = 2 * count_ev
    for course in course_list:
        if course == 0:
            near = [[near_ref[0, part, colour].astype(jnp.float32) for colour in range(3)] for part in range(2)]
        elif course == 1:
            near = [
                [
                    jnp.where(last_row, near_ref[0, part, colour].astype(jnp.float32), pltpu.roll(here[part][colour], sites - LZ, 1))
                    for colour in range(3)
                ]
                for part in range(2)
            ]
        else:
            near = [
                [
                    jnp.where(last_z, pltpu.roll(here[part][colour], LZ - 1, 1), pltpu.roll(here[part][colour], sites - 1, 1))
                    for colour in range(3)
                ]
                for part in range(2)
            ]
        moved_real = []
        moved_imag = []
        for outer in range(3):
            real_part = 0.0
            imag_part = 0.0
            for inner in range(3):
                link_real = link_ref[0, course, 0, outer, inner : inner + 1, :]
                link_imag = link_ref[0, course, 1, outer, inner : inner + 1, :]
                real_part = real_part + link_real * near[0][inner] - link_imag * near[1][inner]
                imag_part = imag_part + link_real * near[1][inner] + link_imag * near[0][inner]
            moved_real.append(real_part.astype(jnp.bfloat16))
            moved_imag.append(imag_part.astype(jnp.bfloat16))
        right = jnp.concatenate(moved_real + moved_imag, axis=1)
        joined = lax.dot_general(left, right, (((1,), (1,)), ((), ())), preferred_element_type=jnp.float32)
        if len(course_list) == 1:
            out_ref[0] = rest[0][0]
            start = pl.multiple_of(slot_ref[course] * rows, rows)
            out_ref[0, pl.ds(start, rows), :] = (joined * scale).astype(out_ref.dtype)
        else:
            start = pl.multiple_of(slot_ref[course] * rows, rows)
            out_ref[0, pl.ds(start, rows), :] = (joined * scale).astype(out_ref.dtype)


def local_sums(eigenvectors, gauge_links, row_in, directions, angle, scale):
    time_count, _, _, count_ev, sites = eigenvectors.shape
    count_ops = directions.shape[0]
    slot_of = jnp.sum(
        (directions[None, :] == jnp.arange(count_ops, dtype=jnp.int32)[:, None]) * jnp.arange(count_ops, dtype=jnp.int32)[None, :],
        axis=1,
    ).astype(jnp.int32)
    row_wide = jnp.pad(row_in, ((0, 0),) * 4 + ((sites - LZ, 0),))
    trig = jnp.stack([jnp.cos(angle), jnp.sin(angle)], 0)
    field_spec = pl.BlockSpec((1, 2, 3, count_ev, sites), lambda t, slot: (t, 0, 0, 0, 0))
    link_spec = pl.BlockSpec((1,) + gauge_links.shape[1:], lambda t, slot: (t, 0, 0, 0, 0, 0))
    trig_spec = pl.BlockSpec(trig.shape, lambda t, slot: (0, 0))
    rows = count_ops * 2 * count_ev
    near_courses = tuple(course for course in range(count_ops) if course != 0)
    left_rows = 2 * count_ev
    left_spec = pl.BlockSpec((1, left_rows, 6 * sites), lambda t, slot: (t, 0, 0))
    first_spec = pltpu.PrefetchScalarGridSpec(
        num_scalar_prefetch=1,
        grid=(time_count,),
        in_specs=[field_spec, field_spec, link_spec, trig_spec],
        out_specs=[pl.BlockSpec((1, rows, count_ev), lambda t, slot: (t, 0, 0)), left_spec],
    )
    partial, left = pl.pallas_call(
        functools.partial(sums_kernel, scale=scale, course_list=near_courses),
        grid_spec=first_spec,
        out_shape=(
            jax.ShapeDtypeStruct((time_count, rows, count_ev), jnp.bfloat16),
            jax.ShapeDtypeStruct((time_count, left_rows, 6 * sites), jnp.bfloat16),
        ),
    )(slot_of, eigenvectors, row_wide, gauge_links, trig)
    return slot_of, left, partial


def second_pass(slot_of, eigenvectors, gauge_links, left, partial, first, far_part, scale):
    count_ev, sites = eigenvectors.shape[3], eigenvectors.shape[4]
    rows = partial.shape[1]
    left_rows = left.shape[1]
    if True:
        span = far_part.shape[0]
        second_spec = pltpu.PrefetchScalarGridSpec(
            num_scalar_prefetch=1,
            grid=(span,),
            in_specs=[
                pl.BlockSpec(memory_space=pl.ANY),
                pl.BlockSpec((1, 2, 3, count_ev, sites), lambda t, slot: (t, 0, 0, 0, 0)),
                pl.BlockSpec((1,) + gauge_links.shape[1:], lambda t, slot, first=first: (t + first, 0, 0, 0, 0, 0)),
                pl.BlockSpec((1, left_rows, 6 * sites), lambda t, slot, first=first: (t + first, 0, 0)),
                pl.BlockSpec((1, rows, count_ev), lambda t, slot, first=first: (t + first, 0, 0)),
            ],
            out_specs=pl.BlockSpec((1, rows, count_ev), lambda t, slot: (t, 0, 0)),
        )
        return pl.pallas_call(
            functools.partial(sums_kernel, scale=scale, course_list=(0,)),
            grid_spec=second_spec,
            out_shape=jax.ShapeDtypeStruct((span, rows, count_ev), jnp.bfloat16),
        )(slot_of, eigenvectors, far_part, gauge_links, left, partial)


def panel_kernel(sink_ref, source_ref, stack_ref, wide_ref, out_ref):
    count_ev = sink_ref.shape[3]
    sink_real = sink_ref[0, 0, 0]
    sink_imag = sink_ref[0, 0, 1]
    sink_wide = jnp.concatenate(
        [
            jnp.concatenate([sink_real, -sink_imag], axis=1),
            jnp.concatenate([sink_imag, sink_real], axis=1),
        ],
        axis=0,
    )
    left = jnp.dot(sink_wide, stack_ref[...], preferred_element_type=jnp.float32)
    source_stack = jnp.concatenate([source_ref[0, 0, 0], source_ref[0, 0, 1]], axis=0)
    right = jnp.dot(wide_ref[...], source_stack, preferred_element_type=jnp.float32)
    total_real = 0.0
    total_imag = 0.0
    half = NSPIN * count_ev
    for spin in range(NSPIN):
        left_real = left[:count_ev, spin * count_ev : (spin + 1) * count_ev]
        left_imag = left[count_ev:, spin * count_ev : (spin + 1) * count_ev]
        right_real = right[spin * count_ev : (spin + 1) * count_ev]
        right_imag = right[half + spin * count_ev : half + (spin + 1) * count_ev]
        total_real = total_real + left_real * right_real + left_imag * right_imag
        total_imag = total_imag + left_imag * right_real - left_real * right_imag
    out_ref[0, 0:1, :] = jnp.sum(total_real, axis=0, keepdims=True)
    out_ref[0, 1:2, :] = jnp.sum(total_imag, axis=0, keepdims=True)


def contract_panel(gathered, panel):
    count_ops, count_ev = gathered.shape[1], panel.shape[1]
    stack = panel.reshape(2 * count_ev, NSPIN * count_ev)
    blocks = panel.reshape(2, count_ev, NSPIN, count_ev).transpose(0, 2, 1, 3).reshape(2, NSPIN * count_ev, count_ev)
    wide = jnp.concatenate(
        [
            jnp.concatenate([blocks[0], -blocks[1]], axis=1),
            jnp.concatenate([blocks[1], blocks[0]], axis=1),
        ],
        axis=0,
    )
    sums = pl.pallas_call(
        panel_kernel,
        grid=(count_ops,),
        in_specs=[
            pl.BlockSpec((1, 1, 2, count_ev, count_ev), lambda a: (0, a, 0, 0, 0)),
            pl.BlockSpec((1, 1, 2, count_ev, count_ev), lambda a: (1, a, 0, 0, 0)),
            pl.BlockSpec(stack.shape, lambda a: (0, 0)),
            pl.BlockSpec(wide.shape, lambda a: (0, 0)),
        ],
        out_specs=pl.BlockSpec((1, 2, count_ev), lambda a: (a, 0, 0)),
        out_shape=jax.ShapeDtypeStruct((count_ops, 2, count_ev), jnp.float32),
    )(gathered, gathered, stack, wide)
    return jnp.sum(sums, axis=-1) * (1.0 / (16.0 * count_ev))


def body(eigenvectors, gauge_links, perambulators, directions, momenta, pair_times):
    time_count = eigenvectors.shape[0]
    count_ev = eigenvectors.shape[3]
    local_sites = eigenvectors.shape[4]
    count_slabs = lax.axis_size("slab")
    nspace = NSPIN * count_slabs
    member = lax.axis_index("member")
    device = lax.axis_index("slab") * NSPIN + member
    half_rows = LY // 2
    extent_x = nspace // 2
    column = jnp.arange(local_sites, dtype=jnp.int32)
    coord_x = device // 2 + 0 * column
    coord_y = device % 2 * half_rows + column // LZ
    coord_z = column % LZ
    angle = phase_angles(momenta, (coord_x, coord_y, coord_z), (extent_x, LY, LZ))[0]
    halves = 3 if time_count % 3 == 0 else (2 if time_count % 2 == 0 else 1)
    span = time_count // halves
    far_tile = [(h * span, shifted(eigenvectors[h * span : (h + 1) * span], SPACE, -2)) for h in range(halves)]
    row_in = swapped(eigenvectors[..., :LZ], SPACE, 0)
    scale = 1.0 / math.sqrt(3.0 * extent_x * LY * LZ)
    slot_of, left, first_partial = local_sums(eigenvectors, gauge_links, row_in, directions, angle, scale)
    partial_chunks = []
    core = member % 2
    swapped_chunks = []
    for half in range(halves):
        first, far_part = far_tile[half]
        if swapped_chunks:
            far_part = lax.optimization_barrier((far_part, swapped_chunks[-1]))[0]
        chunk_partial = second_pass(slot_of, eigenvectors, gauge_links, left, first_partial, first, far_part, scale)
        partial_chunks.append(chunk_partial)
        if count_slabs <= 8:
            part_blocks = chunk_partial.reshape(span, count_slabs, 2, 2, -1, count_ev)
            send = lax.dynamic_index_in_dim(part_blocks, 1 - core, 3, keepdims=False)
            swapped_chunks.append(swapped(send, "member", 0))
    partial = jnp.concatenate(partial_chunks, 0)
    rows = partial.shape[1] // nspace
    if count_slabs <= 8:
        slab = lax.axis_index("slab")
        side = member // 2
        own_parts = []
        for half in range(halves):
            part_blocks = partial_chunks[half].reshape(span, count_slabs, 2, 2, rows, count_ev)
            keep = lax.dynamic_index_in_dim(part_blocks, core, 3, keepdims=False).astype(jnp.float32)
            chunk = keep + swapped_chunks[half].astype(jnp.float32)
            keep = lax.dynamic_index_in_dim(chunk, side, 2, keepdims=False)
            send = lax.dynamic_index_in_dim(chunk, 1 - side, 2, keepdims=False).astype(jnp.bfloat16)
            slab_sum = keep + swapped(send, "member", 1).astype(jnp.float32)
            slab_part = slab_sum.astype(jnp.bfloat16)
            total = lax.dynamic_index_in_dim(slab_sum, slab, 1, keepdims=False)
            for shift in range(1, count_slabs):
                piece = lax.dynamic_index_in_dim(slab_part, (slab + shift) % count_slabs, 1, keepdims=False)
                total = total + shifted(piece, "slab", shift).astype(jnp.float32)
            own_parts.append(total.astype(jnp.bfloat16))
        own_rows = jnp.concatenate(own_parts, 0)
    else:
        own_rows = lax.psum_scatter(partial, SPACE, scatter_dimension=1, tiled=True)
    slabs = jnp.arange(count_slabs, dtype=jnp.int32)
    wanted = jnp.stack([pair_times[slabs, 1], pair_times[slabs, 0]], 1)
    outgoing = jnp.take(own_rows, wanted.reshape(-1), axis=0).reshape(count_slabs, 2, rows, count_ev)
    if count_slabs <= 8:
        pieces = [jnp.take(outgoing, (slab + shift) % count_slabs, axis=0) for shift in range(count_slabs)]
        arrived = [pieces[0]] + [shifted(pieces[shift], "slab", shift) for shift in range(1, count_slabs)]
        arrived = jnp.stack(arrived, 0)
        across = jnp.take(arrived, (slab - jnp.arange(count_slabs, dtype=jnp.int32)) % count_slabs, axis=0)
    else:
        across = lax.all_to_all(outgoing, "slab", 0, 0, tiled=True)
    shared = [across] + [shifted(across, "member", shift) for shift in range(1, NSPIN)]
    shared = jnp.stack(shared, 0)
    within = jnp.take(shared, (member - jnp.arange(NSPIN, dtype=jnp.int32)) % NSPIN, axis=0)
    incoming = within.transpose(1, 0, 2, 3, 4).reshape(nspace, 2, rows, count_ev)
    count_ops = partial.shape[1] // (2 * count_ev)
    gathered = incoming.transpose(1, 0, 2, 3).reshape(2, count_ops, 2, count_ev, count_ev)
    correlators = contract_panel(gathered, perambulators[0])[None]
    return (own_rows, correlators)


def solution(mesh):
    count_cfg = mesh.shape["cfg"]
    count_slabs = mesh.shape["space"] // NSPIN
    split = Mesh(mesh.devices.reshape(count_cfg, count_slabs, NSPIN), ("cfg",) + SPACE)
    placed = (
        P("cfg", None, None, None, SPACE),
        P("cfg", None, None, None, None, SPACE),
        P(("cfg",) + SPACE, None, None, None),
        P(),
        P(),
        P(),
    )
    return jax.shard_map(
        body,
        mesh=split,
        in_specs=placed,
        out_specs=(P("cfg", SPACE, None), P(("cfg",) + SPACE, None, None)),
        check_vma=False,
    )
```

```python
import functools
import math

import jax
import jax.numpy as jnp
from jax import lax
from jax.experimental import pallas as pl
from jax.experimental.pallas import tpu as pltpu
from jax.sharding import Mesh, PartitionSpec as P

NSPIN = 4
LY = 32
LZ = 8
SPACE = ("slab", "member")


def shifted(block, axis, distance):
    devices = range(lax.axis_size(axis))
    route = [((i - distance) % len(devices), i) for i in devices]
    return lax.ppermute(block, axis, route)


def swapped(value, axis, bit):
    return lax.ppermute(value, axis, [(i, i ^ 1 << bit) for i in range(lax.axis_size(axis))])


def phase_angles(momenta, coords, extents):
    fraction = 0.0
    for course in range(3):
        turns = momenta[:, course : course + 1] * coords[course][None, :] % extents[course]
        fraction = fraction + turns.astype(jnp.float32) / extents[course]
    return 2.0 * math.pi * fraction


def sums_kernel(slot_ref, field_ref, near_ref, link_ref, trig_ref, *rest, scale, course_list):
    out_ref = rest[-1] if len(course_list) == 1 else rest[0]
    count_ev, sites = field_ref.shape[3], field_ref.shape[4]
    lane = lax.broadcasted_iota(jnp.int32, (count_ev, sites), 1)
    last_z = lane % LZ == LZ - 1
    last_row = lane >= sites - LZ
    if len(course_list) == 1:
        left = trig_ref[0]
    else:
        cosine = trig_ref[0:1, :]
        sine_part = trig_ref[1:2, :]
        here = [[field_ref[0, part, colour].astype(jnp.float32) for colour in range(3)] for part in range(2)]
        phased_real = [(cosine * here[0][c] - sine_part * here[1][c]).astype(jnp.bfloat16) for c in range(3)]
        phased_imag = [(sine_part * here[0][c] + cosine * here[1][c]).astype(jnp.bfloat16) for c in range(3)]
        real_rows = jnp.concatenate(phased_real + phased_imag, axis=1)
        imag_rows = jnp.concatenate([-v for v in phased_imag] + phased_real, axis=1)
        left = jnp.concatenate([real_rows, imag_rows], axis=0)
        rest[1][0] = left
    rows = 2 * count_ev
    for course in course_list:
        if course == 0:
            near = [[near_ref[0, part, colour].astype(jnp.float32) for colour in range(3)] for part in range(2)]
        elif course == 1:
            near = [
                [
                    jnp.where(last_row, near_ref[0, part, colour].astype(jnp.float32), pltpu.roll(here[part][colour], sites - LZ, 1))
                    for colour in range(3)
                ]
                for part in range(2)
            ]
        else:
            near = [
                [
                    jnp.where(last_z, pltpu.roll(here[part][colour], LZ - 1, 1), pltpu.roll(here[part][colour], sites - 1, 1))
                    for colour in range(3)
                ]
                for part in range(2)
            ]
        moved_real = []
        moved_imag = []
        for outer in range(3):
            real_part = 0.0
            imag_part = 0.0
            for inner in range(3):
                link_real = link_ref[0, course, 0, outer, inner : inner + 1, :]
                link_imag = link_ref[0, course, 1, outer, inner : inner + 1, :]
                real_part = real_part + link_real * near[0][inner] - link_imag * near[1][inner]
                imag_part = imag_part + link_real * near[1][inner] + link_imag * near[0][inner]
            moved_real.append(real_part.astype(jnp.bfloat16))
            moved_imag.append(imag_part.astype(jnp.bfloat16))
        right = jnp.concatenate(moved_real + moved_imag, axis=1)
        joined = lax.dot_general(left, right, (((1,), (1,)), ((), ())), preferred_element_type=jnp.float32)
        if len(course_list) == 1:
            out_ref[0] = rest[0][0]
            start = pl.multiple_of(slot_ref[course] * rows, rows)
            out_ref[0, pl.ds(start, rows), :] = (joined * scale).astype(out_ref.dtype)
        else:
            start = pl.multiple_of(slot_ref[course] * rows, rows)
            out_ref[0, pl.ds(start, rows), :] = (joined * scale).astype(out_ref.dtype)


def local_sums(eigenvectors, gauge_links, row_in, directions, angle, scale):
    time_count, _, _, count_ev, sites = eigenvectors.shape
    count_ops = directions.shape[0]
    slot_of = jnp.sum(
        (directions[None, :] == jnp.arange(count_ops, dtype=jnp.int32)[:, None]) * jnp.arange(count_ops, dtype=jnp.int32)[None, :],
        axis=1,
    ).astype(jnp.int32)
    row_wide = jnp.pad(row_in, ((0, 0),) * 4 + ((sites - LZ, 0),))
    trig = jnp.stack([jnp.cos(angle), jnp.sin(angle)], 0)
    field_spec = pl.BlockSpec((1, 2, 3, count_ev, sites), lambda t, slot: (t, 0, 0, 0, 0))
    link_spec = pl.BlockSpec((1,) + gauge_links.shape[1:], lambda t, slot: (t, 0, 0, 0, 0, 0))
    trig_spec = pl.BlockSpec(trig.shape, lambda t, slot: (0, 0))
    rows = count_ops * 2 * count_ev
    near_courses = tuple(course for course in range(count_ops) if course != 0)
    left_rows = 2 * count_ev
    left_spec = pl.BlockSpec((1, left_rows, 6 * sites), lambda t, slot: (t, 0, 0))
    first_spec = pltpu.PrefetchScalarGridSpec(
        num_scalar_prefetch=1,
        grid=(time_count,),
        in_specs=[field_spec, field_spec, link_spec, trig_spec],
        out_specs=[pl.BlockSpec((1, rows, count_ev), lambda t, slot: (t, 0, 0)), left_spec],
    )
    partial, left = pl.pallas_call(
        functools.partial(sums_kernel, scale=scale, course_list=near_courses),
        grid_spec=first_spec,
        out_shape=(
            jax.ShapeDtypeStruct((time_count, rows, count_ev), jnp.bfloat16),
            jax.ShapeDtypeStruct((time_count, left_rows, 6 * sites), jnp.bfloat16),
        ),
    )(slot_of, eigenvectors, row_wide, gauge_links, trig)
    return slot_of, left, partial


def second_pass(slot_of, eigenvectors, gauge_links, left, partial, first, far_part, scale):
    count_ev, sites = eigenvectors.shape[3], eigenvectors.shape[4]
    rows = partial.shape[1]
    left_rows = left.shape[1]
    if True:
        span = far_part.shape[0]
        second_spec = pltpu.PrefetchScalarGridSpec(
            num_scalar_prefetch=1,
            grid=(span,),
            in_specs=[
                pl.BlockSpec(memory_space=pl.ANY),
                pl.BlockSpec((1, 2, 3, count_ev, sites), lambda t, slot: (t, 0, 0, 0, 0)),
                pl.BlockSpec((1,) + gauge_links.shape[1:], lambda t, slot, first=first: (t + first, 0, 0, 0, 0, 0)),
                pl.BlockSpec((1, left_rows, 6 * sites), lambda t, slot, first=first: (t + first, 0, 0)),
                pl.BlockSpec((1, rows, count_ev), lambda t, slot, first=first: (t + first, 0, 0)),
            ],
            out_specs=pl.BlockSpec((1, rows, count_ev), lambda t, slot: (t, 0, 0)),
        )
        return pl.pallas_call(
            functools.partial(sums_kernel, scale=scale, course_list=(0,)),
            grid_spec=second_spec,
            out_shape=jax.ShapeDtypeStruct((span, rows, count_ev), jnp.bfloat16),
        )(slot_of, eigenvectors, far_part, gauge_links, left, partial)


def panel_kernel(sink_ref, source_ref, stack_ref, wide_ref, out_ref):
    count_ev = sink_ref.shape[3]
    sink_real = sink_ref[0, 0, 0]
    sink_imag = sink_ref[0, 0, 1]
    sink_wide = jnp.concatenate(
        [
            jnp.concatenate([sink_real, -sink_imag], axis=1),
            jnp.concatenate([sink_imag, sink_real], axis=1),
        ],
        axis=0,
    )
    left = jnp.dot(sink_wide, stack_ref[...], preferred_element_type=jnp.float32)
    source_stack = jnp.concatenate([source_ref[0, 0, 0], source_ref[0, 0, 1]], axis=0)
    right = jnp.dot(wide_ref[...], source_stack, preferred_element_type=jnp.float32)
    total_real = 0.0
    total_imag = 0.0
    half = NSPIN * count_ev
    for spin in range(NSPIN):
        left_real = left[:count_ev, spin * count_ev : (spin + 1) * count_ev]
        left_imag = left[count_ev:, spin * count_ev : (spin + 1) * count_ev]
        right_real = right[spin * count_ev : (spin + 1) * count_ev]
        right_imag = right[half + spin * count_ev : half + (spin + 1) * count_ev]
        total_real = total_real + left_real * right_real + left_imag * right_imag
        total_imag = total_imag + left_imag * right_real - left_real * right_imag
    out_ref[0, 0:1, :] = jnp.sum(total_real, axis=0, keepdims=True)
    out_ref[0, 1:2, :] = jnp.sum(total_imag, axis=0, keepdims=True)


def contract_panel(gathered, panel):
    count_ops, count_ev = gathered.shape[1], panel.shape[1]
    stack = panel.reshape(2 * count_ev, NSPIN * count_ev)
    blocks = panel.reshape(2, count_ev, NSPIN, count_ev).transpose(0, 2, 1, 3).reshape(2, NSPIN * count_ev, count_ev)
    wide = jnp.concatenate(
        [
            jnp.concatenate([blocks[0], -blocks[1]], axis=1),
            jnp.concatenate([blocks[1], blocks[0]], axis=1),
        ],
        axis=0,
    )
    sums = pl.pallas_call(
        panel_kernel,
        grid=(count_ops,),
        in_specs=[
            pl.BlockSpec((1, 1, 2, count_ev, count_ev), lambda a: (0, a, 0, 0, 0)),
            pl.BlockSpec((1, 1, 2, count_ev, count_ev), lambda a: (1, a, 0, 0, 0)),
            pl.BlockSpec(stack.shape, lambda a: (0, 0)),
            pl.BlockSpec(wide.shape, lambda a: (0, 0)),
        ],
        out_specs=pl.BlockSpec((1, 2, count_ev), lambda a: (a, 0, 0)),
        out_shape=jax.ShapeDtypeStruct((count_ops, 2, count_ev), jnp.float32),
    )(gathered, gathered, stack, wide)
    return jnp.sum(sums, axis=-1) * (1.0 / (16.0 * count_ev))


def body(eigenvectors, gauge_links, perambulators, directions, momenta, pair_times):
    time_count = eigenvectors.shape[0]
    count_ev = eigenvectors.shape[3]
    local_sites = eigenvectors.shape[4]
    count_slabs = lax.axis_size("slab")
    nspace = NSPIN * count_slabs
    member = lax.axis_index("member")
    device = lax.axis_index("slab") * NSPIN + member
    half_rows = LY // 2
    extent_x = nspace // 2
    column = jnp.arange(local_sites, dtype=jnp.int32)
    coord_x = device // 2 + 0 * column
    coord_y = device % 2 * half_rows + column // LZ
    coord_z = column % LZ
    angle = phase_angles(momenta, (coord_x, coord_y, coord_z), (extent_x, LY, LZ))[0]
    halves = 3 if time_count % 3 == 0 else (2 if time_count % 2 == 0 else 1)
    span = time_count // halves
    far_tile = [(h * span, shifted(eigenvectors[h * span : (h + 1) * span], SPACE, -2)) for h in range(halves)]
    row_in = swapped(eigenvectors[..., :LZ], SPACE, 0)
    scale = 1.0 / math.sqrt(3.0 * extent_x * LY * LZ)
    slot_of, left, first_partial = local_sums(eigenvectors, gauge_links, row_in, directions, angle, scale)
    partial_chunks = []
    core = member % 2
    side = member // 2
    swapped_chunks = []
    chunk_sums = []
    side_chunks = []
    for half in range(halves):
        first, far_part = far_tile[half]
        ties = []
        if half >= 1 and swapped_chunks:
            ties.append(swapped_chunks[half - 1])
        if half >= 2 and side_chunks:
            ties.append(side_chunks[half - 2])
        if ties:
            far_part = lax.optimization_barrier((far_part,) + tuple(ties))[0]
        chunk_partial = second_pass(slot_of, eigenvectors, gauge_links, left, first_partial, first, far_part, scale)
        partial_chunks.append(chunk_partial)
        if count_slabs <= 8:
            part_blocks = chunk_partial.reshape(span, count_slabs, 2, 2, -1, count_ev)
            send = lax.dynamic_index_in_dim(part_blocks, 1 - core, 3, keepdims=False)
            received = swapped(send, "member", 0)
            swapped_chunks.append(received)
            keep = lax.dynamic_index_in_dim(part_blocks, core, 3, keepdims=False).astype(jnp.float32)
            chunk = keep + received.astype(jnp.float32)
            chunk_sums.append(chunk)
            send = lax.dynamic_index_in_dim(chunk, 1 - side, 2, keepdims=False).astype(jnp.bfloat16)
            side_chunks.append(swapped(send, "member", 1))
    partial = jnp.concatenate(partial_chunks, 0)
    rows = partial.shape[1] // nspace
    if count_slabs <= 8:
        slab = lax.axis_index("slab")
        own_parts = []
        for half in range(halves):
            keep = lax.dynamic_index_in_dim(chunk_sums[half], side, 2, keepdims=False)
            slab_sum = keep + side_chunks[half].astype(jnp.float32)
            slab_part = slab_sum.astype(jnp.bfloat16)
            total = lax.dynamic_index_in_dim(slab_sum, slab, 1, keepdims=False)
            for shift in range(1, count_slabs):
                piece = lax.dynamic_index_in_dim(slab_part, (slab + shift) % count_slabs, 1, keepdims=False)
                total = total + shifted(piece, "slab", shift).astype(jnp.float32)
            own_parts.append(total.astype(jnp.bfloat16))
        own_rows = jnp.concatenate(own_parts, 0)
    else:
        own_rows = lax.psum_scatter(partial, SPACE, scatter_dimension=1, tiled=True)
    slabs = jnp.arange(count_slabs, dtype=jnp.int32)
    wanted = jnp.stack([pair_times[slabs, 1], pair_times[slabs, 0]], 1)
    outgoing = jnp.take(own_rows, wanted.reshape(-1), axis=0).reshape(count_slabs, 2, rows, count_ev)
    if count_slabs <= 8:
        pieces = [jnp.take(outgoing, (slab + shift) % count_slabs, axis=0) for shift in range(count_slabs)]
        arrived = [pieces[0]] + [shifted(pieces[shift], "slab", shift) for shift in range(1, count_slabs)]
        arrived = jnp.stack(arrived, 0)
        across = jnp.take(arrived, (slab - jnp.arange(count_slabs, dtype=jnp.int32)) % count_slabs, axis=0)
    else:
        across = lax.all_to_all(outgoing, "slab", 0, 0, tiled=True)
    shared = [across] + [shifted(across, "member", shift) for shift in range(1, NSPIN)]
    shared = jnp.stack(shared, 0)
    within = jnp.take(shared, (member - jnp.arange(NSPIN, dtype=jnp.int32)) % NSPIN, axis=0)
    incoming = within.transpose(1, 0, 2, 3, 4).reshape(nspace, 2, rows, count_ev)
    count_ops = partial.shape[1] // (2 * count_ev)
    gathered = incoming.transpose(1, 0, 2, 3).reshape(2, count_ops, 2, count_ev, count_ev)
    correlators = contract_panel(gathered, perambulators[0])[None]
    return (own_rows, correlators)


def solution(mesh):
    count_cfg = mesh.shape["cfg"]
    count_slabs = mesh.shape["space"] // NSPIN
    split = Mesh(mesh.devices.reshape(count_cfg, count_slabs, NSPIN), ("cfg",) + SPACE)
    placed = (
        P("cfg", None, None, None, SPACE),
        P("cfg", None, None, None, None, SPACE),
        P(("cfg",) + SPACE, None, None, None),
        P(),
        P(),
        P(),
    )
    return jax.shard_map(
        body,
        mesh=split,
        in_specs=placed,
        out_specs=(P("cfg", SPACE, None), P(("cfg",) + SPACE, None, None)),
        check_vma=False,
    )
```

```python
import functools
import math

import jax
import jax.numpy as jnp
from jax import lax
from jax.experimental import pallas as pl
from jax.experimental.pallas import tpu as pltpu
from jax.sharding import Mesh, PartitionSpec as P

NSPIN = 4
LY = 32
LZ = 8
SPACE = ("slab", "member")


def shifted(block, axis, distance):
    devices = range(lax.axis_size(axis))
    route = [((i - distance) % len(devices), i) for i in devices]
    return lax.ppermute(block, axis, route)


def swapped(value, axis, bit):
    return lax.ppermute(value, axis, [(i, i ^ 1 << bit) for i in range(lax.axis_size(axis))])


def phase_angles(momenta, coords, extents):
    fraction = 0.0
    for course in range(3):
        turns = momenta[:, course : course + 1] * coords[course][None, :] % extents[course]
        fraction = fraction + turns.astype(jnp.float32) / extents[course]
    return 2.0 * math.pi * fraction


def sums_kernel(slot_ref, field_ref, near_ref, link_ref, trig_ref, *rest, scale, course_list):
    out_ref = rest[-1] if len(course_list) == 1 else rest[0]
    count_ev, sites = field_ref.shape[3], field_ref.shape[4]
    lane = lax.broadcasted_iota(jnp.int32, (count_ev, sites), 1)
    last_z = lane % LZ == LZ - 1
    last_row = lane >= sites - LZ
    if len(course_list) == 1:
        left = trig_ref[0]
    else:
        cosine = trig_ref[0:1, :]
        sine_part = trig_ref[1:2, :]
        here = [[field_ref[0, part, colour].astype(jnp.float32) for colour in range(3)] for part in range(2)]
        phased_real = [(cosine * here[0][c] - sine_part * here[1][c]).astype(jnp.bfloat16) for c in range(3)]
        phased_imag = [(sine_part * here[0][c] + cosine * here[1][c]).astype(jnp.bfloat16) for c in range(3)]
        real_rows = jnp.concatenate(phased_real + phased_imag, axis=1)
        imag_rows = jnp.concatenate([-v for v in phased_imag] + phased_real, axis=1)
        left = jnp.concatenate([real_rows, imag_rows], axis=0)
        rest[1][0] = left
    rows = 2 * count_ev
    for course in course_list:
        if course == 0:
            near = [[near_ref[0, part, colour].astype(jnp.float32) for colour in range(3)] for part in range(2)]
        elif course == 1:
            near = [
                [
                    jnp.where(last_row, near_ref[0, part, colour].astype(jnp.float32), pltpu.roll(here[part][colour], sites - LZ, 1))
                    for colour in range(3)
                ]
                for part in range(2)
            ]
        else:
            near = [
                [
                    jnp.where(last_z, pltpu.roll(here[part][colour], LZ - 1, 1), pltpu.roll(here[part][colour], sites - 1, 1))
                    for colour in range(3)
                ]
                for part in range(2)
            ]
        moved_real = []
        moved_imag = []
        for outer in range(3):
            real_part = 0.0
            imag_part = 0.0
            for inner in range(3):
                link_real = link_ref[0, course, 0, outer, inner : inner + 1, :]
                link_imag = link_ref[0, course, 1, outer, inner : inner + 1, :]
                real_part = real_part + link_real * near[0][inner] - link_imag * near[1][inner]
                imag_part = imag_part + link_real * near[1][inner] + link_imag * near[0][inner]
            moved_real.append(real_part.astype(jnp.bfloat16))
            moved_imag.append(imag_part.astype(jnp.bfloat16))
        right = jnp.concatenate(moved_real + moved_imag, axis=1)
        joined = lax.dot_general(left, right, (((1,), (1,)), ((), ())), preferred_element_type=jnp.float32)
        if len(course_list) == 1:
            out_ref[0] = rest[0][0]
            start = pl.multiple_of(slot_ref[course] * rows, rows)
            out_ref[0, pl.ds(start, rows), :] = (joined * scale).astype(out_ref.dtype)
        else:
            start = pl.multiple_of(slot_ref[course] * rows, rows)
            out_ref[0, pl.ds(start, rows), :] = (joined * scale).astype(out_ref.dtype)


def local_sums(eigenvectors, gauge_links, row_in, directions, angle, scale):
    time_count, _, _, count_ev, sites = eigenvectors.shape
    count_ops = directions.shape[0]
    slot_of = jnp.sum(
        (directions[None, :] == jnp.arange(count_ops, dtype=jnp.int32)[:, None]) * jnp.arange(count_ops, dtype=jnp.int32)[None, :],
        axis=1,
    ).astype(jnp.int32)
    row_wide = jnp.pad(row_in, ((0, 0),) * 4 + ((sites - LZ, 0),))
    trig = jnp.stack([jnp.cos(angle), jnp.sin(angle)], 0)
    field_spec = pl.BlockSpec((1, 2, 3, count_ev, sites), lambda t, slot: (t, 0, 0, 0, 0))
    link_spec = pl.BlockSpec((1,) + gauge_links.shape[1:], lambda t, slot: (t, 0, 0, 0, 0, 0))
    trig_spec = pl.BlockSpec(trig.shape, lambda t, slot: (0, 0))
    rows = count_ops * 2 * count_ev
    near_courses = tuple(course for course in range(count_ops) if course != 0)
    left_rows = 2 * count_ev
    left_spec = pl.BlockSpec((1, left_rows, 6 * sites), lambda t, slot: (t, 0, 0))
    first_spec = pltpu.PrefetchScalarGridSpec(
        num_scalar_prefetch=1,
        grid=(time_count,),
        in_specs=[field_spec, field_spec, link_spec, trig_spec],
        out_specs=[pl.BlockSpec((1, rows, count_ev), lambda t, slot: (t, 0, 0)), left_spec],
    )
    partial, left = pl.pallas_call(
        functools.partial(sums_kernel, scale=scale, course_list=near_courses),
        grid_spec=first_spec,
        out_shape=(
            jax.ShapeDtypeStruct((time_count, rows, count_ev), jnp.bfloat16),
            jax.ShapeDtypeStruct((time_count, left_rows, 6 * sites), jnp.bfloat16),
        ),
    )(slot_of, eigenvectors, row_wide, gauge_links, trig)
    return slot_of, left, partial


def second_pass(slot_of, eigenvectors, gauge_links, left, partial, first, far_part, scale):
    count_ev, sites = eigenvectors.shape[3], eigenvectors.shape[4]
    rows = partial.shape[1]
    left_rows = left.shape[1]
    if True:
        span = far_part.shape[0]
        second_spec = pltpu.PrefetchScalarGridSpec(
            num_scalar_prefetch=1,
            grid=(span,),
            in_specs=[
                pl.BlockSpec(memory_space=pl.ANY),
                pl.BlockSpec((1, 2, 3, count_ev, sites), lambda t, slot: (t, 0, 0, 0, 0)),
                pl.BlockSpec((1,) + gauge_links.shape[1:], lambda t, slot, first=first: (t + first, 0, 0, 0, 0, 0)),
                pl.BlockSpec((1, left_rows, 6 * sites), lambda t, slot, first=first: (t + first, 0, 0)),
                pl.BlockSpec((1, rows, count_ev), lambda t, slot, first=first: (t + first, 0, 0)),
            ],
            out_specs=pl.BlockSpec((1, rows, count_ev), lambda t, slot: (t, 0, 0)),
        )
        return pl.pallas_call(
            functools.partial(sums_kernel, scale=scale, course_list=(0,)),
            grid_spec=second_spec,
            out_shape=jax.ShapeDtypeStruct((span, rows, count_ev), jnp.bfloat16),
        )(slot_of, eigenvectors, far_part, gauge_links, left, partial)


def panel_kernel(sink_ref, source_ref, stack_ref, wide_ref, out_ref):
    count_ev = sink_ref.shape[3]
    sink_real = sink_ref[0, 0, 0]
    sink_imag = sink_ref[0, 0, 1]
    sink_wide = jnp.concatenate(
        [
            jnp.concatenate([sink_real, -sink_imag], axis=1),
            jnp.concatenate([sink_imag, sink_real], axis=1),
        ],
        axis=0,
    )
    left = jnp.dot(sink_wide, stack_ref[...], preferred_element_type=jnp.float32)
    source_stack = jnp.concatenate([source_ref[0, 0, 0], source_ref[0, 0, 1]], axis=0)
    right = jnp.dot(wide_ref[...], source_stack, preferred_element_type=jnp.float32)
    total_real = 0.0
    total_imag = 0.0
    half = NSPIN * count_ev
    for spin in range(NSPIN):
        left_real = left[:count_ev, spin * count_ev : (spin + 1) * count_ev]
        left_imag = left[count_ev:, spin * count_ev : (spin + 1) * count_ev]
        right_real = right[spin * count_ev : (spin + 1) * count_ev]
        right_imag = right[half + spin * count_ev : half + (spin + 1) * count_ev]
        total_real = total_real + left_real * right_real + left_imag * right_imag
        total_imag = total_imag + left_imag * right_real - left_real * right_imag
    out_ref[0, 0:1, :] = jnp.sum(total_real, axis=0, keepdims=True)
    out_ref[0, 1:2, :] = jnp.sum(total_imag, axis=0, keepdims=True)


def contract_panel(gathered, panel):
    count_ops, count_ev = gathered.shape[1], panel.shape[1]
    stack = panel.reshape(2 * count_ev, NSPIN * count_ev)
    blocks = panel.reshape(2, count_ev, NSPIN, count_ev).transpose(0, 2, 1, 3).reshape(2, NSPIN * count_ev, count_ev)
    wide = jnp.concatenate(
        [
            jnp.concatenate([blocks[0], -blocks[1]], axis=1),
            jnp.concatenate([blocks[1], blocks[0]], axis=1),
        ],
        axis=0,
    )
    sums = pl.pallas_call(
        panel_kernel,
        grid=(count_ops,),
        in_specs=[
            pl.BlockSpec((1, 1, 2, count_ev, count_ev), lambda a: (0, a, 0, 0, 0)),
            pl.BlockSpec((1, 1, 2, count_ev, count_ev), lambda a: (1, a, 0, 0, 0)),
            pl.BlockSpec(stack.shape, lambda a: (0, 0)),
            pl.BlockSpec(wide.shape, lambda a: (0, 0)),
        ],
        out_specs=pl.BlockSpec((1, 2, count_ev), lambda a: (a, 0, 0)),
        out_shape=jax.ShapeDtypeStruct((count_ops, 2, count_ev), jnp.float32),
    )(gathered, gathered, stack, wide)
    return jnp.sum(sums, axis=-1) * (1.0 / (16.0 * count_ev))


def body(eigenvectors, gauge_links, perambulators, directions, momenta, pair_times):
    time_count = eigenvectors.shape[0]
    count_ev = eigenvectors.shape[3]
    local_sites = eigenvectors.shape[4]
    count_slabs = lax.axis_size("slab")
    nspace = NSPIN * count_slabs
    member = lax.axis_index("member")
    device = lax.axis_index("slab") * NSPIN + member
    half_rows = LY // 2
    extent_x = nspace // 2
    column = jnp.arange(local_sites, dtype=jnp.int32)
    coord_x = device // 2 + 0 * column
    coord_y = device % 2 * half_rows + column // LZ
    coord_z = column % LZ
    angle = phase_angles(momenta, (coord_x, coord_y, coord_z), (extent_x, LY, LZ))[0]
    halves = time_count
    span = time_count // halves
    far_tile = [(h * span, shifted(eigenvectors[h * span : (h + 1) * span], SPACE, -2)) for h in range(halves)]
    row_in = swapped(eigenvectors[..., :LZ], SPACE, 0)
    scale = 1.0 / math.sqrt(3.0 * extent_x * LY * LZ)
    slot_of, left, first_partial = local_sums(eigenvectors, gauge_links, row_in, directions, angle, scale)
    partial_chunks = []
    core = member % 2
    swapped_chunks = []
    for half in range(halves):
        first, far_part = far_tile[half]
        if swapped_chunks:
            far_part = lax.optimization_barrier((far_part, swapped_chunks[-1]))[0]
        chunk_partial = second_pass(slot_of, eigenvectors, gauge_links, left, first_partial, first, far_part, scale)
        partial_chunks.append(chunk_partial)
        if count_slabs <= 8:
            part_blocks = chunk_partial.reshape(span, count_slabs, 2, 2, -1, count_ev)
            send = lax.dynamic_index_in_dim(part_blocks, 1 - core, 3, keepdims=False)
            swapped_chunks.append(swapped(send, "member", 0))
    partial = jnp.concatenate(partial_chunks, 0)
    rows = partial.shape[1] // nspace
    if count_slabs <= 8:
        slab = lax.axis_index("slab")
        side = member // 2
        own_parts = []
        for half in range(halves):
            part_blocks = partial_chunks[half].reshape(span, count_slabs, 2, 2, rows, count_ev)
            keep = lax.dynamic_index_in_dim(part_blocks, core, 3, keepdims=False).astype(jnp.float32)
            chunk = keep + swapped_chunks[half].astype(jnp.float32)
            keep = lax.dynamic_index_in_dim(chunk, side, 2, keepdims=False)
            send = lax.dynamic_index_in_dim(chunk, 1 - side, 2, keepdims=False).astype(jnp.bfloat16)
            slab_sum = keep + swapped(send, "member", 1).astype(jnp.float32)
            slab_part = slab_sum.astype(jnp.bfloat16)
            total = lax.dynamic_index_in_dim(slab_sum, slab, 1, keepdims=False)
            for shift in range(1, count_slabs):
                piece = lax.dynamic_index_in_dim(slab_part, (slab + shift) % count_slabs, 1, keepdims=False)
                total = total + shifted(piece, "slab", shift).astype(jnp.float32)
            own_parts.append(total.astype(jnp.bfloat16))
        own_rows = jnp.concatenate(own_parts, 0)
    else:
        own_rows = lax.psum_scatter(partial, SPACE, scatter_dimension=1, tiled=True)
    slabs = jnp.arange(count_slabs, dtype=jnp.int32)
    wanted = jnp.stack([pair_times[slabs, 1], pair_times[slabs, 0]], 1)
    outgoing = jnp.take(own_rows, wanted.reshape(-1), axis=0).reshape(count_slabs, 2, rows, count_ev)
    if count_slabs <= 8:
        pieces = [jnp.take(outgoing, (slab + shift) % count_slabs, axis=0) for shift in range(count_slabs)]
        arrived = [pieces[0]] + [shifted(pieces[shift], "slab", shift) for shift in range(1, count_slabs)]
        arrived = jnp.stack(arrived, 0)
        across = jnp.take(arrived, (slab - jnp.arange(count_slabs, dtype=jnp.int32)) % count_slabs, axis=0)
    else:
        across = lax.all_to_all(outgoing, "slab", 0, 0, tiled=True)
    shared = [across] + [shifted(across, "member", shift) for shift in range(1, NSPIN)]
    shared = jnp.stack(shared, 0)
    within = jnp.take(shared, (member - jnp.arange(NSPIN, dtype=jnp.int32)) % NSPIN, axis=0)
    incoming = within.transpose(1, 0, 2, 3, 4).reshape(nspace, 2, rows, count_ev)
    count_ops = partial.shape[1] // (2 * count_ev)
    gathered = incoming.transpose(1, 0, 2, 3).reshape(2, count_ops, 2, count_ev, count_ev)
    correlators = contract_panel(gathered, perambulators[0])[None]
    return (own_rows, correlators)


def solution(mesh):
    count_cfg = mesh.shape["cfg"]
    count_slabs = mesh.shape["space"] // NSPIN
    split = Mesh(mesh.devices.reshape(count_cfg, count_slabs, NSPIN), ("cfg",) + SPACE)
    placed = (
        P("cfg", None, None, None, SPACE),
        P("cfg", None, None, None, None, SPACE),
        P(("cfg",) + SPACE, None, None, None),
        P(),
        P(),
        P(),
    )
    return jax.shard_map(
        body,
        mesh=split,
        in_specs=placed,
        out_specs=(P("cfg", SPACE, None), P(("cfg",) + SPACE, None, None)),
        check_vma=False,
    )
```

```python
import functools
import math

import jax
import jax.numpy as jnp
from jax import lax
from jax.experimental import pallas as pl
from jax.experimental.pallas import tpu as pltpu
from jax.sharding import Mesh, PartitionSpec as P

NSPIN = 4
LY = 32
LZ = 8
SPACE = ("slab", "member")


def shifted(block, axis, distance):
    devices = range(lax.axis_size(axis))
    route = [((i - distance) % len(devices), i) for i in devices]
    return lax.ppermute(block, axis, route)


def swapped(value, axis, bit):
    return lax.ppermute(value, axis, [(i, i ^ 1 << bit) for i in range(lax.axis_size(axis))])


def phase_angles(momenta, coords, extents):
    fraction = 0.0
    for course in range(3):
        turns = momenta[:, course : course + 1] * coords[course][None, :] % extents[course]
        fraction = fraction + turns.astype(jnp.float32) / extents[course]
    return 2.0 * math.pi * fraction


def sums_kernel(slot_ref, field_ref, near_ref, link_ref, trig_ref, *rest, scale, course_list):
    out_ref = rest[-1] if len(course_list) == 1 else rest[0]
    count_ev, sites = field_ref.shape[3], field_ref.shape[4]
    lane = lax.broadcasted_iota(jnp.int32, (count_ev, sites), 1)
    last_z = lane % LZ == LZ - 1
    last_row = lane >= sites - LZ
    if len(course_list) == 1:
        left = trig_ref[0]
    else:
        cosine = trig_ref[0:1, :]
        sine_part = trig_ref[1:2, :]
        here = [[field_ref[0, part, colour].astype(jnp.float32) for colour in range(3)] for part in range(2)]
        phased_real = [(cosine * here[0][c] - sine_part * here[1][c]).astype(jnp.bfloat16) for c in range(3)]
        phased_imag = [(sine_part * here[0][c] + cosine * here[1][c]).astype(jnp.bfloat16) for c in range(3)]
        real_rows = jnp.concatenate(phased_real + phased_imag, axis=1)
        imag_rows = jnp.concatenate([-v for v in phased_imag] + phased_real, axis=1)
        left = jnp.concatenate([real_rows, imag_rows], axis=0)
        rest[1][0] = left
    rows = 2 * count_ev
    for course in course_list:
        if course == 0:
            near = [[near_ref[0, part, colour].astype(jnp.float32) for colour in range(3)] for part in range(2)]
        elif course == 1:
            near = [
                [
                    jnp.where(last_row, near_ref[0, part, colour].astype(jnp.float32), pltpu.roll(here[part][colour], sites - LZ, 1))
                    for colour in range(3)
                ]
                for part in range(2)
            ]
        else:
            near = [
                [
                    jnp.where(last_z, pltpu.roll(here[part][colour], LZ - 1, 1), pltpu.roll(here[part][colour], sites - 1, 1))
                    for colour in range(3)
                ]
                for part in range(2)
            ]
        moved_real = []
        moved_imag = []
        for outer in range(3):
            real_part = 0.0
            imag_part = 0.0
            for inner in range(3):
                link_real = link_ref[0, course, 0, outer, inner : inner + 1, :]
                link_imag = link_ref[0, course, 1, outer, inner : inner + 1, :]
                real_part = real_part + link_real * near[0][inner] - link_imag * near[1][inner]
                imag_part = imag_part + link_real * near[1][inner] + link_imag * near[0][inner]
            moved_real.append(real_part.astype(jnp.bfloat16))
            moved_imag.append(imag_part.astype(jnp.bfloat16))
        right = jnp.concatenate(moved_real + moved_imag, axis=1)
        joined = lax.dot_general(left, right, (((1,), (1,)), ((), ())), preferred_element_type=jnp.float32)
        if len(course_list) == 1:
            out_ref[0] = rest[0][0]
            start = pl.multiple_of(slot_ref[course] * rows, rows)
            out_ref[0, pl.ds(start, rows), :] = (joined * scale).astype(out_ref.dtype)
        else:
            start = pl.multiple_of(slot_ref[course] * rows, rows)
            out_ref[0, pl.ds(start, rows), :] = (joined * scale).astype(out_ref.dtype)


def local_sums(eigenvectors, gauge_links, row_in, directions, angle, scale):
    time_count, _, _, count_ev, sites = eigenvectors.shape
    count_ops = directions.shape[0]
    slot_of = jnp.sum(
        (directions[None, :] == jnp.arange(count_ops, dtype=jnp.int32)[:, None]) * jnp.arange(count_ops, dtype=jnp.int32)[None, :],
        axis=1,
    ).astype(jnp.int32)
    row_wide = jnp.pad(row_in, ((0, 0),) * 4 + ((sites - LZ, 0),))
    trig = jnp.stack([jnp.cos(angle), jnp.sin(angle)], 0)
    field_spec = pl.BlockSpec((1, 2, 3, count_ev, sites), lambda t, slot: (t, 0, 0, 0, 0))
    link_spec = pl.BlockSpec((1,) + gauge_links.shape[1:], lambda t, slot: (t, 0, 0, 0, 0, 0))
    trig_spec = pl.BlockSpec(trig.shape, lambda t, slot: (0, 0))
    rows = count_ops * 2 * count_ev
    near_courses = tuple(course for course in range(count_ops) if course != 0)
    left_rows = 2 * count_ev
    left_spec = pl.BlockSpec((1, left_rows, 6 * sites), lambda t, slot: (t, 0, 0))
    first_spec = pltpu.PrefetchScalarGridSpec(
        num_scalar_prefetch=1,
        grid=(time_count,),
        in_specs=[field_spec, field_spec, link_spec, trig_spec],
        out_specs=[pl.BlockSpec((1, rows, count_ev), lambda t, slot: (t, 0, 0)), left_spec],
    )
    partial, left = pl.pallas_call(
        functools.partial(sums_kernel, scale=scale, course_list=near_courses),
        grid_spec=first_spec,
        out_shape=(
            jax.ShapeDtypeStruct((time_count, rows, count_ev), jnp.bfloat16),
            jax.ShapeDtypeStruct((time_count, left_rows, 6 * sites), jnp.bfloat16),
        ),
    )(slot_of, eigenvectors, row_wide, gauge_links, trig)
    return slot_of, left, partial


def second_pass(slot_of, eigenvectors, gauge_links, left, partial, first, far_part, scale):
    count_ev, sites = eigenvectors.shape[3], eigenvectors.shape[4]
    rows = partial.shape[1]
    left_rows = left.shape[1]
    if True:
        span = far_part.shape[0]
        second_spec = pltpu.PrefetchScalarGridSpec(
            num_scalar_prefetch=1,
            grid=(span,),
            in_specs=[
                pl.BlockSpec(memory_space=pl.ANY),
                pl.BlockSpec((1, 2, 3, count_ev, sites), lambda t, slot: (t, 0, 0, 0, 0)),
                pl.BlockSpec((1,) + gauge_links.shape[1:], lambda t, slot, first=first: (t + first, 0, 0, 0, 0, 0)),
                pl.BlockSpec((1, left_rows, 6 * sites), lambda t, slot, first=first: (t + first, 0, 0)),
                pl.BlockSpec((1, rows, count_ev), lambda t, slot, first=first: (t + first, 0, 0)),
            ],
            out_specs=pl.BlockSpec((1, rows, count_ev), lambda t, slot: (t, 0, 0)),
        )
        return pl.pallas_call(
            functools.partial(sums_kernel, scale=scale, course_list=(0,)),
            grid_spec=second_spec,
            out_shape=jax.ShapeDtypeStruct((span, rows, count_ev), jnp.bfloat16),
        )(slot_of, eigenvectors, far_part, gauge_links, left, partial)


def panel_kernel(sink_ref, source_ref, stack_ref, wide_ref, out_ref):
    count_ev = sink_ref.shape[3]
    sink_real = sink_ref[0, 0, 0]
    sink_imag = sink_ref[0, 0, 1]
    sink_wide = jnp.concatenate(
        [
            jnp.concatenate([sink_real, -sink_imag], axis=1),
            jnp.concatenate([sink_imag, sink_real], axis=1),
        ],
        axis=0,
    )
    left = jnp.dot(sink_wide, stack_ref[...], preferred_element_type=jnp.float32)
    source_stack = jnp.concatenate([source_ref[0, 0, 0], source_ref[0, 0, 1]], axis=0)
    right = jnp.dot(wide_ref[...], source_stack, preferred_element_type=jnp.float32)
    total_real = 0.0
    total_imag = 0.0
    half = NSPIN * count_ev
    for spin in range(NSPIN):
        left_real = left[:count_ev, spin * count_ev : (spin + 1) * count_ev]
        left_imag = left[count_ev:, spin * count_ev : (spin + 1) * count_ev]
        right_real = right[spin * count_ev : (spin + 1) * count_ev]
        right_imag = right[half + spin * count_ev : half + (spin + 1) * count_ev]
        total_real = total_real + left_real * right_real + left_imag * right_imag
        total_imag = total_imag + left_imag * right_real - left_real * right_imag
    out_ref[0, 0:1, :] = jnp.sum(total_real, axis=0, keepdims=True)
    out_ref[0, 1:2, :] = jnp.sum(total_imag, axis=0, keepdims=True)


def contract_panel(gathered, panel):
    count_ops, count_ev = gathered.shape[1], panel.shape[1]
    stack = panel.reshape(2 * count_ev, NSPIN * count_ev)
    blocks = panel.reshape(2, count_ev, NSPIN, count_ev).transpose(0, 2, 1, 3).reshape(2, NSPIN * count_ev, count_ev)
    wide = jnp.concatenate(
        [
            jnp.concatenate([blocks[0], -blocks[1]], axis=1),
            jnp.concatenate([blocks[1], blocks[0]], axis=1),
        ],
        axis=0,
    )
    sums = pl.pallas_call(
        panel_kernel,
        grid=(count_ops,),
        in_specs=[
            pl.BlockSpec((1, 1, 2, count_ev, count_ev), lambda a: (0, a, 0, 0, 0)),
            pl.BlockSpec((1, 1, 2, count_ev, count_ev), lambda a: (1, a, 0, 0, 0)),
            pl.BlockSpec(stack.shape, lambda a: (0, 0)),
            pl.BlockSpec(wide.shape, lambda a: (0, 0)),
        ],
        out_specs=pl.BlockSpec((1, 2, count_ev), lambda a: (a, 0, 0)),
        out_shape=jax.ShapeDtypeStruct((count_ops, 2, count_ev), jnp.float32),
    )(gathered, gathered, stack, wide)
    return jnp.sum(sums, axis=-1) * (1.0 / (16.0 * count_ev))


def body(eigenvectors, gauge_links, perambulators, directions, momenta, pair_times):
    time_count = eigenvectors.shape[0]
    count_ev = eigenvectors.shape[3]
    local_sites = eigenvectors.shape[4]
    count_slabs = lax.axis_size("slab")
    nspace = NSPIN * count_slabs
    member = lax.axis_index("member")
    device = lax.axis_index("slab") * NSPIN + member
    half_rows = LY // 2
    extent_x = nspace // 2
    column = jnp.arange(local_sites, dtype=jnp.int32)
    coord_x = device // 2 + 0 * column
    coord_y = device % 2 * half_rows + column // LZ
    coord_z = column % LZ
    angle = phase_angles(momenta, (coord_x, coord_y, coord_z), (extent_x, LY, LZ))[0]
    halves = 2 if time_count % 2 == 0 else 1
    span = time_count // halves
    far_tile = [(h * span, shifted(eigenvectors[h * span : (h + 1) * span], SPACE, -2)) for h in range(halves)]
    row_in = swapped(eigenvectors[..., :LZ], SPACE, 0)
    scale = 1.0 / math.sqrt(3.0 * extent_x * LY * LZ)
    slot_of, left, first_partial = local_sums(eigenvectors, gauge_links, row_in, directions, angle, scale)
    partial_chunks = []
    core = member % 2
    swapped_chunks = []
    for half in range(halves):
        first, far_part = far_tile[half]
        if swapped_chunks:
            far_part = lax.optimization_barrier((far_part, swapped_chunks[-1]))[0]
        chunk_partial = second_pass(slot_of, eigenvectors, gauge_links, left, first_partial, first, far_part, scale)
        partial_chunks.append(chunk_partial)
        if count_slabs <= 8:
            part_blocks = chunk_partial.reshape(span, count_slabs, 2, 2, -1, count_ev)
            send = lax.dynamic_index_in_dim(part_blocks, 1 - core, 3, keepdims=False)
            swapped_chunks.append(swapped(send, "member", 0))
    partial = jnp.concatenate(partial_chunks, 0)
    rows = partial.shape[1] // nspace
    if count_slabs <= 8:
        slab = lax.axis_index("slab")
        side = member // 2
        own_parts = []
        for half in range(halves):
            part_blocks = partial_chunks[half].reshape(span, count_slabs, 2, 2, rows, count_ev)
            keep = lax.dynamic_index_in_dim(part_blocks, core, 3, keepdims=False).astype(jnp.float32)
            chunk = keep + swapped_chunks[half].astype(jnp.float32)
            keep = lax.dynamic_index_in_dim(chunk, side, 2, keepdims=False)
            send = lax.dynamic_index_in_dim(chunk, 1 - side, 2, keepdims=False).astype(jnp.bfloat16)
            slab_sum = keep + swapped(send, "member", 1).astype(jnp.float32)
            slab_part = slab_sum.astype(jnp.bfloat16)
            total = lax.dynamic_index_in_dim(slab_sum, slab, 1, keepdims=False)
            for shift in range(1, count_slabs):
                piece = lax.dynamic_index_in_dim(slab_part, (slab + shift) % count_slabs, 1, keepdims=False)
                total = total + shifted(piece, "slab", shift).astype(jnp.float32)
            own_parts.append(total.astype(jnp.bfloat16))
        own_rows = jnp.concatenate(own_parts, 0)
    else:
        own_rows = lax.psum_scatter(partial, SPACE, scatter_dimension=1, tiled=True)
    slabs = jnp.arange(count_slabs, dtype=jnp.int32)
    wanted = jnp.stack([pair_times[slabs, 1], pair_times[slabs, 0]], 1)
    outgoing = jnp.take(own_rows, wanted.reshape(-1), axis=0).reshape(count_slabs, 2, rows, count_ev)
    if count_slabs <= 8:
        pieces = [jnp.take(outgoing, (slab + shift) % count_slabs, axis=0) for shift in range(count_slabs)]
        arrived = [pieces[0]] + [shifted(pieces[shift], "slab", shift) for shift in range(1, count_slabs)]
        arrived = jnp.stack(arrived, 0)
        across = jnp.take(arrived, (slab - jnp.arange(count_slabs, dtype=jnp.int32)) % count_slabs, axis=0)
    else:
        across = lax.all_to_all(outgoing, "slab", 0, 0, tiled=True)
    shared = [across] + [shifted(across, "member", shift) for shift in range(1, NSPIN)]
    shared = jnp.stack(shared, 0)
    within = jnp.take(shared, (member - jnp.arange(NSPIN, dtype=jnp.int32)) % NSPIN, axis=0)
    incoming = within.transpose(1, 0, 2, 3, 4).reshape(nspace, 2, rows, count_ev)
    count_ops = partial.shape[1] // (2 * count_ev)
    gathered = incoming.transpose(1, 0, 2, 3).reshape(2, count_ops, 2, count_ev, count_ev)
    correlators = contract_panel(gathered, perambulators[0])[None]
    return (own_rows, correlators)


def solution(mesh):
    count_cfg = mesh.shape["cfg"]
    count_slabs = mesh.shape["space"] // NSPIN
    split = Mesh(mesh.devices.reshape(count_cfg, count_slabs, NSPIN), ("cfg",) + SPACE)
    placed = (
        P("cfg", None, None, None, SPACE),
        P("cfg", None, None, None, None, SPACE),
        P(("cfg",) + SPACE, None, None, None),
        P(),
        P(),
        P(),
    )
    return jax.shard_map(
        body,
        mesh=split,
        in_specs=placed,
        out_specs=(P("cfg", SPACE, None), P(("cfg",) + SPACE, None, None)),
        check_vma=False,
    )
```

```python
import functools
import math

import jax
import jax.numpy as jnp
from jax import lax
from jax.experimental import pallas as pl
from jax.experimental.pallas import tpu as pltpu
from jax.sharding import Mesh, PartitionSpec as P

NSPIN = 4
LY = 32
LZ = 8
SPACE = ("slab", "member")


def shifted(block, axis, distance):
    devices = range(lax.axis_size(axis))
    route = [((i - distance) % len(devices), i) for i in devices]
    return lax.ppermute(block, axis, route)


def swapped(value, axis, bit):
    return lax.ppermute(value, axis, [(i, i ^ 1 << bit) for i in range(lax.axis_size(axis))])


def phase_angles(momenta, coords, extents):
    fraction = 0.0
    for course in range(3):
        turns = momenta[:, course : course + 1] * coords[course][None, :] % extents[course]
        fraction = fraction + turns.astype(jnp.float32) / extents[course]
    return 2.0 * math.pi * fraction


def sums_kernel(slot_ref, field_ref, near_ref, link_ref, trig_ref, *rest, scale, course_list):
    out_ref = rest[-1] if len(course_list) == 1 else rest[0]
    count_ev, sites = field_ref.shape[3], field_ref.shape[4]
    lane = lax.broadcasted_iota(jnp.int32, (count_ev, sites), 1)
    last_z = lane % LZ == LZ - 1
    last_row = lane >= sites - LZ
    if len(course_list) == 1:
        left = trig_ref[0]
    else:
        cosine = trig_ref[0:1, :]
        sine_part = trig_ref[1:2, :]
        here = [[field_ref[0, part, colour].astype(jnp.float32) for colour in range(3)] for part in range(2)]
        phased_real = [(cosine * here[0][c] - sine_part * here[1][c]).astype(jnp.bfloat16) for c in range(3)]
        phased_imag = [(sine_part * here[0][c] + cosine * here[1][c]).astype(jnp.bfloat16) for c in range(3)]
        real_rows = jnp.concatenate(phased_real + phased_imag, axis=1)
        imag_rows = jnp.concatenate([-v for v in phased_imag] + phased_real, axis=1)
        left = jnp.concatenate([real_rows, imag_rows], axis=0)
        rest[1][0] = left
    rows = 2 * count_ev
    for course in course_list:
        if course == 0:
            near = [[near_ref[0, part, colour].astype(jnp.float32) for colour in range(3)] for part in range(2)]
        elif course == 1:
            near = [
                [
                    jnp.where(last_row, near_ref[0, part, colour].astype(jnp.float32), pltpu.roll(here[part][colour], sites - LZ, 1))
                    for colour in range(3)
                ]
                for part in range(2)
            ]
        else:
            near = [
                [
                    jnp.where(last_z, pltpu.roll(here[part][colour], LZ - 1, 1), pltpu.roll(here[part][colour], sites - 1, 1))
                    for colour in range(3)
                ]
                for part in range(2)
            ]
        moved_real = []
        moved_imag = []
        for outer in range(3):
            real_part = 0.0
            imag_part = 0.0
            for inner in range(3):
                link_real = link_ref[0, course, 0, outer, inner : inner + 1, :]
                link_imag = link_ref[0, course, 1, outer, inner : inner + 1, :]
                real_part = real_part + link_real * near[0][inner] - link_imag * near[1][inner]
                imag_part = imag_part + link_real * near[1][inner] + link_imag * near[0][inner]
            moved_real.append(real_part.astype(jnp.bfloat16))
            moved_imag.append(imag_part.astype(jnp.bfloat16))
        right = jnp.concatenate(moved_real + moved_imag, axis=1)
        joined = lax.dot_general(left, right, (((1,), (1,)), ((), ())), preferred_element_type=jnp.float32)
        if len(course_list) == 1:
            out_ref[0] = rest[0][0]
            start = pl.multiple_of(slot_ref[course] * rows, rows)
            out_ref[0, pl.ds(start, rows), :] = (joined * scale).astype(out_ref.dtype)
        else:
            start = pl.multiple_of(slot_ref[course] * rows, rows)
            out_ref[0, pl.ds(start, rows), :] = (joined * scale).astype(out_ref.dtype)


def local_sums(eigenvectors, gauge_links, row_in, directions, angle, scale):
    time_count, _, _, count_ev, sites = eigenvectors.shape
    count_ops = directions.shape[0]
    slot_of = jnp.sum(
        (directions[None, :] == jnp.arange(count_ops, dtype=jnp.int32)[:, None]) * jnp.arange(count_ops, dtype=jnp.int32)[None, :],
        axis=1,
    ).astype(jnp.int32)
    row_wide = jnp.pad(row_in, ((0, 0),) * 4 + ((sites - LZ, 0),))
    trig = jnp.stack([jnp.cos(angle), jnp.sin(angle)], 0)
    field_spec = pl.BlockSpec((1, 2, 3, count_ev, sites), lambda t, slot: (t, 0, 0, 0, 0))
    link_spec = pl.BlockSpec((1,) + gauge_links.shape[1:], lambda t, slot: (t, 0, 0, 0, 0, 0))
    trig_spec = pl.BlockSpec(trig.shape, lambda t, slot: (0, 0))
    rows = count_ops * 2 * count_ev
    near_courses = tuple(course for course in range(count_ops) if course != 0)
    left_rows = 2 * count_ev
    left_spec = pl.BlockSpec((1, left_rows, 6 * sites), lambda t, slot: (t, 0, 0))
    first_spec = pltpu.PrefetchScalarGridSpec(
        num_scalar_prefetch=1,
        grid=(time_count,),
        in_specs=[field_spec, field_spec, link_spec, trig_spec],
        out_specs=[pl.BlockSpec((1, rows, count_ev), lambda t, slot: (t, 0, 0)), left_spec],
    )
    partial, left = pl.pallas_call(
        functools.partial(sums_kernel, scale=scale, course_list=near_courses),
        grid_spec=first_spec,
        out_shape=(
            jax.ShapeDtypeStruct((time_count, rows, count_ev), jnp.bfloat16),
            jax.ShapeDtypeStruct((time_count, left_rows, 6 * sites), jnp.bfloat16),
        ),
    )(slot_of, eigenvectors, row_wide, gauge_links, trig)
    return slot_of, left, partial


def second_pass(slot_of, eigenvectors, gauge_links, left, partial, first, far_part, scale):
    count_ev, sites = eigenvectors.shape[3], eigenvectors.shape[4]
    rows = partial.shape[1]
    left_rows = left.shape[1]
    if True:
        span = far_part.shape[0]
        second_spec = pltpu.PrefetchScalarGridSpec(
            num_scalar_prefetch=1,
            grid=(span,),
            in_specs=[
                pl.BlockSpec(memory_space=pl.ANY),
                pl.BlockSpec((1, 2, 3, count_ev, sites), lambda t, slot: (t, 0, 0, 0, 0)),
                pl.BlockSpec((1,) + gauge_links.shape[1:], lambda t, slot, first=first: (t + first, 0, 0, 0, 0, 0)),
                pl.BlockSpec((1, left_rows, 6 * sites), lambda t, slot, first=first: (t + first, 0, 0)),
                pl.BlockSpec((1, rows, count_ev), lambda t, slot, first=first: (t + first, 0, 0)),
            ],
            out_specs=pl.BlockSpec((1, rows, count_ev), lambda t, slot: (t, 0, 0)),
        )
        return pl.pallas_call(
            functools.partial(sums_kernel, scale=scale, course_list=(0,)),
            grid_spec=second_spec,
            out_shape=jax.ShapeDtypeStruct((span, rows, count_ev), jnp.bfloat16),
        )(slot_of, eigenvectors, far_part, gauge_links, left, partial)


def panel_kernel(sink_ref, source_ref, stack_ref, wide_ref, out_ref):
    count_ev = sink_ref.shape[3]
    sink_real = sink_ref[0, 0, 0]
    sink_imag = sink_ref[0, 0, 1]
    sink_wide = jnp.concatenate(
        [
            jnp.concatenate([sink_real, -sink_imag], axis=1),
            jnp.concatenate([sink_imag, sink_real], axis=1),
        ],
        axis=0,
    )
    left = jnp.dot(sink_wide, stack_ref[...], preferred_element_type=jnp.float32)
    source_stack = jnp.concatenate([source_ref[0, 0, 0], source_ref[0, 0, 1]], axis=0)
    right = jnp.dot(wide_ref[...], source_stack, preferred_element_type=jnp.float32)
    total_real = 0.0
    total_imag = 0.0
    half = NSPIN * count_ev
    for spin in range(NSPIN):
        left_real = left[:count_ev, spin * count_ev : (spin + 1) * count_ev]
        left_imag = left[count_ev:, spin * count_ev : (spin + 1) * count_ev]
        right_real = right[spin * count_ev : (spin + 1) * count_ev]
        right_imag = right[half + spin * count_ev : half + (spin + 1) * count_ev]
        total_real = total_real + left_real * right_real + left_imag * right_imag
        total_imag = total_imag + left_imag * right_real - left_real * right_imag
    out_ref[0, 0:1, :] = jnp.sum(total_real, axis=0, keepdims=True)
    out_ref[0, 1:2, :] = jnp.sum(total_imag, axis=0, keepdims=True)


def contract_panel(gathered, panel):
    count_ops, count_ev = gathered.shape[1], panel.shape[1]
    stack = panel.reshape(2 * count_ev, NSPIN * count_ev)
    blocks = panel.reshape(2, count_ev, NSPIN, count_ev).transpose(0, 2, 1, 3).reshape(2, NSPIN * count_ev, count_ev)
    wide = jnp.concatenate(
        [
            jnp.concatenate([blocks[0], -blocks[1]], axis=1),
            jnp.concatenate([blocks[1], blocks[0]], axis=1),
        ],
        axis=0,
    )
    sums = pl.pallas_call(
        panel_kernel,
        grid=(count_ops,),
        in_specs=[
            pl.BlockSpec((1, 1, 2, count_ev, count_ev), lambda a: (0, a, 0, 0, 0)),
            pl.BlockSpec((1, 1, 2, count_ev, count_ev), lambda a: (1, a, 0, 0, 0)),
            pl.BlockSpec(stack.shape, lambda a: (0, 0)),
            pl.BlockSpec(wide.shape, lambda a: (0, 0)),
        ],
        out_specs=pl.BlockSpec((1, 2, count_ev), lambda a: (a, 0, 0)),
        out_shape=jax.ShapeDtypeStruct((count_ops, 2, count_ev), jnp.float32),
    )(gathered, gathered, stack, wide)
    return jnp.sum(sums, axis=-1) * (1.0 / (16.0 * count_ev))


def body(eigenvectors, gauge_links, perambulators, directions, momenta, pair_times):
    time_count = eigenvectors.shape[0]
    count_ev = eigenvectors.shape[3]
    local_sites = eigenvectors.shape[4]
    count_slabs = lax.axis_size("slab")
    nspace = NSPIN * count_slabs
    member = lax.axis_index("member")
    device = lax.axis_index("slab") * NSPIN + member
    half_rows = LY // 2
    extent_x = nspace // 2
    column = jnp.arange(local_sites, dtype=jnp.int32)
    coord_x = device // 2 + 0 * column
    coord_y = device % 2 * half_rows + column // LZ
    coord_z = column % LZ
    angle = phase_angles(momenta, (coord_x, coord_y, coord_z), (extent_x, LY, LZ))[0]
    lead = (time_count + 1) // 2
    middle = (time_count - lead + 1) // 2
    sizes = [size for size in (lead, middle, time_count - lead - middle) if size > 0]
    starts = [sum(sizes[:h]) for h in range(len(sizes))]
    halves = len(sizes)
    far_tile = [(starts[h], shifted(eigenvectors[starts[h] : starts[h] + sizes[h]], SPACE, -2)) for h in range(halves)]
    row_in = swapped(eigenvectors[..., :LZ], SPACE, 0)
    scale = 1.0 / math.sqrt(3.0 * extent_x * LY * LZ)
    slot_of, left, first_partial = local_sums(eigenvectors, gauge_links, row_in, directions, angle, scale)
    partial_chunks = []
    core = member % 2
    swapped_chunks = []
    for half in range(halves):
        first, far_part = far_tile[half]
        if swapped_chunks:
            far_part = lax.optimization_barrier((far_part, swapped_chunks[-1]))[0]
        chunk_partial = second_pass(slot_of, eigenvectors, gauge_links, left, first_partial, first, far_part, scale)
        partial_chunks.append(chunk_partial)
        if count_slabs <= 8:
            part_blocks = chunk_partial.reshape(sizes[half], count_slabs, 2, 2, -1, count_ev)
            send = lax.dynamic_index_in_dim(part_blocks, 1 - core, 3, keepdims=False)
            swapped_chunks.append(swapped(send, "member", 0))
    partial = jnp.concatenate(partial_chunks, 0)
    rows = partial.shape[1] // nspace
    if count_slabs <= 8:
        slab = lax.axis_index("slab")
        side = member // 2
        own_parts = []
        for half in range(halves):
            part_blocks = partial_chunks[half].reshape(sizes[half], count_slabs, 2, 2, rows, count_ev)
            keep = lax.dynamic_index_in_dim(part_blocks, core, 3, keepdims=False).astype(jnp.float32)
            chunk = keep + swapped_chunks[half].astype(jnp.float32)
            keep = lax.dynamic_index_in_dim(chunk, side, 2, keepdims=False)
            send = lax.dynamic_index_in_dim(chunk, 1 - side, 2, keepdims=False).astype(jnp.bfloat16)
            slab_sum = keep + swapped(send, "member", 1).astype(jnp.float32)
            slab_part = slab_sum.astype(jnp.bfloat16)
            total = lax.dynamic_index_in_dim(slab_sum, slab, 1, keepdims=False)
            for shift in range(1, count_slabs):
                piece = lax.dynamic_index_in_dim(slab_part, (slab + shift) % count_slabs, 1, keepdims=False)
                total = total + shifted(piece, "slab", shift).astype(jnp.float32)
            own_parts.append(total.astype(jnp.bfloat16))
        own_rows = jnp.concatenate(own_parts, 0)
    else:
        own_rows = lax.psum_scatter(partial, SPACE, scatter_dimension=1, tiled=True)
    slabs = jnp.arange(count_slabs, dtype=jnp.int32)
    wanted = jnp.stack([pair_times[slabs, 1], pair_times[slabs, 0]], 1)
    outgoing = jnp.take(own_rows, wanted.reshape(-1), axis=0).reshape(count_slabs, 2, rows, count_ev)
    if count_slabs <= 8:
        pieces = [jnp.take(outgoing, (slab + shift) % count_slabs, axis=0) for shift in range(count_slabs)]
        arrived = [pieces[0]] + [shifted(pieces[shift], "slab", shift) for shift in range(1, count_slabs)]
        arrived = jnp.stack(arrived, 0)
        across = jnp.take(arrived, (slab - jnp.arange(count_slabs, dtype=jnp.int32)) % count_slabs, axis=0)
    else:
        across = lax.all_to_all(outgoing, "slab", 0, 0, tiled=True)
    shared = [across] + [shifted(across, "member", shift) for shift in range(1, NSPIN)]
    shared = jnp.stack(shared, 0)
    within = jnp.take(shared, (member - jnp.arange(NSPIN, dtype=jnp.int32)) % NSPIN, axis=0)
    incoming = within.transpose(1, 0, 2, 3, 4).reshape(nspace, 2, rows, count_ev)
    count_ops = partial.shape[1] // (2 * count_ev)
    gathered = incoming.transpose(1, 0, 2, 3).reshape(2, count_ops, 2, count_ev, count_ev)
    correlators = contract_panel(gathered, perambulators[0])[None]
    return (own_rows, correlators)


def solution(mesh):
    count_cfg = mesh.shape["cfg"]
    count_slabs = mesh.shape["space"] // NSPIN
    split = Mesh(mesh.devices.reshape(count_cfg, count_slabs, NSPIN), ("cfg",) + SPACE)
    placed = (
        P("cfg", None, None, None, SPACE),
        P("cfg", None, None, None, None, SPACE),
        P(("cfg",) + SPACE, None, None, None),
        P(),
        P(),
        P(),
    )
    return jax.shard_map(
        body,
        mesh=split,
        in_specs=placed,
        out_specs=(P("cfg", SPACE, None), P(("cfg",) + SPACE, None, None)),
        check_vma=False,
    )
```

```python
import functools
import math

import jax
import jax.numpy as jnp
from jax import lax
from jax.experimental import pallas as pl
from jax.experimental.pallas import tpu as pltpu
from jax.sharding import Mesh, PartitionSpec as P

NSPIN = 4
LY = 32
LZ = 8
SPACE = ("slab", "member")


def shifted(block, axis, distance):
    devices = range(lax.axis_size(axis))
    route = [((i - distance) % len(devices), i) for i in devices]
    return lax.ppermute(block, axis, route)


def swapped(value, axis, bit):
    return lax.ppermute(value, axis, [(i, i ^ 1 << bit) for i in range(lax.axis_size(axis))])


def phase_angles(momenta, coords, extents):
    fraction = 0.0
    for course in range(3):
        turns = momenta[:, course : course + 1] * coords[course][None, :] % extents[course]
        fraction = fraction + turns.astype(jnp.float32) / extents[course]
    return 2.0 * math.pi * fraction


def sums_kernel(slot_ref, field_ref, near_ref, link_ref, trig_ref, *rest, scale, course_list):
    out_ref = rest[-1] if len(course_list) == 1 else rest[0]
    count_ev, sites = field_ref.shape[3], field_ref.shape[4]
    lane = lax.broadcasted_iota(jnp.int32, (count_ev, sites), 1)
    last_z = lane % LZ == LZ - 1
    last_row = lane >= sites - LZ
    if len(course_list) == 1:
        left = trig_ref[0]
    else:
        cosine = trig_ref[0:1, :]
        sine_part = trig_ref[1:2, :]
        here = [[field_ref[0, part, colour].astype(jnp.float32) for colour in range(3)] for part in range(2)]
        phased_real = [(cosine * here[0][c] - sine_part * here[1][c]).astype(jnp.bfloat16) for c in range(3)]
        phased_imag = [(sine_part * here[0][c] + cosine * here[1][c]).astype(jnp.bfloat16) for c in range(3)]
        real_rows = jnp.concatenate(phased_real + phased_imag, axis=1)
        imag_rows = jnp.concatenate([-v for v in phased_imag] + phased_real, axis=1)
        left = jnp.concatenate([real_rows, imag_rows], axis=0)
        rest[1][0] = left
    rows = 2 * count_ev
    for course in course_list:
        if course == 0:
            near = [[near_ref[0, part, colour].astype(jnp.float32) for colour in range(3)] for part in range(2)]
        elif course == 1:
            near = [
                [
                    jnp.where(last_row, near_ref[0, part, colour].astype(jnp.float32), pltpu.roll(here[part][colour], sites - LZ, 1))
                    for colour in range(3)
                ]
                for part in range(2)
            ]
        else:
            near = [
                [
                    jnp.where(last_z, pltpu.roll(here[part][colour], LZ - 1, 1), pltpu.roll(here[part][colour], sites - 1, 1))
                    for colour in range(3)
                ]
                for part in range(2)
            ]
        moved_real = []
        moved_imag = []
        for outer in range(3):
            real_part = 0.0
            imag_part = 0.0
            for inner in range(3):
                link_real = link_ref[0, course, 0, outer, inner : inner + 1, :]
                link_imag = link_ref[0, course, 1, outer, inner : inner + 1, :]
                real_part = real_part + link_real * near[0][inner] - link_imag * near[1][inner]
                imag_part = imag_part + link_real * near[1][inner] + link_imag * near[0][inner]
            moved_real.append(real_part.astype(jnp.bfloat16))
            moved_imag.append(imag_part.astype(jnp.bfloat16))
        right = jnp.concatenate(moved_real + moved_imag, axis=1)
        joined = lax.dot_general(left, right, (((1,), (1,)), ((), ())), preferred_element_type=jnp.float32)
        if len(course_list) == 1:
            out_ref[0] = rest[0][0]
            start = pl.multiple_of(slot_ref[course] * rows, rows)
            out_ref[0, pl.ds(start, rows), :] = (joined * scale).astype(out_ref.dtype)
        else:
            start = pl.multiple_of(slot_ref[course] * rows, rows)
            out_ref[0, pl.ds(start, rows), :] = (joined * scale).astype(out_ref.dtype)


def local_sums(eigenvectors, gauge_links, row_in, directions, angle, scale):
    time_count, _, _, count_ev, sites = eigenvectors.shape
    count_ops = directions.shape[0]
    slot_of = jnp.sum(
        (directions[None, :] == jnp.arange(count_ops, dtype=jnp.int32)[:, None]) * jnp.arange(count_ops, dtype=jnp.int32)[None, :],
        axis=1,
    ).astype(jnp.int32)
    row_wide = jnp.pad(row_in, ((0, 0),) * 4 + ((sites - LZ, 0),))
    trig = jnp.stack([jnp.cos(angle), jnp.sin(angle)], 0)
    field_spec = pl.BlockSpec((1, 2, 3, count_ev, sites), lambda t, slot: (t, 0, 0, 0, 0))
    link_spec = pl.BlockSpec((1,) + gauge_links.shape[1:], lambda t, slot: (t, 0, 0, 0, 0, 0))
    trig_spec = pl.BlockSpec(trig.shape, lambda t, slot: (0, 0))
    rows = count_ops * 2 * count_ev
    near_courses = tuple(course for course in range(count_ops) if course != 0)
    left_rows = 2 * count_ev
    left_spec = pl.BlockSpec((1, left_rows, 6 * sites), lambda t, slot: (t, 0, 0))
    first_spec = pltpu.PrefetchScalarGridSpec(
        num_scalar_prefetch=1,
        grid=(time_count,),
        in_specs=[field_spec, field_spec, link_spec, trig_spec],
        out_specs=[pl.BlockSpec((1, rows, count_ev), lambda t, slot: (t, 0, 0)), left_spec],
    )
    partial, left = pl.pallas_call(
        functools.partial(sums_kernel, scale=scale, course_list=near_courses),
        grid_spec=first_spec,
        out_shape=(
            jax.ShapeDtypeStruct((time_count, rows, count_ev), jnp.bfloat16),
            jax.ShapeDtypeStruct((time_count, left_rows, 6 * sites), jnp.bfloat16),
        ),
    )(slot_of, eigenvectors, row_wide, gauge_links, trig)
    return slot_of, left, partial


def second_pass(slot_of, eigenvectors, gauge_links, left, partial, first, far_part, scale):
    count_ev, sites = eigenvectors.shape[3], eigenvectors.shape[4]
    rows = partial.shape[1]
    left_rows = left.shape[1]
    if True:
        span = far_part.shape[0]
        second_spec = pltpu.PrefetchScalarGridSpec(
            num_scalar_prefetch=1,
            grid=(span,),
            in_specs=[
                pl.BlockSpec(memory_space=pl.ANY),
                pl.BlockSpec((1, 2, 3, count_ev, sites), lambda t, slot: (t, 0, 0, 0, 0)),
                pl.BlockSpec((1,) + gauge_links.shape[1:], lambda t, slot, first=first: (t + first, 0, 0, 0, 0, 0)),
                pl.BlockSpec((1, left_rows, 6 * sites), lambda t, slot, first=first: (t + first, 0, 0)),
                pl.BlockSpec((1, rows, count_ev), lambda t, slot, first=first: (t + first, 0, 0)),
            ],
            out_specs=pl.BlockSpec((1, rows, count_ev), lambda t, slot: (t, 0, 0)),
        )
        return pl.pallas_call(
            functools.partial(sums_kernel, scale=scale, course_list=(0,)),
            grid_spec=second_spec,
            out_shape=jax.ShapeDtypeStruct((span, rows, count_ev), jnp.bfloat16),
        )(slot_of, eigenvectors, far_part, gauge_links, left, partial)


def panel_kernel(sink_ref, source_ref, stack_ref, wide_ref, out_ref):
    count_ev = sink_ref.shape[3]
    sink_real = sink_ref[0, 0, 0]
    sink_imag = sink_ref[0, 0, 1]
    sink_wide = jnp.concatenate(
        [
            jnp.concatenate([sink_real, -sink_imag], axis=1),
            jnp.concatenate([sink_imag, sink_real], axis=1),
        ],
        axis=0,
    )
    left = jnp.dot(sink_wide, stack_ref[...], preferred_element_type=jnp.float32)
    source_stack = jnp.concatenate([source_ref[0, 0, 0], source_ref[0, 0, 1]], axis=0)
    right = jnp.dot(wide_ref[...], source_stack, preferred_element_type=jnp.float32)
    total_real = 0.0
    total_imag = 0.0
    half = NSPIN * count_ev
    for spin in range(NSPIN):
        left_real = left[:count_ev, spin * count_ev : (spin + 1) * count_ev]
        left_imag = left[count_ev:, spin * count_ev : (spin + 1) * count_ev]
        right_real = right[spin * count_ev : (spin + 1) * count_ev]
        right_imag = right[half + spin * count_ev : half + (spin + 1) * count_ev]
        total_real = total_real + left_real * right_real + left_imag * right_imag
        total_imag = total_imag + left_imag * right_real - left_real * right_imag
    out_ref[0, 0:1, :] = jnp.sum(total_real, axis=0, keepdims=True)
    out_ref[0, 1:2, :] = jnp.sum(total_imag, axis=0, keepdims=True)


def contract_panel(gathered, panel):
    count_ops, count_ev = gathered.shape[1], panel.shape[1]
    stack = panel.reshape(2 * count_ev, NSPIN * count_ev)
    blocks = panel.reshape(2, count_ev, NSPIN, count_ev).transpose(0, 2, 1, 3).reshape(2, NSPIN * count_ev, count_ev)
    wide = jnp.concatenate(
        [
            jnp.concatenate([blocks[0], -blocks[1]], axis=1),
            jnp.concatenate([blocks[1], blocks[0]], axis=1),
        ],
        axis=0,
    )
    sums = pl.pallas_call(
        panel_kernel,
        grid=(count_ops,),
        in_specs=[
            pl.BlockSpec((1, 1, 2, count_ev, count_ev), lambda a: (0, a, 0, 0, 0)),
            pl.BlockSpec((1, 1, 2, count_ev, count_ev), lambda a: (1, a, 0, 0, 0)),
            pl.BlockSpec(stack.shape, lambda a: (0, 0)),
            pl.BlockSpec(wide.shape, lambda a: (0, 0)),
        ],
        out_specs=pl.BlockSpec((1, 2, count_ev), lambda a: (a, 0, 0)),
        out_shape=jax.ShapeDtypeStruct((count_ops, 2, count_ev), jnp.float32),
    )(gathered, gathered, stack, wide)
    return jnp.sum(sums, axis=-1) * (1.0 / (16.0 * count_ev))


def body(eigenvectors, gauge_links, perambulators, directions, momenta, pair_times):
    time_count = eigenvectors.shape[0]
    count_ev = eigenvectors.shape[3]
    local_sites = eigenvectors.shape[4]
    count_slabs = lax.axis_size("slab")
    nspace = NSPIN * count_slabs
    member = lax.axis_index("member")
    device = lax.axis_index("slab") * NSPIN + member
    half_rows = LY // 2
    extent_x = nspace // 2
    column = jnp.arange(local_sites, dtype=jnp.int32)
    coord_x = device // 2 + 0 * column
    coord_y = device % 2 * half_rows + column // LZ
    coord_z = column % LZ
    angle = phase_angles(momenta, (coord_x, coord_y, coord_z), (extent_x, LY, LZ))[0]
    halves = 3 if time_count % 3 == 0 else (2 if time_count % 2 == 0 else 1)
    span = time_count // halves
    far_tile = [(h * span, shifted(eigenvectors[h * span : (h + 1) * span], SPACE, -2)) for h in range(halves)]
    row_in = swapped(eigenvectors[..., :LZ], SPACE, 0)
    scale = 1.0 / math.sqrt(3.0 * extent_x * LY * LZ)
    slot_of, left, first_partial = local_sums(eigenvectors, gauge_links, row_in, directions, angle, scale)
    partial_chunks = []
    core = member % 2
    swapped_chunks = []
    for half in range(halves):
        first, far_part = far_tile[half]
        if swapped_chunks:
            far_part = lax.optimization_barrier((far_part, swapped_chunks[-1]))[0]
        chunk_partial = second_pass(slot_of, eigenvectors, gauge_links, left, first_partial, first, far_part, scale)
        partial_chunks.append(chunk_partial)
        if count_slabs <= 8:
            part_blocks = chunk_partial.reshape(span, count_slabs, 2, 2, -1, count_ev)
            send = lax.dynamic_index_in_dim(part_blocks, 1 - core, 3, keepdims=False)
            swapped_chunks.append(swapped(send, "member", 0))
    partial = jnp.concatenate(partial_chunks, 0)
    rows = partial.shape[1] // nspace
    if count_slabs <= 8:
        slab = lax.axis_index("slab")
        side = member // 2
        own_parts = []
        for half in range(halves):
            part_blocks = partial_chunks[half].reshape(span, count_slabs, 2, 2, rows, count_ev)
            keep = lax.dynamic_index_in_dim(part_blocks, core, 3, keepdims=False).astype(jnp.float32)
            chunk = keep + swapped_chunks[half].astype(jnp.float32)
            keep = lax.dynamic_index_in_dim(chunk, side, 2, keepdims=False)
            send = lax.dynamic_index_in_dim(chunk, 1 - side, 2, keepdims=False).astype(jnp.bfloat16)
            slab_sum = keep + swapped(send, "member", 1).astype(jnp.float32)
            slab_part = slab_sum.astype(jnp.bfloat16)
            total = lax.dynamic_index_in_dim(slab_sum, slab, 1, keepdims=False)
            for shift in range(1, count_slabs):
                piece = lax.dynamic_index_in_dim(slab_part, (slab + shift) % count_slabs, 1, keepdims=False)
                total = total + shifted(piece, "slab", shift).astype(jnp.float32)
            own_parts.append(total.astype(jnp.bfloat16))
        own_rows = jnp.concatenate(own_parts, 0)
    else:
        own_rows = lax.psum_scatter(partial, SPACE, scatter_dimension=1, tiled=True)
    slabs = jnp.arange(count_slabs, dtype=jnp.int32)
    wanted = jnp.stack([pair_times[slabs, 1], pair_times[slabs, 0]], 1)
    outgoing = jnp.take(own_rows, wanted.reshape(-1), axis=0).reshape(count_slabs, 2, rows, count_ev)
    if count_slabs <= 8:
        pieces = [jnp.take(outgoing, (slab + shift) % count_slabs, axis=0) for shift in range(count_slabs)]
        arrived = [pieces[0]] + [shifted(pieces[shift], "slab", shift) for shift in range(1, count_slabs)]
        arrived = jnp.stack(arrived, 0)
        across = jnp.take(arrived, (slab - jnp.arange(count_slabs, dtype=jnp.int32)) % count_slabs, axis=0)
    else:
        across = lax.all_to_all(outgoing, "slab", 0, 0, tiled=True)
    pair = jnp.stack([across, swapped(across, "member", 0)], 0)
    by_core = jnp.take(pair, (jnp.arange(2, dtype=jnp.int32) + member % 2) % 2, axis=0)
    both = jnp.stack([by_core, swapped(by_core, "member", 1)], 0)
    within = jnp.take(both, (jnp.arange(2, dtype=jnp.int32) + member // 2) % 2, axis=0)
    within = within.reshape((NSPIN,) + across.shape)
    incoming = within.transpose(1, 0, 2, 3, 4).reshape(nspace, 2, rows, count_ev)
    count_ops = partial.shape[1] // (2 * count_ev)
    gathered = incoming.transpose(1, 0, 2, 3).reshape(2, count_ops, 2, count_ev, count_ev)
    correlators = contract_panel(gathered, perambulators[0])[None]
    return (own_rows, correlators)


def solution(mesh):
    count_cfg = mesh.shape["cfg"]
    count_slabs = mesh.shape["space"] // NSPIN
    split = Mesh(mesh.devices.reshape(count_cfg, count_slabs, NSPIN), ("cfg",) + SPACE)
    placed = (
        P("cfg", None, None, None, SPACE),
        P("cfg", None, None, None, None, SPACE),
        P(("cfg",) + SPACE, None, None, None),
        P(),
        P(),
        P(),
    )
    return jax.shard_map(
        body,
        mesh=split,
        in_specs=placed,
        out_specs=(P("cfg", SPACE, None), P(("cfg",) + SPACE, None, None)),
        check_vma=False,
    )
```
